256 devices in a mesh: sec: 16 (over x, y), vel: 16 (over z, core).
Axes of the slice: x: 4, y: 4, z: 8, core: 2. Of those that a mesh axis runs over, the one named last changes fastest.
Arguments:
- distribution: float32 [13824, 4096], P('vel', 'sec'), may hold values from -6 to 6
- collision: float32 [4096], P('sec'), may hold values from 0.05 to 2
- lower_blocks: float32 [25, 4096], P(None, 'sec'), may hold values from -0.6 to 0.6
- upper_blocks: float32 [25, 4096], P(None, 'sec'), may hold values from -0.6 to 0.6
- diag_inverse: float32 [25, 4096], P(None, 'sec'), may hold values from -0.2 to 1.4
Outputs:
- new_distribution: float32 [13824, 4096], P('vel', 'sec')
- macro: float32 [5, 4096], P(None, 'sec')
The draws below stay inside these ranges and needn't reach their ends.
All inputs are finite; a program needn't handle non-finite values.
Results may differ from the reference program's by a relative error of at most 0.0003.
Values sent between devices are 32-bit elements; how exact they have to be, the bound alone decides.
No kernel may reach another device: no remote copies, remote signals or barrier semaphores. Data moves between devices by JAX's collectives and lax.ppermute only.
A program may use at most 64 MiB of HBM per device.

```python
import math
import jax
import jax.numpy as jnp
import numpy as np
from jax import lax

NXI = 24
NV = 13824
TUBES = 128
JACOBI = 4
NEWTON = 2
NL = 32
NC = 4096


def draw_diag_inverse(key, part):
    diag_key, off_key = jax.random.split(jax.random.fold_in(key, 7))
    diagonal = jax.random.uniform(diag_key, (5, 1, NC), jnp.float32, 0.7, 1.3)
    offdiag = jnp.clip(0.08 * jax.random.normal(off_key, (5, 5, NC), jnp.float32), -0.2, 0.2)
    identity = jnp.eye(5, dtype=jnp.float32)[:, :, None]
    matrices = identity * diagonal + (1.0 - identity) * offdiag
    return matrices.reshape(25, NC)


def shard_levels(stream_key, extent, cuts, low, largest):
    def one(position, shards_of):
        draws = jax.random.uniform(jax.random.fold_in(jax.random.fold_in(stream_key, 6), position), (shards_of,), jnp.float32, low / len(cuts), largest / len(cuts))
        return jnp.repeat(jnp.exp(draws), extent[position] // shards_of).reshape((-1,) + (1,) * (len(extent) - position - 1))

    factor_of = one(*cuts[0])
    for cut in cuts[1:]:
        factor_of = factor_of * one(*cut)
    return factor_of


def scatter_about(rng, dims, deviation, bound, shards=(), held_as=jnp.bfloat16):
    drawn = deviation * jax.random.normal(rng, dims, jnp.float32)
    if shards:
        drawn = drawn * shard_levels(rng, dims, shards, -0.22, 0.18)
    return jnp.clip(drawn, -bound, bound).astype(held_as)


def setup_inputs(seed: int = 0) -> dict:
    keys = jax.random.split(jax.random.key(seed), 6)
    return {
        "distribution": scatter_about(keys[0], (NV, NC), 1.0, 6.0, ((0, 16), (1, 16)), jnp.float32),
        "collision": jnp.clip(jnp.exp(math.log(2.0) - 3.6888794 * jax.random.uniform(keys[1], (NC,), jnp.float32) ** shard_levels(keys[1], (NC,), ((0, 16),), -0.2, 0.2)), 0.05, 2.0),
        "lower_blocks": scatter_about(keys[2], (25, NC), 0.15, 0.6, ((1, 16),), jnp.float32),
        "upper_blocks": scatter_about(keys[3], (25, NC), 0.15, 0.6, ((1, 16),), jnp.float32),
        "diag_inverse": draw_diag_inverse(jax.random.fold_in(keys[5], 71), 0),
    }


HIGH = lax.Precision.HIGHEST
pseudo_rate = 1.0

def hermite_rule(count):
    quarter = math.pi ** (-0.25)
    found = []
    last_slope = 1.0
    for index in range(count // 2):
        if index == 0:
            guess = math.sqrt(2.0 * count + 1.0) - 1.85575 * (2.0 * count + 1.0) ** (-0.16667)
        elif index == 1:
            guess = guess - 1.14 * count ** 0.426 / guess
        elif index == 2:
            guess = 1.86 * guess - 0.86 * found[0][0]
        elif index == 3:
            guess = 1.91 * guess - 0.91 * found[1][0]
        else:
            guess = 2.0 * guess - found[index - 2][0]
        for repeat in range(60):
            current = quarter
            previous = 0.0
            for order in range(count):
                older = previous
                previous = current
                current = guess * math.sqrt(2.0 / (order + 1)) * previous - math.sqrt(order / (order + 1.0)) * older
            last_slope = math.sqrt(2.0 * count) * previous
            guess = guess - current / last_slope
        found.append((guess, 2.0 / (last_slope * last_slope)))
    positive = found[::-1]
    points = [-pair[0] for pair in found] + [pair[0] for pair in positive]
    weights = [pair[1] for pair in found] + [pair[1] for pair in positive]
    return (np.array(points), np.array(weights))

def node_tables(axis_points):
    points, weights = hermite_rule(axis_points)
    node_index = np.arange(axis_points ** 3)
    idx_x = node_index % axis_points
    idx_z = node_index // axis_points % axis_points
    idx_y = node_index // (axis_points * axis_points)
    along_x = points[idx_x]
    along_y = points[idx_y]
    along_z = points[idx_z]
    node_weight = weights[idx_x] * weights[idx_y] * weights[idx_z] / math.pi ** 1.5
    energy = along_x ** 2 + along_y ** 2 + along_z ** 2 - 1.5
    moment_basis = np.stack([along_x * 0.0 + 1.0, along_x, along_y, along_z, energy])
    norm_scale = np.array([1.0, 0.5, 0.5, 0.5, 1.5])
    return (along_x, node_weight, moment_basis * node_weight[None, :], moment_basis / norm_scale[:, None])

def apply_block(matrices, vector):
    shaped = matrices.reshape((5, 5) + vector.shape[1:])
    return lax.optimization_barrier(jnp.sum(shaped * vector[None], axis=1))

def newton_sums(loaded, signed, shift_mass, shift_flow):
    growth = jnp.exp(shift_mass + shift_flow * signed)
    scaled = loaded * growth
    excess = loaded * (growth - 1.0)
    return jnp.stack([jnp.sum(scaled), jnp.sum(scaled * signed), jnp.sum(scaled * signed * signed), jnp.sum(excess), jnp.sum(excess * signed)])

def newton_update(shift_mass, shift_flow, sums, goal_mass, goal_flow):
    resid_mass = sums[3] - goal_mass
    resid_flow = sums[4] - goal_flow
    determinant = sums[0] * sums[2] - sums[1] * sums[1]
    new_mass = shift_mass - (sums[2] * resid_mass - sums[1] * resid_flow) / determinant
    new_flow = shift_flow - (sums[0] * resid_flow - sums[1] * resid_mass) / determinant
    return (new_mass, new_flow)

def reference(distribution, collision, lower_blocks, upper_blocks, diag_inverse):
    along_x, node_weight, weighted_np, rebuild_np = node_tables(NXI)
    weighted = jnp.asarray(weighted_np, jnp.float32)
    rebuild = jnp.asarray(rebuild_np, jnp.float32)
    signed = jnp.asarray(along_x, jnp.float32)
    node_mass = jnp.asarray(node_weight, jnp.float32)
    old_moments = jnp.dot(weighted, distribution, precision=HIGH)
    target = jnp.dot(rebuild.T, old_moments, precision=HIGH)
    thickness = collision.reshape(NL, TUBES)

    def sweep_block(inputs):
        goal_part, heading, old_part = inputs
        node_speed = jnp.abs(heading)[:, None, None]
        denominator = node_speed * NL + thickness[None] + pseudo_rate
        carry_rate = node_speed * NL / denominator
        drive_term = (thickness[None] * goal_part + pseudo_rate * old_part) / denominator

        def advance(carried, inputs_here):
            value = inputs_here[0] * carried + inputs_here[1]
            return (value, value)
        start = jnp.zeros((goal_part.shape[0], TUBES), jnp.float32)
        rate_lines = jnp.moveaxis(carry_rate, 1, 0)
        drive_lines = jnp.moveaxis(drive_term, 1, 0)
        _, forward = lax.scan(advance, start, (rate_lines, drive_lines))
        _, backward = lax.scan(advance, start, (rate_lines, drive_lines), reverse=True)
        chosen = jnp.where(heading[None, :, None] > 0, forward, backward)
        return jnp.moveaxis(chosen, 0, 1)
    plane = NXI * NXI
    swept = lax.map(sweep_block, (target.reshape(NXI, plane, NL, TUBES), signed.reshape(NXI, plane), distribution.reshape(NXI, plane, NL, TUBES)))
    half_field = swept.reshape(NV, NC)
    half_moments = jnp.dot(weighted, half_field, precision=HIGH)
    residual = (half_moments - old_moments).reshape(5, NL, TUBES)
    lower_r = lower_blocks.reshape(25, NL, TUBES)
    upper_r = upper_blocks.reshape(25, NL, TUBES)
    inverse_r = diag_inverse.reshape(25, NL, TUBES)
    correction = apply_block(inverse_r, residual)
    edge_zero = jnp.zeros((5, 1, TUBES), jnp.float32)
    for sweep_index in range(JACOBI):
        from_left = jnp.concatenate([edge_zero, correction[:, :-1]], axis=1)
        from_right = jnp.concatenate([correction[:, 1:], edge_zero], axis=1)
        correction = apply_block(inverse_r, residual - apply_block(lower_r, from_left) - apply_block(upper_r, from_right))
    correction = correction.reshape(5, NC)
    macro = half_moments + correction
    synthetic = half_field + jnp.dot(rebuild.T, correction, precision=HIGH)
    totals = lax.optimization_barrier(jnp.sum(old_moments - macro, axis=1))
    loaded = node_mass * lax.optimization_barrier(jnp.sum(jnp.abs(synthetic), axis=1))
    shift_mass = jnp.zeros((), jnp.float32)
    shift_flow = jnp.zeros((), jnp.float32)
    for newton_turn in range(NEWTON):
        sums = newton_sums(loaded, signed, shift_mass, shift_flow)
        shift_mass, shift_flow = newton_update(shift_mass, shift_flow, sums, totals[0], totals[1])
    growth = jnp.exp(shift_mass + shift_flow * signed)
    new_distribution = synthetic + jnp.abs(synthetic) * (growth[:, None] - 1.0)
    return (new_distribution, macro)
```

```python
import math

import jax
import jax.numpy as jnp
import numpy as np
from jax import lax
from jax.sharding import PartitionSpec as P

NXI = 24
TUBES = 128
JACOBI = 4
NEWTON = 2


HIGH = lax.Precision.HIGHEST
pseudo_rate = 1.0


def passed_along(block, axis, distance):
    devices = range(lax.axis_size(axis))
    route = [(i - distance, i) for i in devices if i - distance in devices]
    return lax.ppermute(block, axis, route)


def extended(array, sides, width):
    for axis, dim in sides:
        count, length = (lax.axis_size(axis), array.shape[dim])
        up = [(i, (i + 1) % count) for i in range(count - 1)]
        down = [(j, i) for i, j in up]
        last = lax.slice_in_dim(array, length - width, length, axis=dim)
        first = lax.slice_in_dim(array, 0, width, axis=dim)
        before = lax.ppermute(last, axis, up)
        after = lax.ppermute(first, axis, down)
        array = jnp.concatenate([before, array, after], axis=dim)
    return array


def hermite_rule(count):
    quarter = math.pi ** (-0.25)
    found = []
    last_slope = 1.0
    for index in range(count // 2):
        if index == 0:
            guess = math.sqrt(2.0 * count + 1.0) - 1.85575 * (2.0 * count + 1.0) ** (-0.16667)
        elif index == 1:
            guess = guess - 1.14 * count**0.426 / guess
        elif index == 2:
            guess = 1.86 * guess - 0.86 * found[0][0]
        elif index == 3:
            guess = 1.91 * guess - 0.91 * found[1][0]
        else:
            guess = 2.0 * guess - found[index - 2][0]
        for repeat in range(60):
            current = quarter
            previous = 0.0
            for order in range(count):
                older = previous
                previous = current
                current = (
                    guess * math.sqrt(2.0 / (order + 1)) * previous
                    - math.sqrt(order / (order + 1.0)) * older
                )
            last_slope = math.sqrt(2.0 * count) * previous
            guess = guess - current / last_slope
        found.append((guess, 2.0 / (last_slope * last_slope)))
    positive = found[::-1]
    points = [-pair[0] for pair in found] + [pair[0] for pair in positive]
    weights = [pair[1] for pair in found] + [pair[1] for pair in positive]
    return (np.array(points), np.array(weights))


def node_tables(axis_points):
    points, weights = hermite_rule(axis_points)
    node_index = np.arange(axis_points**3)
    idx_x = node_index % axis_points
    idx_z = node_index // axis_points % axis_points
    idx_y = node_index // (axis_points * axis_points)
    along_x = points[idx_x]
    along_y = points[idx_y]
    along_z = points[idx_z]
    node_weight = weights[idx_x] * weights[idx_y] * weights[idx_z] / math.pi**1.5
    energy = along_x**2 + along_y**2 + along_z**2 - 1.5
    moment_basis = np.stack([along_x * 0.0 + 1.0, along_x, along_y, along_z, energy])
    norm_scale = np.array([1.0, 0.5, 0.5, 0.5, 1.5])
    return (
        along_x,
        node_weight,
        moment_basis * node_weight[None, :],
        moment_basis / norm_scale[:, None],
    )


def apply_block(matrices, vector):
    shaped = matrices.reshape((5, 5) + vector.shape[1:])
    return jnp.sum(shaped * vector[None], axis=1)


def affine_combine(earlier_map, later_map):
    return (later_map[0] * earlier_map[0], later_map[0] * earlier_map[1] + later_map[1])


def newton_sums(loaded, signed, shift_mass, shift_flow):
    growth = jnp.exp(shift_mass + shift_flow * signed)
    scaled = loaded * growth
    excess = loaded * (growth - 1.0)
    return jnp.stack(
        [
            jnp.sum(scaled),
            jnp.sum(scaled * signed),
            jnp.sum(scaled * signed * signed),
            jnp.sum(excess),
            jnp.sum(excess * signed),
        ]
    )


def newton_update(shift_mass, shift_flow, sums, goal_mass, goal_flow):
    resid_mass = sums[3] - goal_mass
    resid_flow = sums[4] - goal_flow
    determinant = sums[0] * sums[2] - sums[1] * sums[1]
    new_mass = shift_mass - (sums[2] * resid_mass - sums[1] * resid_flow) / determinant
    new_flow = shift_flow - (sums[0] * resid_flow - sums[1] * resid_mass) / determinant
    return (new_mass, new_flow)


def received(block, distance):
    count = lax.axis_size("sec")
    if abs(distance) >= count:
        return jnp.zeros_like(block)
    return passed_along(block, "sec", distance)


def exclusive_inflow(rate, drive, sign):
    count = lax.axis_size("sec")

    def fetch(a, b, distance):
        got = received(jnp.concatenate([a, b], axis=0), sign * distance)
        return got[:1], got[1:]

    near_a, near_b = fetch(rate, drive, 1)
    span = 1
    if count > 2:
        far_a, far_b = fetch(rate, drive, 2)
        near_a, near_b = near_a * far_a, near_a * far_b + near_b
        span = 2
    while span < count - 1:
        got_a, got_b = fetch(near_a, near_b, span)
        near_a, near_b = near_a * got_a, near_a * got_b + near_b
        span *= 2
    return near_b


def with_halo(array, width):
    parts = [received(array, d) for d in range(width, 0, -1)]
    parts.append(array)
    parts.extend(received(array, -d) for d in range(1, width + 1))
    return jnp.concatenate(parts, axis=1)


def body(distribution, collision, lower_blocks, upper_blocks, diag_inverse):
    node_count = distribution.shape[0]
    cell_count = distribution.shape[1]
    length = cell_count // TUBES
    node_rows = node_count // NXI
    half_nodes = NXI // 2
    along_x, node_weight, weighted_np, rebuild_np = node_tables(NXI)
    all_mass = jnp.asarray(node_weight, jnp.float32)
    offset = lax.axis_index("vel") * node_count
    weighted = lax.dynamic_slice_in_dim(
        jnp.asarray(weighted_np, jnp.float32), offset, node_count, 1
    )
    rebuild = lax.dynamic_slice_in_dim(jnp.asarray(rebuild_np, jnp.float32), offset, node_count, 1)
    node_mass = lax.dynamic_slice_in_dim(all_mass, offset, node_count, 0)
    line_signed = jnp.asarray(along_x[:NXI], jnp.float32)
    old_moments = lax.psum(jnp.dot(weighted, distribution, precision=HIGH), "vel")
    target = jnp.dot(rebuild.T, old_moments, precision=HIGH)
    total_length = length * lax.axis_size("sec")
    thickness = collision.reshape(1, 1, length, TUBES)
    node_speed = jnp.abs(line_signed).reshape(1, NXI, 1, 1)
    denominator = node_speed * total_length + thickness + pseudo_rate
    carry_rate = node_speed * total_length / denominator
    drive_term = (
        thickness * target.reshape(node_rows, NXI, length, TUBES)
        + pseudo_rate * distribution.reshape(node_rows, NXI, length, TUBES)
    ) / denominator
    prod_neg, local_neg = lax.associative_scan(
        affine_combine,
        (jnp.broadcast_to(carry_rate[:, :half_nodes], (1, half_nodes, length, TUBES)),
         drive_term[:, :half_nodes]),
        reverse=True,
        axis=2,
    )
    prod_pos, local_pos = lax.associative_scan(
        affine_combine,
        (jnp.broadcast_to(carry_rate[:, half_nodes:], (1, NXI - half_nodes, length, TUBES)),
         drive_term[:, half_nodes:]),
        axis=2,
    )
    inflow_pos = exclusive_inflow(prod_pos[:, :, -1], local_pos[:, :, -1], 1)
    inflow_neg = exclusive_inflow(prod_neg[:, :, 0], local_neg[:, :, 0], -1)
    field_neg = local_neg + prod_neg * inflow_neg[:, :, None, :]
    field_pos = local_pos + prod_pos * inflow_pos[:, :, None, :]
    half_field = jnp.concatenate([field_neg, field_pos], axis=1).reshape(node_count, cell_count)
    half_moments = lax.psum(jnp.dot(weighted, half_field, precision=HIGH), "vel")
    residual = (half_moments - old_moments).reshape(5, length, TUBES)
    width = min(-(-JACOBI // length), lax.axis_size("sec") - 1)
    blocks = jnp.concatenate([lower_blocks, upper_blocks, diag_inverse], axis=0)
    blocks_wide = with_halo(blocks.reshape(75, length, TUBES), width)
    lower_r = blocks_wide[:25]
    upper_r = blocks_wide[25:50]
    inverse_r = blocks_wide[50:]
    residual_wide = with_halo(residual, width)
    correction = apply_block(inverse_r, residual_wide)
    edge_zero = jnp.zeros((5, 1, TUBES), jnp.float32)
    for sweep_index in range(JACOBI):
        from_left = jnp.concatenate([edge_zero, correction[:, :-1]], axis=1)
        from_right = jnp.concatenate([correction[:, 1:], edge_zero], axis=1)
        correction = apply_block(
            inverse_r,
            residual_wide - apply_block(lower_r, from_left) - apply_block(upper_r, from_right),
        )
    correction = correction[:, width * length : (width + 1) * length].reshape(5, cell_count)
    macro = half_moments + correction
    synthetic = half_field + jnp.dot(rebuild.T, correction, precision=HIGH)
    local_totals = jnp.sum(old_moments - macro, axis=1)[0:2]
    magnitude = jnp.sum(jnp.abs(synthetic), axis=1)
    line_loaded = jnp.sum((node_mass * magnitude).reshape(node_rows, NXI), axis=0)
    first_copy = (lax.axis_index("vel") == 0).astype(jnp.float32)
    gathered = lax.psum(
        jnp.concatenate([line_loaded, local_totals * first_copy]), ("sec", "vel")
    )
    loaded = gathered[:NXI]
    goals = gathered[NXI:]
    shift_mass = jnp.zeros((), jnp.float32)
    shift_flow = jnp.zeros((), jnp.float32)
    for newton_turn in range(NEWTON):
        sums = newton_sums(loaded, line_signed, shift_mass, shift_flow)
        shift_mass, shift_flow = newton_update(shift_mass, shift_flow, sums, goals[0], goals[1])
    growth = jnp.exp(shift_mass + shift_flow * line_signed)
    synthetic_rows = synthetic.reshape(node_rows, NXI, cell_count)
    new_distribution = synthetic_rows + jnp.abs(synthetic_rows) * (growth[None, :, None] - 1.0)
    return (new_distribution.reshape(node_count, cell_count), macro)


def solution(mesh):
    in_specs = (P("vel", "sec"), P("sec"), P(None, "sec"), P(None, "sec"), P(None, "sec"))
    out_specs = (P("vel", "sec"), P(None, "sec"))
    return jax.shard_map(body, mesh=mesh, in_specs=in_specs, out_specs=out_specs, check_vma=False)
```

```python
import math

import jax
import jax.numpy as jnp
import numpy as np
from jax import lax
from jax.sharding import PartitionSpec as P

NXI = 24
TUBES = 128
JACOBI = 4
NEWTON = 2


HIGH = lax.Precision.HIGHEST
pseudo_rate = 1.0


def passed_along(block, axis, distance):
    devices = range(lax.axis_size(axis))
    route = [(i - distance, i) for i in devices if i - distance in devices]
    return lax.ppermute(block, axis, route)


def extended(array, sides, width):
    for axis, dim in sides:
        count, length = (lax.axis_size(axis), array.shape[dim])
        up = [(i, (i + 1) % count) for i in range(count - 1)]
        down = [(j, i) for i, j in up]
        last = lax.slice_in_dim(array, length - width, length, axis=dim)
        first = lax.slice_in_dim(array, 0, width, axis=dim)
        before = lax.ppermute(last, axis, up)
        after = lax.ppermute(first, axis, down)
        array = jnp.concatenate([before, array, after], axis=dim)
    return array


def hermite_rule(count):
    quarter = math.pi ** (-0.25)
    found = []
    last_slope = 1.0
    for index in range(count // 2):
        if index == 0:
            guess = math.sqrt(2.0 * count + 1.0) - 1.85575 * (2.0 * count + 1.0) ** (-0.16667)
        elif index == 1:
            guess = guess - 1.14 * count**0.426 / guess
        elif index == 2:
            guess = 1.86 * guess - 0.86 * found[0][0]
        elif index == 3:
            guess = 1.91 * guess - 0.91 * found[1][0]
        else:
            guess = 2.0 * guess - found[index - 2][0]
        for repeat in range(60):
            current = quarter
            previous = 0.0
            for order in range(count):
                older = previous
                previous = current
                current = (
                    guess * math.sqrt(2.0 / (order + 1)) * previous
                    - math.sqrt(order / (order + 1.0)) * older
                )
            last_slope = math.sqrt(2.0 * count) * previous
            guess = guess - current / last_slope
        found.append((guess, 2.0 / (last_slope * last_slope)))
    positive = found[::-1]
    points = [-pair[0] for pair in found] + [pair[0] for pair in positive]
    weights = [pair[1] for pair in found] + [pair[1] for pair in positive]
    return (np.array(points), np.array(weights))


def node_tables(axis_points):
    points, weights = hermite_rule(axis_points)
    node_index = np.arange(axis_points**3)
    idx_x = node_index % axis_points
    idx_z = node_index // axis_points % axis_points
    idx_y = node_index // (axis_points * axis_points)
    along_x = points[idx_x]
    along_y = points[idx_y]
    along_z = points[idx_z]
    node_weight = weights[idx_x] * weights[idx_y] * weights[idx_z] / math.pi**1.5
    energy = along_x**2 + along_y**2 + along_z**2 - 1.5
    moment_basis = np.stack([along_x * 0.0 + 1.0, along_x, along_y, along_z, energy])
    norm_scale = np.array([1.0, 0.5, 0.5, 0.5, 1.5])
    return (
        along_x,
        node_weight,
        moment_basis * node_weight[None, :],
        moment_basis / norm_scale[:, None],
    )


def apply_block(matrices, vector):
    shaped = matrices.reshape((5, 5) + vector.shape[1:])
    return jnp.sum(shaped * vector[None], axis=1)


def affine_combine(earlier_map, later_map):
    return (later_map[0] * earlier_map[0], later_map[0] * earlier_map[1] + later_map[1])


def newton_sums(loaded, signed, shift_mass, shift_flow):
    growth = jnp.exp(shift_mass + shift_flow * signed)
    scaled = loaded * growth
    excess = loaded * (growth - 1.0)
    return jnp.stack(
        [
            jnp.sum(scaled),
            jnp.sum(scaled * signed),
            jnp.sum(scaled * signed * signed),
            jnp.sum(excess),
            jnp.sum(excess * signed),
        ]
    )


def newton_update(shift_mass, shift_flow, sums, goal_mass, goal_flow):
    resid_mass = sums[3] - goal_mass
    resid_flow = sums[4] - goal_flow
    determinant = sums[0] * sums[2] - sums[1] * sums[1]
    new_mass = shift_mass - (sums[2] * resid_mass - sums[1] * resid_flow) / determinant
    new_flow = shift_flow - (sums[0] * resid_flow - sums[1] * resid_mass) / determinant
    return (new_mass, new_flow)


def received(block, distance):
    count = lax.axis_size("sec")
    if abs(distance) >= count:
        return jnp.zeros_like(block)
    return passed_along(block, "sec", distance)


def exclusive_inflow(rate, drive, sign):
    count = lax.axis_size("sec")

    def fetch(a, b, distance):
        got = received(jnp.concatenate([a, b], axis=0), sign * distance)
        return got[:1], got[1:]

    near_a, near_b = fetch(rate, drive, 1)
    span = 1
    if count > 2:
        far_a, far_b = fetch(rate, drive, 2)
        near_a, near_b = near_a * far_a, near_a * far_b + near_b
        span = 2
    while span < count - 1:
        got_a, got_b = fetch(near_a, near_b, span)
        near_a, near_b = near_a * got_a, near_a * got_b + near_b
        span *= 2
    return near_b


def with_halo(array, width):
    parts = [received(array, d) for d in range(width, 0, -1)]
    parts.append(array)
    parts.extend(received(array, -d) for d in range(1, width + 1))
    return jnp.concatenate(parts, axis=1)


def tree_sum(block, axes):
    for axis in axes:
        count = lax.axis_size(axis)
        if count & (count - 1):
            block = lax.psum(block, axis)
            continue
        bit = 1
        while bit < count:
            block = block + lax.ppermute(block, axis, [(i, i ^ bit) for i in range(count)])
            bit *= 2
    return block


def body(distribution, collision, lower_blocks, upper_blocks, diag_inverse):
    node_count = distribution.shape[0]
    cell_count = distribution.shape[1]
    length = cell_count // TUBES
    node_rows = node_count // NXI
    half_nodes = NXI // 2
    along_x, node_weight, weighted_np, rebuild_np = node_tables(NXI)
    all_mass = jnp.asarray(node_weight, jnp.float32)
    offset = lax.axis_index("vel") * node_count
    weighted = lax.dynamic_slice_in_dim(
        jnp.asarray(weighted_np, jnp.float32), offset, node_count, 1
    )
    rebuild = lax.dynamic_slice_in_dim(jnp.asarray(rebuild_np, jnp.float32), offset, node_count, 1)
    node_mass = lax.dynamic_slice_in_dim(all_mass, offset, node_count, 0)
    line_signed = jnp.asarray(along_x[:NXI], jnp.float32)
    old_moments = tree_sum(jnp.dot(weighted, distribution, precision=HIGH), ("vel",))
    target = jnp.dot(rebuild.T, old_moments, precision=HIGH)
    total_length = length * lax.axis_size("sec")
    thickness = collision.reshape(1, 1, length, TUBES)
    node_speed = jnp.abs(line_signed).reshape(1, NXI, 1, 1)
    denominator = node_speed * total_length + thickness + pseudo_rate
    carry_rate = node_speed * total_length / denominator
    drive_term = (
        thickness * target.reshape(node_rows, NXI, length, TUBES)
        + pseudo_rate * distribution.reshape(node_rows, NXI, length, TUBES)
    ) / denominator
    prod_neg, local_neg = lax.associative_scan(
        affine_combine,
        (jnp.broadcast_to(carry_rate[:, :half_nodes], (1, half_nodes, length, TUBES)),
         drive_term[:, :half_nodes]),
        reverse=True,
        axis=2,
    )
    prod_pos, local_pos = lax.associative_scan(
        affine_combine,
        (jnp.broadcast_to(carry_rate[:, half_nodes:], (1, NXI - half_nodes, length, TUBES)),
         drive_term[:, half_nodes:]),
        axis=2,
    )
    inflow_pos = exclusive_inflow(prod_pos[:, :, -1], local_pos[:, :, -1], 1)
    inflow_neg = exclusive_inflow(prod_neg[:, :, 0], local_neg[:, :, 0], -1)
    field_neg = local_neg + prod_neg * inflow_neg[:, :, None, :]
    field_pos = local_pos + prod_pos * inflow_pos[:, :, None, :]
    half_field = jnp.concatenate([field_neg, field_pos], axis=1).reshape(node_count, cell_count)
    half_moments = tree_sum(jnp.dot(weighted, half_field, precision=HIGH), ("vel",))
    residual = (half_moments - old_moments).reshape(5, length, TUBES)
    width = min(-(-JACOBI // length), lax.axis_size("sec") - 1)
    blocks = jnp.concatenate([lower_blocks, upper_blocks, diag_inverse], axis=0)
    blocks_wide = with_halo(blocks.reshape(75, length, TUBES), width)
    lower_r = blocks_wide[:25]
    upper_r = blocks_wide[25:50]
    inverse_r = blocks_wide[50:]
    residual_wide = with_halo(residual, width)
    correction = apply_block(inverse_r, residual_wide)
    edge_zero = jnp.zeros((5, 1, TUBES), jnp.float32)
    for sweep_index in range(JACOBI):
        from_left = jnp.concatenate([edge_zero, correction[:, :-1]], axis=1)
        from_right = jnp.concatenate([correction[:, 1:], edge_zero], axis=1)
        correction = apply_block(
            inverse_r,
            residual_wide - apply_block(lower_r, from_left) - apply_block(upper_r, from_right),
        )
    correction = correction[:, width * length : (width + 1) * length].reshape(5, cell_count)
    macro = half_moments + correction
    synthetic = half_field + jnp.dot(rebuild.T, correction, precision=HIGH)
    local_totals = jnp.sum(old_moments - macro, axis=1)[0:2]
    magnitude = jnp.sum(jnp.abs(synthetic), axis=1)
    line_loaded = jnp.sum((node_mass * magnitude).reshape(node_rows, NXI), axis=0)
    first_copy = (lax.axis_index("vel") == 0).astype(jnp.float32)
    gathered = tree_sum(
        jnp.concatenate([line_loaded, local_totals * first_copy]), ("vel", "sec")
    )
    loaded = gathered[:NXI]
    goals = gathered[NXI:]
    shift_mass = jnp.zeros((), jnp.float32)
    shift_flow = jnp.zeros((), jnp.float32)
    for newton_turn in range(NEWTON):
        sums = newton_sums(loaded, line_signed, shift_mass, shift_flow)
        shift_mass, shift_flow = newton_update(shift_mass, shift_flow, sums, goals[0], goals[1])
    growth = jnp.exp(shift_mass + shift_flow * line_signed)
    synthetic_rows = synthetic.reshape(node_rows, NXI, cell_count)
    new_distribution = synthetic_rows + jnp.abs(synthetic_rows) * (growth[None, :, None] - 1.0)
    return (new_distribution.reshape(node_count, cell_count), macro)


def solution(mesh):
    in_specs = (P("vel", "sec"), P("sec"), P(None, "sec"), P(None, "sec"), P(None, "sec"))
    out_specs = (P("vel", "sec"), P(None, "sec"))
    return jax.shard_map(body, mesh=mesh, in_specs=in_specs, out_specs=out_specs, check_vma=False)
```

```python
import math

import jax
import jax.numpy as jnp
import numpy as np
from jax import lax
from jax.sharding import PartitionSpec as P

NXI = 24
TUBES = 128
JACOBI = 4
NEWTON = 2


HIGH = lax.Precision.HIGHEST
pseudo_rate = 1.0


def passed_along(block, axis, distance):
    devices = range(lax.axis_size(axis))
    route = [(i - distance, i) for i in devices if i - distance in devices]
    return lax.ppermute(block, axis, route)


def extended(array, sides, width):
    for axis, dim in sides:
        count, length = (lax.axis_size(axis), array.shape[dim])
        up = [(i, (i + 1) % count) for i in range(count - 1)]
        down = [(j, i) for i, j in up]
        last = lax.slice_in_dim(array, length - width, length, axis=dim)
        first = lax.slice_in_dim(array, 0, width, axis=dim)
        before = lax.ppermute(last, axis, up)
        after = lax.ppermute(first, axis, down)
        array = jnp.concatenate([before, array, after], axis=dim)
    return array


def hermite_rule(count):
    quarter = math.pi ** (-0.25)
    found = []
    last_slope = 1.0
    for index in range(count // 2):
        if index == 0:
            guess = math.sqrt(2.0 * count + 1.0) - 1.85575 * (2.0 * count + 1.0) ** (-0.16667)
        elif index == 1:
            guess = guess - 1.14 * count**0.426 / guess
        elif index == 2:
            guess = 1.86 * guess - 0.86 * found[0][0]
        elif index == 3:
            guess = 1.91 * guess - 0.91 * found[1][0]
        else:
            guess = 2.0 * guess - found[index - 2][0]
        for repeat in range(60):
            current = quarter
            previous = 0.0
            for order in range(count):
                older = previous
                previous = current
                current = (
                    guess * math.sqrt(2.0 / (order + 1)) * previous
                    - math.sqrt(order / (order + 1.0)) * older
                )
            last_slope = math.sqrt(2.0 * count) * previous
            guess = guess - current / last_slope
        found.append((guess, 2.0 / (last_slope * last_slope)))
    positive = found[::-1]
    points = [-pair[0] for pair in found] + [pair[0] for pair in positive]
    weights = [pair[1] for pair in found] + [pair[1] for pair in positive]
    return (np.array(points), np.array(weights))


def node_tables(axis_points):
    points, weights = hermite_rule(axis_points)
    node_index = np.arange(axis_points**3)
    idx_x = node_index % axis_points
    idx_z = node_index // axis_points % axis_points
    idx_y = node_index // (axis_points * axis_points)
    along_x = points[idx_x]
    along_y = points[idx_y]
    along_z = points[idx_z]
    node_weight = weights[idx_x] * weights[idx_y] * weights[idx_z] / math.pi**1.5
    energy = along_x**2 + along_y**2 + along_z**2 - 1.5
    moment_basis = np.stack([along_x * 0.0 + 1.0, along_x, along_y, along_z, energy])
    norm_scale = np.array([1.0, 0.5, 0.5, 0.5, 1.5])
    return (
        along_x,
        node_weight,
        moment_basis * node_weight[None, :],
        moment_basis / norm_scale[:, None],
    )


def apply_block(matrices, vector):
    shaped = matrices.reshape((5, 5) + vector.shape[1:])
    return jnp.sum(shaped * vector[None], axis=1)


def affine_combine(earlier_map, later_map):
    return (later_map[0] * earlier_map[0], later_map[0] * earlier_map[1] + later_map[1])


def newton_sums(loaded, signed, shift_mass, shift_flow):
    growth = jnp.exp(shift_mass + shift_flow * signed)
    scaled = loaded * growth
    excess = loaded * (growth - 1.0)
    return jnp.stack(
        [
            jnp.sum(scaled),
            jnp.sum(scaled * signed),
            jnp.sum(scaled * signed * signed),
            jnp.sum(excess),
            jnp.sum(excess * signed),
        ]
    )


def newton_update(shift_mass, shift_flow, sums, goal_mass, goal_flow):
    resid_mass = sums[3] - goal_mass
    resid_flow = sums[4] - goal_flow
    determinant = sums[0] * sums[2] - sums[1] * sums[1]
    new_mass = shift_mass - (sums[2] * resid_mass - sums[1] * resid_flow) / determinant
    new_flow = shift_flow - (sums[0] * resid_flow - sums[1] * resid_mass) / determinant
    return (new_mass, new_flow)


def received(block, distance):
    count = lax.axis_size("sec")
    if abs(distance) >= count:
        return jnp.zeros_like(block)
    return passed_along(block, "sec", distance)


def exclusive_inflow(rate, drive, sign):
    count = lax.axis_size("sec")

    def fetch(a, b, distance):
        got = received(jnp.concatenate([a, b], axis=0), sign * distance)
        return got[:1], got[1:]

    near_a, near_b = fetch(rate, drive, 1)
    span = 1
    if count > 2:
        far_a, far_b = fetch(rate, drive, 2)
        near_a, near_b = near_a * far_a, near_a * far_b + near_b
        span = 2
    while span < count - 1:
        got_a, got_b = fetch(near_a, near_b, span)
        near_a, near_b = near_a * got_a, near_a * got_b + near_b
        span *= 2
    return near_b


def with_halo(array, width):
    parts = [received(array, d) for d in range(width, 0, -1)]
    parts.append(array)
    parts.extend(received(array, -d) for d in range(1, width + 1))
    return jnp.concatenate(parts, axis=1)


def tree_sum(block, axes):
    for axis in axes:
        count = lax.axis_size(axis)
        if count & (count - 1):
            block = lax.psum(block, axis)
            continue
        bit = 1
        while bit < count:
            block = block + lax.ppermute(block, axis, [(i, i ^ bit) for i in range(count)])
            bit *= 2
    return block


def body(distribution, collision, lower_blocks, upper_blocks, diag_inverse):
    node_count = distribution.shape[0]
    cell_count = distribution.shape[1]
    length = cell_count // TUBES
    node_rows = node_count // NXI
    half_nodes = NXI // 2
    along_x, node_weight, weighted_np, rebuild_np = node_tables(NXI)
    all_mass = jnp.asarray(node_weight, jnp.float32)
    offset = lax.axis_index("vel") * node_count
    weighted = lax.dynamic_slice_in_dim(
        jnp.asarray(weighted_np, jnp.float32), offset, node_count, 1
    )
    rebuild = lax.dynamic_slice_in_dim(jnp.asarray(rebuild_np, jnp.float32), offset, node_count, 1)
    node_mass = lax.dynamic_slice_in_dim(all_mass, offset, node_count, 0)
    line_signed = jnp.asarray(along_x[:NXI], jnp.float32)
    old_moments = tree_sum(jnp.dot(weighted, distribution, precision=HIGH), ("vel",))
    target = jnp.dot(rebuild.T, old_moments, precision=HIGH)
    total_length = length * lax.axis_size("sec")
    thickness = collision.reshape(1, 1, length, TUBES)
    node_speed = jnp.abs(line_signed).reshape(1, NXI, 1, 1)
    denominator = node_speed * total_length + thickness + pseudo_rate
    carry_rate = node_speed * total_length / denominator
    drive_term = (
        thickness * target.reshape(node_rows, NXI, length, TUBES)
        + pseudo_rate * distribution.reshape(node_rows, NXI, length, TUBES)
    ) / denominator
    prod_neg, local_neg = lax.associative_scan(
        affine_combine,
        (jnp.broadcast_to(carry_rate[:, :half_nodes], (1, half_nodes, length, TUBES)),
         drive_term[:, :half_nodes]),
        reverse=True,
        axis=2,
    )
    prod_pos, local_pos = lax.associative_scan(
        affine_combine,
        (jnp.broadcast_to(carry_rate[:, half_nodes:], (1, NXI - half_nodes, length, TUBES)),
         drive_term[:, half_nodes:]),
        axis=2,
    )
    inflow_pos = exclusive_inflow(prod_pos[:, :, -1], local_pos[:, :, -1], 1)
    inflow_neg = exclusive_inflow(prod_neg[:, :, 0], local_neg[:, :, 0], -1)
    field_neg = local_neg + prod_neg * inflow_neg[:, :, None, :]
    field_pos = local_pos + prod_pos * inflow_pos[:, :, None, :]
    half_field = jnp.concatenate([field_neg, field_pos], axis=1).reshape(node_count, cell_count)
    half_moments = tree_sum(jnp.dot(weighted, half_field, precision=HIGH), ("vel",))
    residual = (half_moments - old_moments).reshape(5, length, TUBES)
    width = min(-(-JACOBI // length), lax.axis_size("sec") - 1)
    blocks = jnp.concatenate([lower_blocks, upper_blocks, diag_inverse], axis=0)
    blocks_wide = with_halo(blocks.reshape(75, length, TUBES), width)
    lower_r = blocks_wide[:25]
    upper_r = blocks_wide[25:50]
    inverse_r = blocks_wide[50:]
    residual_wide = with_halo(residual, width)
    correction = apply_block(inverse_r, residual_wide)
    edge_zero = jnp.zeros((5, 1, TUBES), jnp.float32)
    for sweep_index in range(JACOBI):
        from_left = jnp.concatenate([edge_zero, correction[:, :-1]], axis=1)
        from_right = jnp.concatenate([correction[:, 1:], edge_zero], axis=1)
        correction = apply_block(
            inverse_r,
            residual_wide - apply_block(lower_r, from_left) - apply_block(upper_r, from_right),
        )
    correction = correction[:, width * length : (width + 1) * length].reshape(5, cell_count)
    macro = half_moments + correction
    synthetic = half_field + jnp.dot(rebuild.T, correction, precision=HIGH)
    local_totals = jnp.sum(old_moments - macro, axis=1)[0:2]
    magnitude = jnp.sum(jnp.abs(synthetic), axis=1)
    line_loaded = jnp.sum((node_mass * magnitude).reshape(node_rows, NXI), axis=0)
    first_copy = (lax.axis_index("vel") == 0).astype(jnp.float32)
    gathered = tree_sum(
        jnp.concatenate([line_loaded, local_totals * first_copy]), ("vel", "sec")
    )
    loaded = gathered[:NXI]
    goal_mass = jnp.broadcast_to(gathered[NXI], (NXI,))
    goal_flow = jnp.broadcast_to(gathered[NXI + 1], (NXI,))
    spread = jnp.ones((NXI, NXI), jnp.float32)
    shift_mass = jnp.zeros((NXI,), jnp.float32)
    shift_flow = jnp.zeros((NXI,), jnp.float32)
    for newton_turn in range(NEWTON):
        growth = jnp.exp(shift_mass + shift_flow * line_signed)
        scaled = loaded * growth
        excess = loaded * (growth - 1.0)
        terms = jnp.stack(
            [scaled, scaled * line_signed, scaled * line_signed * line_signed, excess, excess * line_signed]
        )
        sums = jnp.dot(terms, spread, precision=HIGH)
        shift_mass, shift_flow = newton_update(shift_mass, shift_flow, sums, goal_mass, goal_flow)
    growth = jnp.exp(shift_mass + shift_flow * line_signed)
    synthetic_rows = synthetic.reshape(node_rows, NXI, cell_count)
    new_distribution = synthetic_rows + jnp.abs(synthetic_rows) * (growth[None, :, None] - 1.0)
    return (new_distribution.reshape(node_count, cell_count), macro)


def solution(mesh):
    in_specs = (P("vel", "sec"), P("sec"), P(None, "sec"), P(None, "sec"), P(None, "sec"))
    out_specs = (P("vel", "sec"), P(None, "sec"))
    return jax.shard_map(body, mesh=mesh, in_specs=in_specs, out_specs=out_specs, check_vma=False)
```

```python
import math

import jax
import jax.numpy as jnp
import numpy as np
from jax import lax
from jax.sharding import PartitionSpec as P

NXI = 24
TUBES = 128
JACOBI = 4
NEWTON = 2


HIGH = lax.Precision.HIGHEST
pseudo_rate = 1.0


def passed_along(block, axis, distance):
    devices = range(lax.axis_size(axis))
    route = [(i - distance, i) for i in devices if i - distance in devices]
    return lax.ppermute(block, axis, route)


def extended(array, sides, width):
    for axis, dim in sides:
        count, length = (lax.axis_size(axis), array.shape[dim])
        up = [(i, (i + 1) % count) for i in range(count - 1)]
        down = [(j, i) for i, j in up]
        last = lax.slice_in_dim(array, length - width, length, axis=dim)
        first = lax.slice_in_dim(array, 0, width, axis=dim)
        before = lax.ppermute(last, axis, up)
        after = lax.ppermute(first, axis, down)
        array = jnp.concatenate([before, array, after], axis=dim)
    return array


def hermite_rule(count):
    quarter = math.pi ** (-0.25)
    found = []
    last_slope = 1.0
    for index in range(count // 2):
        if index == 0:
            guess = math.sqrt(2.0 * count + 1.0) - 1.85575 * (2.0 * count + 1.0) ** (-0.16667)
        elif index == 1:
            guess = guess - 1.14 * count**0.426 / guess
        elif index == 2:
            guess = 1.86 * guess - 0.86 * found[0][0]
        elif index == 3:
            guess = 1.91 * guess - 0.91 * found[1][0]
        else:
            guess = 2.0 * guess - found[index - 2][0]
        for repeat in range(60):
            current = quarter
            previous = 0.0
            for order in range(count):
                older = previous
                previous = current
                current = (
                    guess * math.sqrt(2.0 / (order + 1)) * previous
                    - math.sqrt(order / (order + 1.0)) * older
                )
            last_slope = math.sqrt(2.0 * count) * previous
            guess = guess - current / last_slope
        found.append((guess, 2.0 / (last_slope * last_slope)))
    positive = found[::-1]
    points = [-pair[0] for pair in found] + [pair[0] for pair in positive]
    weights = [pair[1] for pair in found] + [pair[1] for pair in positive]
    return (np.array(points), np.array(weights))


def node_tables(axis_points):
    points, weights = hermite_rule(axis_points)
    node_index = np.arange(axis_points**3)
    idx_x = node_index % axis_points
    idx_z = node_index // axis_points % axis_points
    idx_y = node_index // (axis_points * axis_points)
    along_x = points[idx_x]
    along_y = points[idx_y]
    along_z = points[idx_z]
    node_weight = weights[idx_x] * weights[idx_y] * weights[idx_z] / math.pi**1.5
    energy = along_x**2 + along_y**2 + along_z**2 - 1.5
    moment_basis = np.stack([along_x * 0.0 + 1.0, along_x, along_y, along_z, energy])
    norm_scale = np.array([1.0, 0.5, 0.5, 0.5, 1.5])
    return (
        along_x,
        node_weight,
        moment_basis * node_weight[None, :],
        moment_basis / norm_scale[:, None],
    )


def apply_block(matrices, vector):
    shaped = matrices.reshape((5, 5) + vector.shape[1:])
    return jnp.sum(shaped * vector[None], axis=1)


def affine_combine(earlier_map, later_map):
    return (later_map[0] * earlier_map[0], later_map[0] * earlier_map[1] + later_map[1])


def newton_sums(loaded, signed, shift_mass, shift_flow):
    growth = jnp.exp(shift_mass + shift_flow * signed)
    scaled = loaded * growth
    excess = loaded * (growth - 1.0)
    return jnp.stack(
        [
            jnp.sum(scaled),
            jnp.sum(scaled * signed),
            jnp.sum(scaled * signed * signed),
            jnp.sum(excess),
            jnp.sum(excess * signed),
        ]
    )


def newton_update(shift_mass, shift_flow, sums, goal_mass, goal_flow):
    resid_mass = sums[3] - goal_mass
    resid_flow = sums[4] - goal_flow
    determinant = sums[0] * sums[2] - sums[1] * sums[1]
    new_mass = shift_mass - (sums[2] * resid_mass - sums[1] * resid_flow) / determinant
    new_flow = shift_flow - (sums[0] * resid_flow - sums[1] * resid_mass) / determinant
    return (new_mass, new_flow)


def received(block, distance):
    count = lax.axis_size("sec")
    if abs(distance) >= count:
        return jnp.zeros_like(block)
    return passed_along(block, "sec", distance)


def fetched(state, distance, sign):
    rate, drive = state
    got = received(jnp.concatenate([rate, drive], axis=0), sign * distance)
    return got[:1], got[1:]


def scan_first(rate, drive, sign):
    near_a, near_b = fetched((rate, drive), 1, sign)
    if lax.axis_size("sec") <= 2:
        return (near_a, near_b), 1
    far_a, far_b = fetched((rate, drive), 2, sign)
    return (near_a * far_a, near_a * far_b + near_b), 2


def scan_next(state, span, sign):
    got_a, got_b = fetched(state, span, sign)
    return (state[0] * got_a, state[0] * got_b + state[1]), span * 2


def exclusive_inflow(rate, drive, sign):
    state, span = scan_first(rate, drive, sign)
    while span < lax.axis_size("sec") - 1:
        state, span = scan_next(state, span, sign)
    return state[1]


def with_halo(array, width):
    parts = [received(array, d) for d in range(width, 0, -1)]
    parts.append(array)
    parts.extend(received(array, -d) for d in range(1, width + 1))
    return jnp.concatenate(parts, axis=1)


def tree_sum(block, axes):
    for axis in axes:
        count = lax.axis_size(axis)
        if count & (count - 1):
            block = lax.psum(block, axis)
            continue
        bit = 1
        while bit < count:
            block = block + lax.ppermute(block, axis, [(i, i ^ bit) for i in range(count)])
            bit *= 2
    return block


def local_sweep(carry_rate, drive):
    half_nodes = NXI // 2
    shape = (1, half_nodes) + drive.shape[2:]
    prod_neg, local_neg = lax.associative_scan(
        affine_combine,
        (jnp.broadcast_to(carry_rate[:, :half_nodes], shape), drive[:, :half_nodes]),
        reverse=True,
        axis=2,
    )
    prod_pos, local_pos = lax.associative_scan(
        affine_combine,
        (jnp.broadcast_to(carry_rate[:, half_nodes:], shape), drive[:, half_nodes:]),
        axis=2,
    )
    return prod_neg, local_neg, prod_pos, local_pos


def joined_field(sweep, inflow_neg, inflow_pos):
    prod_neg, local_neg, prod_pos, local_pos = sweep
    field_neg = local_neg + prod_neg * inflow_neg[:, :, None, :]
    field_pos = local_pos + prod_pos * inflow_pos[:, :, None, :]
    return jnp.concatenate([field_neg, field_pos], axis=1)


def swept_field(carry_rate, drive):
    sweep = local_sweep(carry_rate, drive)
    inflow_pos = exclusive_inflow(sweep[2][:, :, -1], sweep[3][:, :, -1], 1)
    inflow_neg = exclusive_inflow(sweep[0][:, :, 0], sweep[1][:, :, 0], -1)
    return joined_field(sweep, inflow_neg, inflow_pos)


def scan_beside_sum(sweep, block, axis):
    count = lax.axis_size("sec")
    pos, span = scan_first(sweep[2][:, :, -1], sweep[3][:, :, -1], 1)
    neg, _ = scan_first(sweep[0][:, :, 0], sweep[1][:, :, 0], -1)
    members = lax.axis_size(axis)
    bit = 1
    if members & (members - 1):
        block = lax.psum(block, axis)
        bit = members
    elif bit < members:
        block = block + lax.ppermute(block, axis, [(i, i ^ bit) for i in range(members)])
        bit *= 2
    pos, neg, block = lax.optimization_barrier((pos, neg, block))
    while span < count - 1 or bit < members:
        if span < count - 1:
            pos, next_span = scan_next(pos, span, 1)
            neg, _ = scan_next(neg, span, -1)
            span = next_span
        if bit < members:
            block = block + lax.ppermute(block, axis, [(i, i ^ bit) for i in range(members)])
            bit *= 2
        pos, neg, block = lax.optimization_barrier((pos, neg, block))
    return joined_field(sweep, neg[1], pos[1]), block


def body(distribution, collision, lower_blocks, upper_blocks, diag_inverse):
    node_count = distribution.shape[0]
    cell_count = distribution.shape[1]
    length = cell_count // TUBES
    node_rows = node_count // NXI
    half_nodes = NXI // 2
    along_x, node_weight, weighted_np, rebuild_np = node_tables(NXI)
    all_mass = jnp.asarray(node_weight, jnp.float32)
    offset = lax.axis_index("vel") * node_count
    weighted = lax.dynamic_slice_in_dim(
        jnp.asarray(weighted_np, jnp.float32), offset, node_count, 1
    )
    rebuild = lax.dynamic_slice_in_dim(jnp.asarray(rebuild_np, jnp.float32), offset, node_count, 1)
    node_mass = lax.dynamic_slice_in_dim(all_mass, offset, node_count, 0)
    line_signed = jnp.asarray(along_x[:NXI], jnp.float32)
    total_length = length * lax.axis_size("sec")
    thickness = collision.reshape(1, 1, length, TUBES)
    node_speed = jnp.abs(line_signed).reshape(1, NXI, 1, 1)
    denominator = node_speed * total_length + thickness + pseudo_rate
    carry_rate = node_speed * total_length / denominator
    own_drive = pseudo_rate * distribution.reshape(node_rows, NXI, length, TUBES) / denominator
    own_field, old_moments = scan_beside_sum(
        local_sweep(carry_rate, own_drive),
        jnp.dot(weighted, distribution, precision=HIGH),
        "vel",
    )
    moment_drive = thickness * old_moments.reshape(5, 1, length, TUBES) / denominator
    moment_field = swept_field(carry_rate, moment_drive)
    basis = rebuild.reshape(5, node_rows, NXI, 1, 1)
    half_field = own_field + jnp.sum(basis * moment_field[:, None], axis=0)
    half_field = half_field.reshape(node_count, cell_count)
    half_moments = tree_sum(jnp.dot(weighted, half_field, precision=HIGH), ("vel",))
    residual = (half_moments - old_moments).reshape(5, length, TUBES)
    width = min(-(-JACOBI // length), lax.axis_size("sec") - 1)
    blocks = jnp.concatenate([lower_blocks, upper_blocks, diag_inverse], axis=0)
    blocks_wide = with_halo(blocks.reshape(75, length, TUBES), width)
    lower_r = blocks_wide[:25]
    upper_r = blocks_wide[25:50]
    inverse_r = blocks_wide[50:]
    residual_wide = with_halo(residual, width)
    correction = apply_block(inverse_r, residual_wide)
    edge_zero = jnp.zeros((5, 1, TUBES), jnp.float32)
    for sweep_index in range(JACOBI):
        from_left = jnp.concatenate([edge_zero, correction[:, :-1]], axis=1)
        from_right = jnp.concatenate([correction[:, 1:], edge_zero], axis=1)
        correction = apply_block(
            inverse_r,
            residual_wide - apply_block(lower_r, from_left) - apply_block(upper_r, from_right),
        )
    correction = correction[:, width * length : (width + 1) * length].reshape(5, cell_count)
    macro = half_moments + correction
    synthetic = half_field + jnp.dot(rebuild.T, correction, precision=HIGH)
    local_totals = jnp.sum(old_moments - macro, axis=1)[0:2]
    magnitude = jnp.sum(jnp.abs(synthetic), axis=1)
    line_loaded = jnp.sum((node_mass * magnitude).reshape(node_rows, NXI), axis=0)
    first_copy = (lax.axis_index("vel") == 0).astype(jnp.float32)
    gathered = tree_sum(
        jnp.concatenate([line_loaded, local_totals * first_copy]), ("vel", "sec")
    )
    loaded = gathered[:NXI]
    goal_mass = jnp.broadcast_to(gathered[NXI], (NXI,))
    goal_flow = jnp.broadcast_to(gathered[NXI + 1], (NXI,))
    spread = jnp.ones((NXI, NXI), jnp.float32)
    shift_mass = jnp.zeros((NXI,), jnp.float32)
    shift_flow = jnp.zeros((NXI,), jnp.float32)
    for newton_turn in range(NEWTON):
        growth = jnp.exp(shift_mass + shift_flow * line_signed)
        scaled = loaded * growth
        excess = loaded * (growth - 1.0)
        terms = jnp.stack(
            [scaled, scaled * line_signed, scaled * line_signed * line_signed, excess, excess * line_signed]
        )
        sums = jnp.dot(terms, spread, precision=HIGH)
        shift_mass, shift_flow = newton_update(shift_mass, shift_flow, sums, goal_mass, goal_flow)
    growth = jnp.exp(shift_mass + shift_flow * line_signed)
    synthetic_rows = synthetic.reshape(node_rows, NXI, cell_count)
    new_distribution = synthetic_rows + jnp.abs(synthetic_rows) * (growth[None, :, None] - 1.0)
    return (new_distribution.reshape(node_count, cell_count), macro)


def solution(mesh):
    in_specs = (P("vel", "sec"), P("sec"), P(None, "sec"), P(None, "sec"), P(None, "sec"))
    out_specs = (P("vel", "sec"), P(None, "sec"))
    return jax.shard_map(body, mesh=mesh, in_specs=in_specs, out_specs=out_specs, check_vma=False)
```

```python
import math

import jax
import jax.numpy as jnp
import numpy as np
from jax import lax
from jax.sharding import PartitionSpec as P

NXI = 24
TUBES = 128
JACOBI = 4
NEWTON = 2


HIGH = lax.Precision.HIGHEST
pseudo_rate = 1.0


def passed_along(block, axis, distance):
    devices = range(lax.axis_size(axis))
    route = [(i - distance, i) for i in devices if i - distance in devices]
    return lax.ppermute(block, axis, route)


def extended(array, sides, width):
    for axis, dim in sides:
        count, length = (lax.axis_size(axis), array.shape[dim])
        up = [(i, (i + 1) % count) for i in range(count - 1)]
        down = [(j, i) for i, j in up]
        last = lax.slice_in_dim(array, length - width, length, axis=dim)
        first = lax.slice_in_dim(array, 0, width, axis=dim)
        before = lax.ppermute(last, axis, up)
        after = lax.ppermute(first, axis, down)
        array = jnp.concatenate([before, array, after], axis=dim)
    return array


def hermite_rule(count):
    quarter = math.pi ** (-0.25)
    found = []
    last_slope = 1.0
    for index in range(count // 2):
        if index == 0:
            guess = math.sqrt(2.0 * count + 1.0) - 1.85575 * (2.0 * count + 1.0) ** (-0.16667)
        elif index == 1:
            guess = guess - 1.14 * count**0.426 / guess
        elif index == 2:
            guess = 1.86 * guess - 0.86 * found[0][0]
        elif index == 3:
            guess = 1.91 * guess - 0.91 * found[1][0]
        else:
            guess = 2.0 * guess - found[index - 2][0]
        for repeat in range(60):
            current = quarter
            previous = 0.0
            for order in range(count):
                older = previous
                previous = current
                current = (
                    guess * math.sqrt(2.0 / (order + 1)) * previous
                    - math.sqrt(order / (order + 1.0)) * older
                )
            last_slope = math.sqrt(2.0 * count) * previous
            guess = guess - current / last_slope
        found.append((guess, 2.0 / (last_slope * last_slope)))
    positive = found[::-1]
    points = [-pair[0] for pair in found] + [pair[0] for pair in positive]
    weights = [pair[1] for pair in found] + [pair[1] for pair in positive]
    return (np.array(points), np.array(weights))


def node_tables(axis_points):
    points, weights = hermite_rule(axis_points)
    node_index = np.arange(axis_points**3)
    idx_x = node_index % axis_points
    idx_z = node_index // axis_points % axis_points
    idx_y = node_index // (axis_points * axis_points)
    along_x = points[idx_x]
    along_y = points[idx_y]
    along_z = points[idx_z]
    node_weight = weights[idx_x] * weights[idx_y] * weights[idx_z] / math.pi**1.5
    energy = along_x**2 + along_y**2 + along_z**2 - 1.5
    moment_basis = np.stack([along_x * 0.0 + 1.0, along_x, along_y, along_z, energy])
    norm_scale = np.array([1.0, 0.5, 0.5, 0.5, 1.5])
    return (
        along_x,
        node_weight,
        moment_basis * node_weight[None, :],
        moment_basis / norm_scale[:, None],
    )


def apply_block(matrices, vector):
    shaped = matrices.reshape((5, 5) + vector.shape[1:])
    return jnp.sum(shaped * vector[None], axis=1)


def affine_combine(earlier_map, later_map):
    return (later_map[0] * earlier_map[0], later_map[0] * earlier_map[1] + later_map[1])


def newton_sums(loaded, signed, shift_mass, shift_flow):
    growth = jnp.exp(shift_mass + shift_flow * signed)
    scaled = loaded * growth
    excess = loaded * (growth - 1.0)
    return jnp.stack(
        [
            jnp.sum(scaled),
            jnp.sum(scaled * signed),
            jnp.sum(scaled * signed * signed),
            jnp.sum(excess),
            jnp.sum(excess * signed),
        ]
    )


def newton_update(shift_mass, shift_flow, sums, goal_mass, goal_flow):
    resid_mass = sums[3] - goal_mass
    resid_flow = sums[4] - goal_flow
    determinant = sums[0] * sums[2] - sums[1] * sums[1]
    new_mass = shift_mass - (sums[2] * resid_mass - sums[1] * resid_flow) / determinant
    new_flow = shift_flow - (sums[0] * resid_flow - sums[1] * resid_mass) / determinant
    return (new_mass, new_flow)


def received(block, distance):
    count = lax.axis_size("sec")
    if abs(distance) >= count:
        return jnp.zeros_like(block)
    return passed_along(block, "sec", distance)


def fetched(state, distance, sign):
    rate, drive = state
    got = received(jnp.concatenate([rate, drive], axis=0), sign * distance)
    return got[:1], got[1:]


def scan_first(rate, drive, sign):
    near_a, near_b = fetched((rate, drive), 1, sign)
    if lax.axis_size("sec") <= 2:
        return (near_a, near_b), 1
    far_a, far_b = fetched((rate, drive), 2, sign)
    return (near_a * far_a, near_a * far_b + near_b), 2


def scan_next(state, span, sign):
    got_a, got_b = fetched(state, span, sign)
    return (state[0] * got_a, state[0] * got_b + state[1]), span * 2


def exclusive_inflow(rate, drive, sign):
    state, span = scan_first(rate, drive, sign)
    while span < lax.axis_size("sec") - 1:
        state, span = scan_next(state, span, sign)
    return state[1]


def with_halo(array, width):
    parts = [received(array, d) for d in range(width, 0, -1)]
    parts.append(array)
    parts.extend(received(array, -d) for d in range(1, width + 1))
    return jnp.concatenate(parts, axis=1)


def tree_sum(block, axes):
    for axis in axes:
        count = lax.axis_size(axis)
        if count & (count - 1):
            block = lax.psum(block, axis)
            continue
        bit = 1
        while bit < count:
            block = block + lax.ppermute(block, axis, [(i, i ^ bit) for i in range(count)])
            bit *= 2
    return block


def local_sweep(carry_rate, drive):
    half_nodes = NXI // 2
    shape = (1, half_nodes) + drive.shape[2:]
    prod_neg, local_neg = lax.associative_scan(
        affine_combine,
        (jnp.broadcast_to(carry_rate[:, :half_nodes], shape), drive[:, :half_nodes]),
        reverse=True,
        axis=2,
    )
    prod_pos, local_pos = lax.associative_scan(
        affine_combine,
        (jnp.broadcast_to(carry_rate[:, half_nodes:], shape), drive[:, half_nodes:]),
        axis=2,
    )
    return prod_neg, local_neg, prod_pos, local_pos


def joined_field(sweep, inflow_neg, inflow_pos):
    prod_neg, local_neg, prod_pos, local_pos = sweep
    field_neg = local_neg + prod_neg * inflow_neg[:, :, None, :]
    field_pos = local_pos + prod_pos * inflow_pos[:, :, None, :]
    return jnp.concatenate([field_neg, field_pos], axis=1)


def swept_field(carry_rate, drive):
    sweep = local_sweep(carry_rate, drive)
    inflow_pos = exclusive_inflow(sweep[2][:, :, -1], sweep[3][:, :, -1], 1)
    inflow_neg = exclusive_inflow(sweep[0][:, :, 0], sweep[1][:, :, 0], -1)
    return joined_field(sweep, inflow_neg, inflow_pos)


def body(distribution, collision, lower_blocks, upper_blocks, diag_inverse):
    node_count = distribution.shape[0]
    cell_count = distribution.shape[1]
    length = cell_count // TUBES
    node_rows = node_count // NXI
    half_nodes = NXI // 2
    along_x, node_weight, weighted_np, rebuild_np = node_tables(NXI)
    all_mass = jnp.asarray(node_weight, jnp.float32)
    offset = lax.axis_index("vel") * node_count
    weighted = lax.dynamic_slice_in_dim(
        jnp.asarray(weighted_np, jnp.float32), offset, node_count, 1
    )
    rebuild = lax.dynamic_slice_in_dim(jnp.asarray(rebuild_np, jnp.float32), offset, node_count, 1)
    node_mass = lax.dynamic_slice_in_dim(all_mass, offset, node_count, 0)
    line_signed = jnp.asarray(along_x[:NXI], jnp.float32)
    total_length = length * lax.axis_size("sec")
    thickness = collision.reshape(1, 1, length, TUBES)
    node_speed = jnp.abs(line_signed).reshape(1, NXI, 1, 1)
    denominator = node_speed * total_length + thickness + pseudo_rate
    carry_rate = node_speed * total_length / denominator
    own_drive = pseudo_rate * distribution.reshape(node_rows, NXI, length, TUBES) / denominator
    count = lax.axis_size("sec")
    own_sweep = local_sweep(carry_rate, own_drive)
    own_pos, own_span = scan_first(own_sweep[2][:, :, -1], own_sweep[3][:, :, -1], 1)
    own_neg, _ = scan_first(own_sweep[0][:, :, 0], own_sweep[1][:, :, 0], -1)
    old_moments = tree_sum(jnp.dot(weighted, distribution, precision=HIGH), ("vel",))
    own_pos, own_neg, old_moments = lax.optimization_barrier((own_pos, own_neg, old_moments))
    moment_drive = thickness * old_moments.reshape(5, 1, length, TUBES) / denominator
    moment_sweep = local_sweep(carry_rate, moment_drive)
    moment_pos, moment_span = scan_first(moment_sweep[2][:, :, -1], moment_sweep[3][:, :, -1], 1)
    moment_neg, _ = scan_first(moment_sweep[0][:, :, 0], moment_sweep[1][:, :, 0], -1)
    while True:
        if own_span < count - 1:
            own_pos, next_span = scan_next(own_pos, own_span, 1)
            own_neg, _ = scan_next(own_neg, own_span, -1)
            own_span = next_span
        own_pos, own_neg, moment_pos, moment_neg = lax.optimization_barrier(
            (own_pos, own_neg, moment_pos, moment_neg)
        )
        if moment_span >= count - 1 and own_span >= count - 1:
            break
        if moment_span < count - 1:
            moment_pos, next_span = scan_next(moment_pos, moment_span, 1)
            moment_neg, _ = scan_next(moment_neg, moment_span, -1)
            moment_span = next_span
    own_field = joined_field(own_sweep, own_neg[1], own_pos[1])
    moment_field = joined_field(moment_sweep, moment_neg[1], moment_pos[1])
    basis = rebuild.reshape(5, node_rows, NXI, 1, 1)
    half_field = own_field + jnp.sum(basis * moment_field[:, None], axis=0)
    half_field = half_field.reshape(node_count, cell_count)
    half_moments = tree_sum(jnp.dot(weighted, half_field, precision=HIGH), ("vel",))
    residual = (half_moments - old_moments).reshape(5, length, TUBES)
    width = min(-(-JACOBI // length), lax.axis_size("sec") - 1)
    blocks = jnp.concatenate([lower_blocks, upper_blocks, diag_inverse], axis=0)
    wide = with_halo(
        jnp.concatenate([blocks.reshape(75, length, TUBES), residual], axis=0), width
    )
    lower_r = wide[:25]
    upper_r = wide[25:50]
    inverse_r = wide[50:75]
    residual_wide = wide[75:]
    correction = apply_block(inverse_r, residual_wide)
    edge_zero = jnp.zeros((5, 1, TUBES), jnp.float32)
    for sweep_index in range(JACOBI):
        from_left = jnp.concatenate([edge_zero, correction[:, :-1]], axis=1)
        from_right = jnp.concatenate([correction[:, 1:], edge_zero], axis=1)
        correction = apply_block(
            inverse_r,
            residual_wide - apply_block(lower_r, from_left) - apply_block(upper_r, from_right),
        )
    correction = correction[:, width * length : (width + 1) * length].reshape(5, cell_count)
    macro = half_moments + correction
    synthetic = half_field + jnp.dot(rebuild.T, correction, precision=HIGH)
    local_totals = jnp.sum(old_moments - macro, axis=1)[0:2]
    magnitude = jnp.sum(jnp.abs(synthetic), axis=1)
    line_loaded = jnp.sum((node_mass * magnitude).reshape(node_rows, NXI), axis=0)
    first_copy = (lax.axis_index("vel") == 0).astype(jnp.float32)
    gathered = tree_sum(
        jnp.concatenate([line_loaded, local_totals * first_copy]), ("vel", "sec")
    )
    loaded = gathered[:NXI]
    goal_mass = jnp.broadcast_to(gathered[NXI], (NXI,))
    goal_flow = jnp.broadcast_to(gathered[NXI + 1], (NXI,))
    spread = jnp.ones((NXI, NXI), jnp.float32)
    shift_mass = jnp.zeros((NXI,), jnp.float32)
    shift_flow = jnp.zeros((NXI,), jnp.float32)
    for newton_turn in range(NEWTON):
        growth = jnp.exp(shift_mass + shift_flow * line_signed)
        scaled = loaded * growth
        excess = loaded * (growth - 1.0)
        terms = jnp.stack(
            [scaled, scaled * line_signed, scaled * line_signed * line_signed, excess, excess * line_signed]
        )
        sums = jnp.dot(terms, spread, precision=HIGH)
        shift_mass, shift_flow = newton_update(shift_mass, shift_flow, sums, goal_mass, goal_flow)
    growth = jnp.exp(shift_mass + shift_flow * line_signed)
    synthetic_rows = synthetic.reshape(node_rows, NXI, cell_count)
    new_distribution = synthetic_rows + jnp.abs(synthetic_rows) * (growth[None, :, None] - 1.0)
    return (new_distribution.reshape(node_count, cell_count), macro)


def solution(mesh):
    in_specs = (P("vel", "sec"), P("sec"), P(None, "sec"), P(None, "sec"), P(None, "sec"))
    out_specs = (P("vel", "sec"), P(None, "sec"))
    return jax.shard_map(body, mesh=mesh, in_specs=in_specs, out_specs=out_specs, check_vma=False)
```

```python
import math

import jax
import jax.numpy as jnp
import numpy as np
from jax import lax
from jax.sharding import PartitionSpec as P

NXI = 24
TUBES = 128
JACOBI = 4
NEWTON = 2


HIGH = lax.Precision.HIGHEST
pseudo_rate = 1.0


def passed_along(block, axis, distance):
    devices = range(lax.axis_size(axis))
    route = [(i - distance, i) for i in devices if i - distance in devices]
    return lax.ppermute(block, axis, route)


def extended(array, sides, width):
    for axis, dim in sides:
        count, length = (lax.axis_size(axis), array.shape[dim])
        up = [(i, (i + 1) % count) for i in range(count - 1)]
        down = [(j, i) for i, j in up]
        last = lax.slice_in_dim(array, length - width, length, axis=dim)
        first = lax.slice_in_dim(array, 0, width, axis=dim)
        before = lax.ppermute(last, axis, up)
        after = lax.ppermute(first, axis, down)
        array = jnp.concatenate([before, array, after], axis=dim)
    return array


def hermite_rule(count):
    quarter = math.pi ** (-0.25)
    found = []
    last_slope = 1.0
    for index in range(count // 2):
        if index == 0:
            guess = math.sqrt(2.0 * count + 1.0) - 1.85575 * (2.0 * count + 1.0) ** (-0.16667)
        elif index == 1:
            guess = guess - 1.14 * count**0.426 / guess
        elif index == 2:
            guess = 1.86 * guess - 0.86 * found[0][0]
        elif index == 3:
            guess = 1.91 * guess - 0.91 * found[1][0]
        else:
            guess = 2.0 * guess - found[index - 2][0]
        for repeat in range(60):
            current = quarter
            previous = 0.0
            for order in range(count):
                older = previous
                previous = current
                current = (
                    guess * math.sqrt(2.0 / (order + 1)) * previous
                    - math.sqrt(order / (order + 1.0)) * older
                )
            last_slope = math.sqrt(2.0 * count) * previous
            guess = guess - current / last_slope
        found.append((guess, 2.0 / (last_slope * last_slope)))
    positive = found[::-1]
    points = [-pair[0] for pair in found] + [pair[0] for pair in positive]
    weights = [pair[1] for pair in found] + [pair[1] for pair in positive]
    return (np.array(points), np.array(weights))


def node_tables(axis_points):
    points, weights = hermite_rule(axis_points)
    node_index = np.arange(axis_points**3)
    idx_x = node_index % axis_points
    idx_z = node_index // axis_points % axis_points
    idx_y = node_index // (axis_points * axis_points)
    along_x = points[idx_x]
    along_y = points[idx_y]
    along_z = points[idx_z]
    node_weight = weights[idx_x] * weights[idx_y] * weights[idx_z] / math.pi**1.5
    energy = along_x**2 + along_y**2 + along_z**2 - 1.5
    moment_basis = np.stack([along_x * 0.0 + 1.0, along_x, along_y, along_z, energy])
    norm_scale = np.array([1.0, 0.5, 0.5, 0.5, 1.5])
    return (
        along_x,
        node_weight,
        moment_basis * node_weight[None, :],
        moment_basis / norm_scale[:, None],
    )


def apply_block(matrices, vector):
    shaped = matrices.reshape((5, 5) + vector.shape[1:])
    return jnp.sum(shaped * vector[None], axis=1)


def affine_combine(earlier_map, later_map):
    return (later_map[0] * earlier_map[0], later_map[0] * earlier_map[1] + later_map[1])


def newton_sums(loaded, signed, shift_mass, shift_flow):
    growth = jnp.exp(shift_mass + shift_flow * signed)
    scaled = loaded * growth
    excess = loaded * (growth - 1.0)
    return jnp.stack(
        [
            jnp.sum(scaled),
            jnp.sum(scaled * signed),
            jnp.sum(scaled * signed * signed),
            jnp.sum(excess),
            jnp.sum(excess * signed),
        ]
    )


def newton_update(shift_mass, shift_flow, sums, goal_mass, goal_flow):
    resid_mass = sums[3] - goal_mass
    resid_flow = sums[4] - goal_flow
    determinant = sums[0] * sums[2] - sums[1] * sums[1]
    new_mass = shift_mass - (sums[2] * resid_mass - sums[1] * resid_flow) / determinant
    new_flow = shift_flow - (sums[0] * resid_flow - sums[1] * resid_mass) / determinant
    return (new_mass, new_flow)


def received(block, distance):
    count = lax.axis_size("sec")
    if abs(distance) >= count:
        return jnp.zeros_like(block)
    return passed_along(block, "sec", distance)


def fetched(state, distance, sign):
    rate, drive = state
    got = received(jnp.concatenate([rate, drive], axis=0), sign * distance)
    return got[:1], got[1:]


def scan_first(rate, drive, sign):
    near_a, near_b = fetched((rate, drive), 1, sign)
    if lax.axis_size("sec") <= 2:
        return (near_a, near_b), 1
    far_a, far_b = fetched((rate, drive), 2, sign)
    return (near_a * far_a, near_a * far_b + near_b), 2


def scan_next(state, span, sign):
    got_a, got_b = fetched(state, span, sign)
    return (state[0] * got_a, state[0] * got_b + state[1]), span * 2


def exclusive_inflow(rate, drive, sign):
    state, span = scan_first(rate, drive, sign)
    while span < lax.axis_size("sec") - 1:
        state, span = scan_next(state, span, sign)
    return state[1]


def with_halo(array, width):
    parts = [received(array, d) for d in range(width, 0, -1)]
    parts.append(array)
    parts.extend(received(array, -d) for d in range(1, width + 1))
    return jnp.concatenate(parts, axis=1)


def tree_sum(block, axes):
    for axis in axes:
        count = lax.axis_size(axis)
        if count & (count - 1):
            block = lax.psum(block, axis)
            continue
        bit = 1
        while bit < count:
            block = block + lax.ppermute(block, axis, [(i, i ^ bit) for i in range(count)])
            bit *= 2
    return block


def local_sweep(carry_rate, drive):
    half_nodes = NXI // 2
    shape = (1, half_nodes) + drive.shape[2:]
    prod_neg, local_neg = lax.associative_scan(
        affine_combine,
        (jnp.broadcast_to(carry_rate[:, :half_nodes], shape), drive[:, :half_nodes]),
        reverse=True,
        axis=2,
    )
    prod_pos, local_pos = lax.associative_scan(
        affine_combine,
        (jnp.broadcast_to(carry_rate[:, half_nodes:], shape), drive[:, half_nodes:]),
        axis=2,
    )
    return prod_neg, local_neg, prod_pos, local_pos


def joined_field(sweep, inflow_neg, inflow_pos):
    prod_neg, local_neg, prod_pos, local_pos = sweep
    field_neg = local_neg + prod_neg * inflow_neg[:, :, None, :]
    field_pos = local_pos + prod_pos * inflow_pos[:, :, None, :]
    return jnp.concatenate([field_neg, field_pos], axis=1)


def swept_field(carry_rate, drive):
    sweep = local_sweep(carry_rate, drive)
    inflow_pos = exclusive_inflow(sweep[2][:, :, -1], sweep[3][:, :, -1], 1)
    inflow_neg = exclusive_inflow(sweep[0][:, :, 0], sweep[1][:, :, 0], -1)
    return joined_field(sweep, inflow_neg, inflow_pos)


def caught_up_side(own, own_span, rate, drive, count, sign):
    reach = min(2 * own_span, count - 1)
    own_rows = own[1].shape[0]
    moment_rows = drive.shape[0]
    fetched_maps = {}
    for distance in range(1, reach + 1):
        if distance == own_span and own_span < count - 1:
            packed = jnp.concatenate([own[0], own[1], rate, drive], axis=0)
            got = received(packed, sign * distance)
            got_own = (got[:1], got[1 : 1 + own_rows])
            fetched_maps[distance] = (got[1 + own_rows : 2 + own_rows], got[2 + own_rows :])
        else:
            got = received(jnp.concatenate([rate, drive], axis=0), sign * distance)
            fetched_maps[distance] = (got[:1], got[1:])
    if own_span < count - 1:
        own = (own[0] * got_own[0], own[0] * got_own[1] + own[1])
    acc_a, acc_b = fetched_maps[reach]
    for distance in range(reach - 1, 0, -1):
        near_a, near_b = fetched_maps[distance]
        acc_a, acc_b = near_a * acc_a, near_a * acc_b + near_b
    return own, (acc_a, acc_b)


def caught_up(own_pos, own_neg, own_span, moment_sweep, count):
    own_pos, moment_pos = caught_up_side(
        own_pos, own_span, moment_sweep[2][:, :, -1], moment_sweep[3][:, :, -1], count, 1
    )
    own_neg, moment_neg = caught_up_side(
        own_neg, own_span, moment_sweep[0][:, :, 0], moment_sweep[1][:, :, 0], count, -1
    )
    return lax.optimization_barrier((own_pos, own_neg, moment_pos, moment_neg))


def joint_next(own, moment, span, sign):
    own_rows = own[1].shape[0]
    packed = jnp.concatenate([own[0], own[1], moment[1]], axis=0)
    got = received(packed, sign * span)
    got_a, got_own, got_moment = got[:1], got[1 : 1 + own_rows], got[1 + own_rows :]
    return (
        (own[0] * got_a, own[0] * got_own + own[1]),
        (own[0] * got_a, own[0] * got_moment + moment[1]),
    )


def body(distribution, collision, lower_blocks, upper_blocks, diag_inverse):
    node_count = distribution.shape[0]
    cell_count = distribution.shape[1]
    length = cell_count // TUBES
    node_rows = node_count // NXI
    half_nodes = NXI // 2
    along_x, node_weight, weighted_np, rebuild_np = node_tables(NXI)
    all_mass = jnp.asarray(node_weight, jnp.float32)
    offset = lax.axis_index("vel") * node_count
    weighted = lax.dynamic_slice_in_dim(
        jnp.asarray(weighted_np, jnp.float32), offset, node_count, 1
    )
    rebuild = lax.dynamic_slice_in_dim(jnp.asarray(rebuild_np, jnp.float32), offset, node_count, 1)
    node_mass = lax.dynamic_slice_in_dim(all_mass, offset, node_count, 0)
    line_signed = jnp.asarray(along_x[:NXI], jnp.float32)
    total_length = length * lax.axis_size("sec")
    thickness = collision.reshape(1, 1, length, TUBES)
    node_speed = jnp.abs(line_signed).reshape(1, NXI, 1, 1)
    denominator = node_speed * total_length + thickness + pseudo_rate
    carry_rate = node_speed * total_length / denominator
    own_drive = pseudo_rate * distribution.reshape(node_rows, NXI, length, TUBES) / denominator
    count = lax.axis_size("sec")
    own_sweep = local_sweep(carry_rate, own_drive)
    own_pos, own_span = scan_first(own_sweep[2][:, :, -1], own_sweep[3][:, :, -1], 1)
    own_neg, _ = scan_first(own_sweep[0][:, :, 0], own_sweep[1][:, :, 0], -1)
    old_moments = tree_sum(jnp.dot(weighted, distribution, precision=HIGH), ("vel",))
    own_pos, own_neg, old_moments = lax.optimization_barrier((own_pos, own_neg, old_moments))
    moment_drive = thickness * old_moments.reshape(5, 1, length, TUBES) / denominator
    moment_sweep = local_sweep(carry_rate, moment_drive)
    own_pos, own_neg, moment_pos, moment_neg = caught_up(
        own_pos, own_neg, own_span, moment_sweep, count
    )
    span = min(2 * own_span, count)
    while span < count - 1:
        own_pos, moment_pos = joint_next(own_pos, moment_pos, span, 1)
        own_neg, moment_neg = joint_next(own_neg, moment_neg, span, -1)
        span *= 2
        own_pos, own_neg, moment_pos, moment_neg = lax.optimization_barrier(
            (own_pos, own_neg, moment_pos, moment_neg)
        )
    own_field = joined_field(own_sweep, own_neg[1], own_pos[1])
    moment_field = joined_field(moment_sweep, moment_neg[1], moment_pos[1])
    basis = rebuild.reshape(5, node_rows, NXI, 1, 1)
    half_field = own_field + jnp.sum(basis * moment_field[:, None], axis=0)
    half_field = half_field.reshape(node_count, cell_count)
    half_moments = tree_sum(jnp.dot(weighted, half_field, precision=HIGH), ("vel",))
    residual = (half_moments - old_moments).reshape(5, length, TUBES)
    width = min(-(-JACOBI // length), lax.axis_size("sec") - 1)
    blocks = jnp.concatenate([lower_blocks, upper_blocks, diag_inverse], axis=0)
    wide = with_halo(
        jnp.concatenate([blocks.reshape(75, length, TUBES), residual], axis=0), width
    )
    lower_r = wide[:25]
    upper_r = wide[25:50]
    inverse_r = wide[50:75]
    residual_wide = wide[75:]
    correction = apply_block(inverse_r, residual_wide)
    edge_zero = jnp.zeros((5, 1, TUBES), jnp.float32)
    for sweep_index in range(JACOBI):
        from_left = jnp.concatenate([edge_zero, correction[:, :-1]], axis=1)
        from_right = jnp.concatenate([correction[:, 1:], edge_zero], axis=1)
        correction = apply_block(
            inverse_r,
            residual_wide - apply_block(lower_r, from_left) - apply_block(upper_r, from_right),
        )
    correction = correction[:, width * length : (width + 1) * length].reshape(5, cell_count)
    macro = half_moments + correction
    synthetic = half_field + jnp.dot(rebuild.T, correction, precision=HIGH)
    local_totals = jnp.sum(old_moments - macro, axis=1)[0:2]
    magnitude = jnp.sum(jnp.abs(synthetic), axis=1)
    line_loaded = jnp.sum((node_mass * magnitude).reshape(node_rows, NXI), axis=0)
    first_copy = (lax.axis_index("vel") == 0).astype(jnp.float32)
    gathered = tree_sum(
        jnp.concatenate([line_loaded, local_totals * first_copy]), ("vel", "sec")
    )
    loaded = gathered[:NXI]
    goal_mass = jnp.broadcast_to(gathered[NXI], (NXI,))
    goal_flow = jnp.broadcast_to(gathered[NXI + 1], (NXI,))
    spread = jnp.ones((NXI, NXI), jnp.float32)
    shift_mass = jnp.zeros((NXI,), jnp.float32)
    shift_flow = jnp.zeros((NXI,), jnp.float32)
    for newton_turn in range(NEWTON):
        growth = jnp.exp(shift_mass + shift_flow * line_signed)
        scaled = loaded * growth
        excess = loaded * (growth - 1.0)
        terms = jnp.stack(
            [scaled, scaled * line_signed, scaled * line_signed * line_signed, excess, excess * line_signed]
        )
        sums = jnp.dot(terms, spread, precision=HIGH)
        shift_mass, shift_flow = newton_update(shift_mass, shift_flow, sums, goal_mass, goal_flow)
    growth = jnp.exp(shift_mass + shift_flow * line_signed)
    synthetic_rows = synthetic.reshape(node_rows, NXI, cell_count)
    new_distribution = synthetic_rows + jnp.abs(synthetic_rows) * (growth[None, :, None] - 1.0)
    return (new_distribution.reshape(node_count, cell_count), macro)


def solution(mesh):
    in_specs = (P("vel", "sec"), P("sec"), P(None, "sec"), P(None, "sec"), P(None, "sec"))
    out_specs = (P("vel", "sec"), P(None, "sec"))
    return jax.shard_map(body, mesh=mesh, in_specs=in_specs, out_specs=out_specs, check_vma=False)
```

```python
import math

import jax
import jax.numpy as jnp
import numpy as np
from jax import lax
from jax.sharding import PartitionSpec as P

NXI = 24
TUBES = 128
JACOBI = 4
NEWTON = 2


HIGH = lax.Precision.HIGHEST
pseudo_rate = 1.0


def passed_along(block, axis, distance):
    devices = range(lax.axis_size(axis))
    route = [(i - distance, i) for i in devices if i - distance in devices]
    return lax.ppermute(block, axis, route)


def extended(array, sides, width):
    for axis, dim in sides:
        count, length = (lax.axis_size(axis), array.shape[dim])
        up = [(i, (i + 1) % count) for i in range(count - 1)]
        down = [(j, i) for i, j in up]
        last = lax.slice_in_dim(array, length - width, length, axis=dim)
        first = lax.slice_in_dim(array, 0, width, axis=dim)
        before = lax.ppermute(last, axis, up)
        after = lax.ppermute(first, axis, down)
        array = jnp.concatenate([before, array, after], axis=dim)
    return array


def hermite_rule(count):
    quarter = math.pi ** (-0.25)
    found = []
    last_slope = 1.0
    for index in range(count // 2):
        if index == 0:
            guess = math.sqrt(2.0 * count + 1.0) - 1.85575 * (2.0 * count + 1.0) ** (-0.16667)
        elif index == 1:
            guess = guess - 1.14 * count**0.426 / guess
        elif index == 2:
            guess = 1.86 * guess - 0.86 * found[0][0]
        elif index == 3:
            guess = 1.91 * guess - 0.91 * found[1][0]
        else:
            guess = 2.0 * guess - found[index - 2][0]
        for repeat in range(60):
            current = quarter
            previous = 0.0
            for order in range(count):
                older = previous
                previous = current
                current = (
                    guess * math.sqrt(2.0 / (order + 1)) * previous
                    - math.sqrt(order / (order + 1.0)) * older
                )
            last_slope = math.sqrt(2.0 * count) * previous
            guess = guess - current / last_slope
        found.append((guess, 2.0 / (last_slope * last_slope)))
    positive = found[::-1]
    points = [-pair[0] for pair in found] + [pair[0] for pair in positive]
    weights = [pair[1] for pair in found] + [pair[1] for pair in positive]
    return (np.array(points), np.array(weights))


def node_tables(axis_points):
    points, weights = hermite_rule(axis_points)
    node_index = np.arange(axis_points**3)
    idx_x = node_index % axis_points
    idx_z = node_index // axis_points % axis_points
    idx_y = node_index // (axis_points * axis_points)
    along_x = points[idx_x]
    along_y = points[idx_y]
    along_z = points[idx_z]
    node_weight = weights[idx_x] * weights[idx_y] * weights[idx_z] / math.pi**1.5
    energy = along_x**2 + along_y**2 + along_z**2 - 1.5
    moment_basis = np.stack([along_x * 0.0 + 1.0, along_x, along_y, along_z, energy])
    norm_scale = np.array([1.0, 0.5, 0.5, 0.5, 1.5])
    return (
        along_x,
        node_weight,
        moment_basis * node_weight[None, :],
        moment_basis / norm_scale[:, None],
    )


def apply_block(matrices, vector):
    shaped = matrices.reshape((5, 5) + vector.shape[1:])
    return jnp.sum(shaped * vector[None], axis=1)


def affine_combine(earlier_map, later_map):
    return (later_map[0] * earlier_map[0], later_map[0] * earlier_map[1] + later_map[1])


def newton_sums(loaded, signed, shift_mass, shift_flow):
    growth = jnp.exp(shift_mass + shift_flow * signed)
    scaled = loaded * growth
    excess = loaded * (growth - 1.0)
    return jnp.stack(
        [
            jnp.sum(scaled),
            jnp.sum(scaled * signed),
            jnp.sum(scaled * signed * signed),
            jnp.sum(excess),
            jnp.sum(excess * signed),
        ]
    )


def newton_update(shift_mass, shift_flow, sums, goal_mass, goal_flow):
    resid_mass = sums[3] - goal_mass
    resid_flow = sums[4] - goal_flow
    determinant = sums[0] * sums[2] - sums[1] * sums[1]
    new_mass = shift_mass - (sums[2] * resid_mass - sums[1] * resid_flow) / determinant
    new_flow = shift_flow - (sums[0] * resid_flow - sums[1] * resid_mass) / determinant
    return (new_mass, new_flow)


def received(block, distance):
    count = lax.axis_size("sec")
    if abs(distance) >= count:
        return jnp.zeros_like(block)
    return passed_along(block, "sec", distance)


def fetched(state, distance, sign):
    rate, drive = state
    got = received(jnp.concatenate([rate, drive], axis=0), sign * distance)
    return got[:1], got[1:]


def scan_first(rate, drive, sign):
    near_a, near_b = fetched((rate, drive), 1, sign)
    if lax.axis_size("sec") <= 2:
        return (near_a, near_b), 1
    far_a, far_b = fetched((rate, drive), 2, sign)
    return (near_a * far_a, near_a * far_b + near_b), 2


def scan_next(state, span, sign):
    got_a, got_b = fetched(state, span, sign)
    return (state[0] * got_a, state[0] * got_b + state[1]), span * 2


def exclusive_inflow(rate, drive, sign):
    state, span = scan_first(rate, drive, sign)
    while span < lax.axis_size("sec") - 1:
        state, span = scan_next(state, span, sign)
    return state[1]


def with_halo(array, width):
    parts = [received(array, d) for d in range(width, 0, -1)]
    parts.append(array)
    parts.extend(received(array, -d) for d in range(1, width + 1))
    return jnp.concatenate(parts, axis=1)


def tree_sum(block, axes):
    for axis in axes:
        count = lax.axis_size(axis)
        if count & (count - 1):
            block = lax.psum(block, axis)
            continue
        bit = 1
        while bit < count:
            block = block + lax.ppermute(block, axis, [(i, i ^ bit) for i in range(count)])
            bit *= 2
    return block


def local_sweep(carry_rate, drive):
    half_nodes = NXI // 2
    shape = (1, half_nodes) + drive.shape[2:]
    prod_neg, local_neg = lax.associative_scan(
        affine_combine,
        (jnp.broadcast_to(carry_rate[:, :half_nodes], shape), drive[:, :half_nodes]),
        reverse=True,
        axis=2,
    )
    prod_pos, local_pos = lax.associative_scan(
        affine_combine,
        (jnp.broadcast_to(carry_rate[:, half_nodes:], shape), drive[:, half_nodes:]),
        axis=2,
    )
    return prod_neg, local_neg, prod_pos, local_pos


def joined_field(sweep, inflow_neg, inflow_pos):
    prod_neg, local_neg, prod_pos, local_pos = sweep
    field_neg = local_neg + prod_neg * inflow_neg[:, :, None, :]
    field_pos = local_pos + prod_pos * inflow_pos[:, :, None, :]
    return jnp.concatenate([field_neg, field_pos], axis=1)


def swept_field(carry_rate, drive):
    sweep = local_sweep(carry_rate, drive)
    inflow_pos = exclusive_inflow(sweep[2][:, :, -1], sweep[3][:, :, -1], 1)
    inflow_neg = exclusive_inflow(sweep[0][:, :, 0], sweep[1][:, :, 0], -1)
    return joined_field(sweep, inflow_neg, inflow_pos)


def caught_up_side(own, own_span, rate, drive, count, sign):
    reach = min(2 * own_span, count - 1)
    own_rows = own[1].shape[0]
    moment_rows = drive.shape[0]
    fetched_maps = {}
    for distance in range(1, reach + 1):
        if distance == own_span and own_span < count - 1:
            packed = jnp.concatenate([own[0], own[1], rate, drive], axis=0)
            got = received(packed, sign * distance)
            got_own = (got[:1], got[1 : 1 + own_rows])
            fetched_maps[distance] = (got[1 + own_rows : 2 + own_rows], got[2 + own_rows :])
        else:
            got = received(jnp.concatenate([rate, drive], axis=0), sign * distance)
            fetched_maps[distance] = (got[:1], got[1:])
    if own_span < count - 1:
        own = (own[0] * got_own[0], own[0] * got_own[1] + own[1])
    acc_a, acc_b = fetched_maps[reach]
    for distance in range(reach - 1, 0, -1):
        near_a, near_b = fetched_maps[distance]
        acc_a, acc_b = near_a * acc_a, near_a * acc_b + near_b
    return own, (acc_a, acc_b)


def caught_up(own_pos, own_neg, own_span, moment_sweep, count):
    own_pos, moment_pos = caught_up_side(
        own_pos, own_span, moment_sweep[2][:, :, -1], moment_sweep[3][:, :, -1], count, 1
    )
    own_neg, moment_neg = caught_up_side(
        own_neg, own_span, moment_sweep[0][:, :, 0], moment_sweep[1][:, :, 0], count, -1
    )
    return lax.optimization_barrier((own_pos, own_neg, moment_pos, moment_neg))


def joint_next(own, moment, span, sign):
    own_rows = own[1].shape[0]
    packed = jnp.concatenate([own[0], own[1], moment[1]], axis=0)
    got = received(packed, sign * span)
    got_a, got_own, got_moment = got[:1], got[1 : 1 + own_rows], got[1 + own_rows :]
    return (
        (own[0] * got_a, own[0] * got_own + own[1]),
        (own[0] * got_a, own[0] * got_moment + moment[1]),
    )


def paired_inflow(pos, neg):
    count = lax.axis_size("sec")
    pos, span = scan_first(pos[0], pos[1], 1)
    neg, _ = scan_first(neg[0], neg[1], -1)
    pos, neg = lax.optimization_barrier((pos, neg))
    while span < count - 1:
        pos, next_span = scan_next(pos, span, 1)
        neg, _ = scan_next(neg, span, -1)
        span = next_span
        pos, neg = lax.optimization_barrier((pos, neg))
    return pos[1], neg[1]


def body(distribution, collision, lower_blocks, upper_blocks, diag_inverse):
    node_count = distribution.shape[0]
    cell_count = distribution.shape[1]
    length = cell_count // TUBES
    node_rows = node_count // NXI
    half_nodes = NXI // 2
    along_x, node_weight, weighted_np, rebuild_np = node_tables(NXI)
    all_mass = jnp.asarray(node_weight, jnp.float32)
    offset = lax.axis_index("vel") * node_count
    weighted = lax.dynamic_slice_in_dim(
        jnp.asarray(weighted_np, jnp.float32), offset, node_count, 1
    )
    rebuild = lax.dynamic_slice_in_dim(jnp.asarray(rebuild_np, jnp.float32), offset, node_count, 1)
    node_mass = lax.dynamic_slice_in_dim(all_mass, offset, node_count, 0)
    line_signed = jnp.asarray(along_x[:NXI], jnp.float32)
    total_length = length * lax.axis_size("sec")
    thickness = collision.reshape(1, 1, length, TUBES)
    node_speed = jnp.abs(line_signed).reshape(1, NXI, 1, 1)
    denominator = node_speed * total_length + thickness + pseudo_rate
    carry_rate = node_speed * total_length / denominator
    own_drive = pseudo_rate * distribution.reshape(node_rows, NXI, length, TUBES) / denominator
    own_sweep = local_sweep(carry_rate, own_drive)
    old_part = jnp.dot(weighted, distribution, precision=HIGH)
    moment_drive = thickness * old_part.reshape(5, 1, length, TUBES) / denominator
    moment_sweep = local_sweep(carry_rate, moment_drive)
    own_rows = own_sweep[1].shape[0]
    inflow_pos, inflow_neg = paired_inflow(
        (own_sweep[2][:, :, -1],
         jnp.concatenate([own_sweep[3][:, :, -1], moment_sweep[3][:, :, -1]], axis=0)),
        (own_sweep[0][:, :, 0],
         jnp.concatenate([own_sweep[1][:, :, 0], moment_sweep[1][:, :, 0]], axis=0)),
    )
    own_field = joined_field(own_sweep, inflow_neg[:own_rows], inflow_pos[:own_rows])
    moment_part = joined_field(moment_sweep, inflow_neg[own_rows:], inflow_pos[own_rows:])
    coupling = jnp.asarray(np.einsum(
        "irx,jrx->ijx",
        weighted_np.reshape(5, -1, NXI),
        rebuild_np.reshape(5, -1, NXI),
    ), jnp.float32)
    half_part = jnp.dot(
        weighted, own_field.reshape(node_count, cell_count), precision=HIGH
    ) + jnp.tensordot(coupling, moment_part, axes=([1, 2], [0, 1]), precision=HIGH).reshape(
        5, cell_count
    )
    summed = tree_sum(
        jnp.concatenate([half_part, old_part, moment_part.reshape(5 * NXI, cell_count)], axis=0),
        ("vel",),
    )
    half_moments = summed[:5]
    old_moments = summed[5:10]
    moment_field = summed[10:].reshape(5, NXI, length, TUBES)
    basis = rebuild.reshape(5, node_rows, NXI, 1, 1)
    half_field = own_field + jnp.sum(basis * moment_field[:, None], axis=0)
    half_field = half_field.reshape(node_count, cell_count)
    residual = (half_moments - old_moments).reshape(5, length, TUBES)
    width = min(-(-JACOBI // length), lax.axis_size("sec") - 1)
    blocks = jnp.concatenate([lower_blocks, upper_blocks, diag_inverse], axis=0)
    wide = with_halo(
        jnp.concatenate([blocks.reshape(75, length, TUBES), residual], axis=0), width
    )
    lower_r = wide[:25]
    upper_r = wide[25:50]
    inverse_r = wide[50:75]
    residual_wide = wide[75:]
    correction = apply_block(inverse_r, residual_wide)
    edge_zero = jnp.zeros((5, 1, TUBES), jnp.float32)
    for sweep_index in range(JACOBI):
        from_left = jnp.concatenate([edge_zero, correction[:, :-1]], axis=1)
        from_right = jnp.concatenate([correction[:, 1:], edge_zero], axis=1)
        correction = apply_block(
            inverse_r,
            residual_wide - apply_block(lower_r, from_left) - apply_block(upper_r, from_right),
        )
    correction = correction[:, width * length : (width + 1) * length].reshape(5, cell_count)
    macro = half_moments + correction
    synthetic = half_field + jnp.dot(rebuild.T, correction, precision=HIGH)
    local_totals = jnp.sum(old_moments - macro, axis=1)[0:2]
    magnitude = jnp.sum(jnp.abs(synthetic), axis=1)
    line_loaded = jnp.sum((node_mass * magnitude).reshape(node_rows, NXI), axis=0)
    first_copy = (lax.axis_index("vel") == 0).astype(jnp.float32)
    gathered = tree_sum(
        jnp.concatenate([line_loaded, local_totals * first_copy]), ("vel", "sec")
    )
    loaded = gathered[:NXI]
    goal_mass = jnp.broadcast_to(gathered[NXI], (NXI,))
    goal_flow = jnp.broadcast_to(gathered[NXI + 1], (NXI,))
    spread = jnp.ones((NXI, NXI), jnp.float32)
    shift_mass = jnp.zeros((NXI,), jnp.float32)
    shift_flow = jnp.zeros((NXI,), jnp.float32)
    for newton_turn in range(NEWTON):
        growth = jnp.exp(shift_mass + shift_flow * line_signed)
        scaled = loaded * growth
        excess = loaded * (growth - 1.0)
        terms = jnp.stack(
            [scaled, scaled * line_signed, scaled * line_signed * line_signed, excess, excess * line_signed]
        )
        sums = jnp.dot(terms, spread, precision=HIGH)
        shift_mass, shift_flow = newton_update(shift_mass, shift_flow, sums, goal_mass, goal_flow)
    growth = jnp.exp(shift_mass + shift_flow * line_signed)
    synthetic_rows = synthetic.reshape(node_rows, NXI, cell_count)
    new_distribution = synthetic_rows + jnp.abs(synthetic_rows) * (growth[None, :, None] - 1.0)
    return (new_distribution.reshape(node_count, cell_count), macro)


def solution(mesh):
    in_specs = (P("vel", "sec"), P("sec"), P(None, "sec"), P(None, "sec"), P(None, "sec"))
    out_specs = (P("vel", "sec"), P(None, "sec"))
    return jax.shard_map(body, mesh=mesh, in_specs=in_specs, out_specs=out_specs, check_vma=False)
```

```python
import math

import jax
import jax.numpy as jnp
import numpy as np
from jax import lax
from jax.sharding import PartitionSpec as P

NXI = 24
TUBES = 128
JACOBI = 4
NEWTON = 2


HIGH = lax.Precision.HIGHEST
pseudo_rate = 1.0


def passed_along(block, axis, distance):
    devices = range(lax.axis_size(axis))
    route = [(i - distance, i) for i in devices if i - distance in devices]
    return lax.ppermute(block, axis, route)


def extended(array, sides, width):
    for axis, dim in sides:
        count, length = (lax.axis_size(axis), array.shape[dim])
        up = [(i, (i + 1) % count) for i in range(count - 1)]
        down = [(j, i) for i, j in up]
        last = lax.slice_in_dim(array, length - width, length, axis=dim)
        first = lax.slice_in_dim(array, 0, width, axis=dim)
        before = lax.ppermute(last, axis, up)
        after = lax.ppermute(first, axis, down)
        array = jnp.concatenate([before, array, after], axis=dim)
    return array


def hermite_rule(count):
    quarter = math.pi ** (-0.25)
    found = []
    last_slope = 1.0
    for index in range(count // 2):
        if index == 0:
            guess = math.sqrt(2.0 * count + 1.0) - 1.85575 * (2.0 * count + 1.0) ** (-0.16667)
        elif index == 1:
            guess = guess - 1.14 * count**0.426 / guess
        elif index == 2:
            guess = 1.86 * guess - 0.86 * found[0][0]
        elif index == 3:
            guess = 1.91 * guess - 0.91 * found[1][0]
        else:
            guess = 2.0 * guess - found[index - 2][0]
        for repeat in range(60):
            current = quarter
            previous = 0.0
            for order in range(count):
                older = previous
                previous = current
                current = (
                    guess * math.sqrt(2.0 / (order + 1)) * previous
                    - math.sqrt(order / (order + 1.0)) * older
                )
            last_slope = math.sqrt(2.0 * count) * previous
            guess = guess - current / last_slope
        found.append((guess, 2.0 / (last_slope * last_slope)))
    positive = found[::-1]
    points = [-pair[0] for pair in found] + [pair[0] for pair in positive]
    weights = [pair[1] for pair in found] + [pair[1] for pair in positive]
    return (np.array(points), np.array(weights))


def node_tables(axis_points):
    points, weights = hermite_rule(axis_points)
    node_index = np.arange(axis_points**3)
    idx_x = node_index % axis_points
    idx_z = node_index // axis_points % axis_points
    idx_y = node_index // (axis_points * axis_points)
    along_x = points[idx_x]
    along_y = points[idx_y]
    along_z = points[idx_z]
    node_weight = weights[idx_x] * weights[idx_y] * weights[idx_z] / math.pi**1.5
    energy = along_x**2 + along_y**2 + along_z**2 - 1.5
    moment_basis = np.stack([along_x * 0.0 + 1.0, along_x, along_y, along_z, energy])
    norm_scale = np.array([1.0, 0.5, 0.5, 0.5, 1.5])
    return (
        along_x,
        node_weight,
        moment_basis * node_weight[None, :],
        moment_basis / norm_scale[:, None],
    )


def apply_block(matrices, vector):
    shaped = matrices.reshape((5, 5) + vector.shape[1:])
    return jnp.sum(shaped * vector[None], axis=1)


def affine_combine(earlier_map, later_map):
    return (later_map[0] * earlier_map[0], later_map[0] * earlier_map[1] + later_map[1])


def newton_sums(loaded, signed, shift_mass, shift_flow):
    growth = jnp.exp(shift_mass + shift_flow * signed)
    scaled = loaded * growth
    excess = loaded * (growth - 1.0)
    return jnp.stack(
        [
            jnp.sum(scaled),
            jnp.sum(scaled * signed),
            jnp.sum(scaled * signed * signed),
            jnp.sum(excess),
            jnp.sum(excess * signed),
        ]
    )


def newton_update(shift_mass, shift_flow, sums, goal_mass, goal_flow):
    resid_mass = sums[3] - goal_mass
    resid_flow = sums[4] - goal_flow
    determinant = sums[0] * sums[2] - sums[1] * sums[1]
    new_mass = shift_mass - (sums[2] * resid_mass - sums[1] * resid_flow) / determinant
    new_flow = shift_flow - (sums[0] * resid_flow - sums[1] * resid_mass) / determinant
    return (new_mass, new_flow)


def received(block, distance):
    count = lax.axis_size("sec")
    if abs(distance) >= count:
        return jnp.zeros_like(block)
    return passed_along(block, "sec", distance)


def fetched(state, distance, sign):
    rate, drive = state
    got = received(jnp.concatenate([rate, drive], axis=0), sign * distance)
    return got[:1], got[1:]


def scan_first(rate, drive, sign):
    near_a, near_b = fetched((rate, drive), 1, sign)
    if lax.axis_size("sec") <= 2:
        return (near_a, near_b), 1
    far_a, far_b = fetched((rate, drive), 2, sign)
    return (near_a * far_a, near_a * far_b + near_b), 2


def scan_next(state, span, sign):
    got_a, got_b = fetched(state, span, sign)
    return (state[0] * got_a, state[0] * got_b + state[1]), span * 2


def exclusive_inflow(rate, drive, sign):
    state, span = scan_first(rate, drive, sign)
    while span < lax.axis_size("sec") - 1:
        state, span = scan_next(state, span, sign)
    return state[1]


def with_halo(array, width):
    parts = [received(array, d) for d in range(width, 0, -1)]
    parts.append(array)
    parts.extend(received(array, -d) for d in range(1, width + 1))
    return jnp.concatenate(parts, axis=1)


def group_sum(block, axis, low_bit, members):
    count = lax.axis_size(axis)
    if members == 2:
        pairs = [(i, i ^ (1 << low_bit)) for i in range(count)]
        return block + lax.ppermute(block, axis, pairs)
    mine = (lax.axis_index(axis) >> low_bit) % members
    shifted = [block]
    for step in range(1, members):
        pairs = []
        for i in range(count):
            place = (i >> low_bit) % members
            base = i - (place << low_bit)
            pairs.append((base + (((place + step) % members) << low_bit), i))
        shifted.append(lax.ppermute(block, axis, pairs))
    stacked = jnp.stack(shifted)
    total = None
    for member in range(members):
        value = lax.dynamic_index_in_dim(stacked, (member - mine) % members, 0, keepdims=False)
        total = value if total is None else total + value
    return total


def sum_plan(axis, count):
    bits = count.bit_length() - 1
    plan = []
    bit = 0
    if axis == "vel" and bits % 2 == 1:
        plan.append((0, 2))
        bit = 1
    elif axis == "vel" and bits >= 2:
        plan.append((0, 2))
        bit = 1
    while bit + 1 < bits:
        plan.append((bit, 4))
        bit += 2
    if bit < bits:
        plan.append((bit, 2))
    return plan


def tree_sum(block, axes):
    for axis in axes:
        count = lax.axis_size(axis)
        if count & (count - 1):
            block = lax.psum(block, axis)
            continue
        for low_bit, members in sum_plan(axis, count):
            block = group_sum(block, axis, low_bit, members)
    return block


def local_sweep(carry_rate, drive):
    half_nodes = NXI // 2
    shape = (1, half_nodes) + drive.shape[2:]
    prod_neg, local_neg = lax.associative_scan(
        affine_combine,
        (jnp.broadcast_to(carry_rate[:, :half_nodes], shape), drive[:, :half_nodes]),
        reverse=True,
        axis=2,
    )
    prod_pos, local_pos = lax.associative_scan(
        affine_combine,
        (jnp.broadcast_to(carry_rate[:, half_nodes:], shape), drive[:, half_nodes:]),
        axis=2,
    )
    return prod_neg, local_neg, prod_pos, local_pos


def joined_field(sweep, inflow_neg, inflow_pos):
    prod_neg, local_neg, prod_pos, local_pos = sweep
    field_neg = local_neg + prod_neg * inflow_neg[:, :, None, :]
    field_pos = local_pos + prod_pos * inflow_pos[:, :, None, :]
    return jnp.concatenate([field_neg, field_pos], axis=1)


def swept_field(carry_rate, drive):
    sweep = local_sweep(carry_rate, drive)
    inflow_pos = exclusive_inflow(sweep[2][:, :, -1], sweep[3][:, :, -1], 1)
    inflow_neg = exclusive_inflow(sweep[0][:, :, 0], sweep[1][:, :, 0], -1)
    return joined_field(sweep, inflow_neg, inflow_pos)


def caught_up_side(own, own_span, rate, drive, count, sign):
    reach = min(2 * own_span, count - 1)
    own_rows = own[1].shape[0]
    moment_rows = drive.shape[0]
    fetched_maps = {}
    for distance in range(1, reach + 1):
        if distance == own_span and own_span < count - 1:
            packed = jnp.concatenate([own[0], own[1], rate, drive], axis=0)
            got = received(packed, sign * distance)
            got_own = (got[:1], got[1 : 1 + own_rows])
            fetched_maps[distance] = (got[1 + own_rows : 2 + own_rows], got[2 + own_rows :])
        else:
            got = received(jnp.concatenate([rate, drive], axis=0), sign * distance)
            fetched_maps[distance] = (got[:1], got[1:])
    if own_span < count - 1:
        own = (own[0] * got_own[0], own[0] * got_own[1] + own[1])
    acc_a, acc_b = fetched_maps[reach]
    for distance in range(reach - 1, 0, -1):
        near_a, near_b = fetched_maps[distance]
        acc_a, acc_b = near_a * acc_a, near_a * acc_b + near_b
    return own, (acc_a, acc_b)


def caught_up(own_pos, own_neg, own_span, moment_sweep, count):
    own_pos, moment_pos = caught_up_side(
        own_pos, own_span, moment_sweep[2][:, :, -1], moment_sweep[3][:, :, -1], count, 1
    )
    own_neg, moment_neg = caught_up_side(
        own_neg, own_span, moment_sweep[0][:, :, 0], moment_sweep[1][:, :, 0], count, -1
    )
    return lax.optimization_barrier((own_pos, own_neg, moment_pos, moment_neg))


def joint_next(own, moment, span, sign):
    own_rows = own[1].shape[0]
    packed = jnp.concatenate([own[0], own[1], moment[1]], axis=0)
    got = received(packed, sign * span)
    got_a, got_own, got_moment = got[:1], got[1 : 1 + own_rows], got[1 + own_rows :]
    return (
        (own[0] * got_a, own[0] * got_own + own[1]),
        (own[0] * got_a, own[0] * got_moment + moment[1]),
    )


def body(distribution, collision, lower_blocks, upper_blocks, diag_inverse):
    node_count = distribution.shape[0]
    cell_count = distribution.shape[1]
    length = cell_count // TUBES
    node_rows = node_count // NXI
    half_nodes = NXI // 2
    along_x, node_weight, weighted_np, rebuild_np = node_tables(NXI)
    all_mass = jnp.asarray(node_weight, jnp.float32)
    offset = lax.axis_index("vel") * node_count
    weighted = lax.dynamic_slice_in_dim(
        jnp.asarray(weighted_np, jnp.float32), offset, node_count, 1
    )
    rebuild = lax.dynamic_slice_in_dim(jnp.asarray(rebuild_np, jnp.float32), offset, node_count, 1)
    node_mass = lax.dynamic_slice_in_dim(all_mass, offset, node_count, 0)
    line_signed = jnp.asarray(along_x[:NXI], jnp.float32)
    total_length = length * lax.axis_size("sec")
    thickness = collision.reshape(1, 1, length, TUBES)
    node_speed = jnp.abs(line_signed).reshape(1, NXI, 1, 1)
    denominator = node_speed * total_length + thickness + pseudo_rate
    carry_rate = node_speed * total_length / denominator
    own_drive = pseudo_rate * distribution.reshape(node_rows, NXI, length, TUBES) / denominator
    count = lax.axis_size("sec")
    own_sweep = local_sweep(carry_rate, own_drive)
    own_pos, own_span = scan_first(own_sweep[2][:, :, -1], own_sweep[3][:, :, -1], 1)
    own_neg, _ = scan_first(own_sweep[0][:, :, 0], own_sweep[1][:, :, 0], -1)
    old_moments = tree_sum(jnp.dot(weighted, distribution, precision=HIGH), ("vel",))
    own_pos, own_neg, old_moments = lax.optimization_barrier((own_pos, own_neg, old_moments))
    moment_drive = thickness * old_moments.reshape(5, 1, length, TUBES) / denominator
    moment_sweep = local_sweep(carry_rate, moment_drive)
    own_pos, own_neg, moment_pos, moment_neg = caught_up(
        own_pos, own_neg, own_span, moment_sweep, count
    )
    span = min(2 * own_span, count)
    while span < count - 1:
        own_pos, moment_pos = joint_next(own_pos, moment_pos, span, 1)
        own_neg, moment_neg = joint_next(own_neg, moment_neg, span, -1)
        span *= 2
        own_pos, own_neg, moment_pos, moment_neg = lax.optimization_barrier(
            (own_pos, own_neg, moment_pos, moment_neg)
        )
    own_field = joined_field(own_sweep, own_neg[1], own_pos[1])
    moment_field = joined_field(moment_sweep, moment_neg[1], moment_pos[1])
    basis = rebuild.reshape(5, node_rows, NXI, 1, 1)
    half_field = own_field + jnp.sum(basis * moment_field[:, None], axis=0)
    half_field = half_field.reshape(node_count, cell_count)
    half_moments = tree_sum(jnp.dot(weighted, half_field, precision=HIGH), ("vel",))
    residual = (half_moments - old_moments).reshape(5, length, TUBES)
    width = min(-(-JACOBI // length), lax.axis_size("sec") - 1)
    blocks = jnp.concatenate([lower_blocks, upper_blocks, diag_inverse], axis=0)
    wide = with_halo(
        jnp.concatenate([blocks.reshape(75, length, TUBES), residual], axis=0), width
    )
    lower_r = wide[:25]
    upper_r = wide[25:50]
    inverse_r = wide[50:75]
    residual_wide = wide[75:]
    correction = apply_block(inverse_r, residual_wide)
    edge_zero = jnp.zeros((5, 1, TUBES), jnp.float32)
    for sweep_index in range(JACOBI):
        from_left = jnp.concatenate([edge_zero, correction[:, :-1]], axis=1)
        from_right = jnp.concatenate([correction[:, 1:], edge_zero], axis=1)
        correction = apply_block(
            inverse_r,
            residual_wide - apply_block(lower_r, from_left) - apply_block(upper_r, from_right),
        )
    correction = correction[:, width * length : (width + 1) * length].reshape(5, cell_count)
    macro = half_moments + correction
    synthetic = half_field + jnp.dot(rebuild.T, correction, precision=HIGH)
    local_totals = jnp.sum(old_moments - macro, axis=1)[0:2]
    magnitude = jnp.sum(jnp.abs(synthetic), axis=1)
    line_loaded = jnp.sum((node_mass * magnitude).reshape(node_rows, NXI), axis=0)
    first_copy = (lax.axis_index("vel") == 0).astype(jnp.float32)
    gathered = tree_sum(
        jnp.concatenate([line_loaded, local_totals * first_copy]), ("vel", "sec")
    )
    loaded = gathered[:NXI]
    goal_mass = jnp.broadcast_to(gathered[NXI], (NXI,))
    goal_flow = jnp.broadcast_to(gathered[NXI + 1], (NXI,))
    spread = jnp.ones((NXI, NXI), jnp.float32)
    shift_mass = jnp.zeros((NXI,), jnp.float32)
    shift_flow = jnp.zeros((NXI,), jnp.float32)
    for newton_turn in range(NEWTON):
        growth = jnp.exp(shift_mass + shift_flow * line_signed)
        scaled = loaded * growth
        excess = loaded * (growth - 1.0)
        terms = jnp.stack(
            [scaled, scaled * line_signed, scaled * line_signed * line_signed, excess, excess * line_signed]
        )
        sums = jnp.dot(terms, spread, precision=HIGH)
        shift_mass, shift_flow = newton_update(shift_mass, shift_flow, sums, goal_mass, goal_flow)
    growth = jnp.exp(shift_mass + shift_flow * line_signed)
    synthetic_rows = synthetic.reshape(node_rows, NXI, cell_count)
    new_distribution = synthetic_rows + jnp.abs(synthetic_rows) * (growth[None, :, None] - 1.0)
    return (new_distribution.reshape(node_count, cell_count), macro)


def solution(mesh):
    in_specs = (P("vel", "sec"), P("sec"), P(None, "sec"), P(None, "sec"), P(None, "sec"))
    out_specs = (P("vel", "sec"), P(None, "sec"))
    return jax.shard_map(body, mesh=mesh, in_specs=in_specs, out_specs=out_specs, check_vma=False)
```

```python
import math

import jax
import jax.numpy as jnp
import numpy as np
from jax import lax
from jax.sharding import PartitionSpec as P

NXI = 24
TUBES = 128
JACOBI = 4
NEWTON = 2


HIGH = lax.Precision.HIGHEST
pseudo_rate = 1.0


def passed_along(block, axis, distance):
    devices = range(lax.axis_size(axis))
    route = [(i - distance, i) for i in devices if i - distance in devices]
    return lax.ppermute(block, axis, route)


def extended(array, sides, width):
    for axis, dim in sides:
        count, length = (lax.axis_size(axis), array.shape[dim])
        up = [(i, (i + 1) % count) for i in range(count - 1)]
        down = [(j, i) for i, j in up]
        last = lax.slice_in_dim(array, length - width, length, axis=dim)
        first = lax.slice_in_dim(array, 0, width, axis=dim)
        before = lax.ppermute(last, axis, up)
        after = lax.ppermute(first, axis, down)
        array = jnp.concatenate([before, array, after], axis=dim)
    return array


def hermite_rule(count):
    quarter = math.pi ** (-0.25)
    found = []
    last_slope = 1.0
    for index in range(count // 2):
        if index == 0:
            guess = math.sqrt(2.0 * count + 1.0) - 1.85575 * (2.0 * count + 1.0) ** (-0.16667)
        elif index == 1:
            guess = guess - 1.14 * count**0.426 / guess
        elif index == 2:
            guess = 1.86 * guess - 0.86 * found[0][0]
        elif index == 3:
            guess = 1.91 * guess - 0.91 * found[1][0]
        else:
            guess = 2.0 * guess - found[index - 2][0]
        for repeat in range(60):
            current = quarter
            previous = 0.0
            for order in range(count):
                older = previous
                previous = current
                current = (
                    guess * math.sqrt(2.0 / (order + 1)) * previous
                    - math.sqrt(order / (order + 1.0)) * older
                )
            last_slope = math.sqrt(2.0 * count) * previous
            guess = guess - current / last_slope
        found.append((guess, 2.0 / (last_slope * last_slope)))
    positive = found[::-1]
    points = [-pair[0] for pair in found] + [pair[0] for pair in positive]
    weights = [pair[1] for pair in found] + [pair[1] for pair in positive]
    return (np.array(points), np.array(weights))


def node_tables(axis_points):
    points, weights = hermite_rule(axis_points)
    node_index = np.arange(axis_points**3)
    idx_x = node_index % axis_points
    idx_z = node_index // axis_points % axis_points
    idx_y = node_index // (axis_points * axis_points)
    along_x = points[idx_x]
    along_y = points[idx_y]
    along_z = points[idx_z]
    node_weight = weights[idx_x] * weights[idx_y] * weights[idx_z] / math.pi**1.5
    energy = along_x**2 + along_y**2 + along_z**2 - 1.5
    moment_basis = np.stack([along_x * 0.0 + 1.0, along_x, along_y, along_z, energy])
    norm_scale = np.array([1.0, 0.5, 0.5, 0.5, 1.5])
    return (
        along_x,
        node_weight,
        moment_basis * node_weight[None, :],
        moment_basis / norm_scale[:, None],
    )


def apply_block(matrices, vector):
    shaped = matrices.reshape((5, 5) + vector.shape[1:])
    return jnp.sum(shaped * vector[None], axis=1)


def affine_combine(earlier_map, later_map):
    return (later_map[0] * earlier_map[0], later_map[0] * earlier_map[1] + later_map[1])


def newton_sums(loaded, signed, shift_mass, shift_flow):
    growth = jnp.exp(shift_mass + shift_flow * signed)
    scaled = loaded * growth
    excess = loaded * (growth - 1.0)
    return jnp.stack(
        [
            jnp.sum(scaled),
            jnp.sum(scaled * signed),
            jnp.sum(scaled * signed * signed),
            jnp.sum(excess),
            jnp.sum(excess * signed),
        ]
    )


def newton_update(shift_mass, shift_flow, sums, goal_mass, goal_flow):
    resid_mass = sums[3] - goal_mass
    resid_flow = sums[4] - goal_flow
    determinant = sums[0] * sums[2] - sums[1] * sums[1]
    new_mass = shift_mass - (sums[2] * resid_mass - sums[1] * resid_flow) / determinant
    new_flow = shift_flow - (sums[0] * resid_flow - sums[1] * resid_mass) / determinant
    return (new_mass, new_flow)


def received(block, distance):
    count = lax.axis_size("sec")
    if abs(distance) >= count:
        return jnp.zeros_like(block)
    return passed_along(block, "sec", distance)


def fetched(state, distance, sign):
    rate, drive = state
    got = received(jnp.concatenate([rate, drive], axis=0), sign * distance)
    return got[:1], got[1:]


def scan_first(rate, drive, sign):
    near_a, near_b = fetched((rate, drive), 1, sign)
    if lax.axis_size("sec") <= 2:
        return (near_a, near_b), 1
    far_a, far_b = fetched((rate, drive), 2, sign)
    return (near_a * far_a, near_a * far_b + near_b), 2


def scan_next(state, span, sign):
    got_a, got_b = fetched(state, span, sign)
    return (state[0] * got_a, state[0] * got_b + state[1]), span * 2


def exclusive_inflow(rate, drive, sign):
    state, span = scan_first(rate, drive, sign)
    while span < lax.axis_size("sec") - 1:
        state, span = scan_next(state, span, sign)
    return state[1]


def with_halo(array, width):
    parts = [received(array, d) for d in range(width, 0, -1)]
    parts.append(array)
    parts.extend(received(array, -d) for d in range(1, width + 1))
    return jnp.concatenate(parts, axis=1)


def group_sum(block, axis, low_bit, members):
    count = lax.axis_size(axis)
    if members == 2:
        pairs = [(i, i ^ (1 << low_bit)) for i in range(count)]
        return block + lax.ppermute(block, axis, pairs)
    mine = (lax.axis_index(axis) >> low_bit) % members
    shifted = [block]
    for step in range(1, members):
        pairs = []
        for i in range(count):
            place = (i >> low_bit) % members
            base = i - (place << low_bit)
            pairs.append((base + (((place + step) % members) << low_bit), i))
        shifted.append(lax.ppermute(block, axis, pairs))
    stacked = jnp.stack(shifted)
    total = None
    for member in range(members):
        value = lax.dynamic_index_in_dim(stacked, (member - mine) % members, 0, keepdims=False)
        total = value if total is None else total + value
    return total


def sum_plan(axis, count):
    bits = count.bit_length() - 1
    plan = []
    bit = 0
    if axis == "vel" and bits % 2 == 1:
        plan.append((0, 2))
        bit = 1
    elif axis == "vel" and bits >= 2:
        plan.append((0, 2))
        bit = 1
    while bit + 1 < bits:
        plan.append((bit, 4))
        bit += 2
    if bit < bits:
        plan.append((bit, 2))
    return plan


def tree_sum(block, axes):
    for axis in axes:
        count = lax.axis_size(axis)
        if count & (count - 1):
            block = lax.psum(block, axis)
            continue
        for low_bit, members in sum_plan(axis, count):
            block = group_sum(block, axis, low_bit, members)
    return block


def local_sweep(carry_rate, drive):
    half_nodes = NXI // 2
    shape = (1, half_nodes) + drive.shape[2:]
    prod_neg, local_neg = lax.associative_scan(
        affine_combine,
        (jnp.broadcast_to(carry_rate[:, :half_nodes], shape), drive[:, :half_nodes]),
        reverse=True,
        axis=2,
    )
    prod_pos, local_pos = lax.associative_scan(
        affine_combine,
        (jnp.broadcast_to(carry_rate[:, half_nodes:], shape), drive[:, half_nodes:]),
        axis=2,
    )
    return prod_neg, local_neg, prod_pos, local_pos


def joined_field(sweep, inflow_neg, inflow_pos):
    prod_neg, local_neg, prod_pos, local_pos = sweep
    field_neg = local_neg + prod_neg * inflow_neg[:, :, None, :]
    field_pos = local_pos + prod_pos * inflow_pos[:, :, None, :]
    return jnp.concatenate([field_neg, field_pos], axis=1)


def swept_field(carry_rate, drive):
    sweep = local_sweep(carry_rate, drive)
    inflow_pos = exclusive_inflow(sweep[2][:, :, -1], sweep[3][:, :, -1], 1)
    inflow_neg = exclusive_inflow(sweep[0][:, :, 0], sweep[1][:, :, 0], -1)
    return joined_field(sweep, inflow_neg, inflow_pos)


def caught_up_side(own, own_span, rate, drive, count, sign):
    reach = min(2 * own_span, count - 1)
    own_rows = own[1].shape[0]
    moment_rows = drive.shape[0]
    fetched_maps = {}
    for distance in range(1, reach + 1):
        if distance == own_span and own_span < count - 1:
            packed = jnp.concatenate([own[0], own[1], rate, drive], axis=0)
            got = received(packed, sign * distance)
            got_own = (got[:1], got[1 : 1 + own_rows])
            fetched_maps[distance] = (got[1 + own_rows : 2 + own_rows], got[2 + own_rows :])
        else:
            got = received(jnp.concatenate([rate, drive], axis=0), sign * distance)
            fetched_maps[distance] = (got[:1], got[1:])
    if own_span < count - 1:
        own = (own[0] * got_own[0], own[0] * got_own[1] + own[1])
    acc_a, acc_b = fetched_maps[reach]
    for distance in range(reach - 1, 0, -1):
        near_a, near_b = fetched_maps[distance]
        acc_a, acc_b = near_a * acc_a, near_a * acc_b + near_b
    return own, (acc_a, acc_b)


def caught_up(own_pos, own_neg, own_span, moment_sweep, count):
    own_pos, moment_pos = caught_up_side(
        own_pos, own_span, moment_sweep[2][:, :, -1], moment_sweep[3][:, :, -1], count, 1
    )
    own_neg, moment_neg = caught_up_side(
        own_neg, own_span, moment_sweep[0][:, :, 0], moment_sweep[1][:, :, 0], count, -1
    )
    return lax.optimization_barrier((own_pos, own_neg, moment_pos, moment_neg))


def joint_next(own, moment, span, sign):
    own_rows = own[1].shape[0]
    packed = jnp.concatenate([own[0], own[1], moment[1]], axis=0)
    got = received(packed, sign * span)
    got_a, got_own, got_moment = got[:1], got[1 : 1 + own_rows], got[1 + own_rows :]
    return (
        (own[0] * got_a, own[0] * got_own + own[1]),
        (own[0] * got_a, own[0] * got_moment + moment[1]),
    )


def body(distribution, collision, lower_blocks, upper_blocks, diag_inverse):
    node_count = distribution.shape[0]
    cell_count = distribution.shape[1]
    length = cell_count // TUBES
    node_rows = node_count // NXI
    half_nodes = NXI // 2
    along_x, node_weight, weighted_np, rebuild_np = node_tables(NXI)
    all_mass = jnp.asarray(node_weight, jnp.float32)
    offset = lax.axis_index("vel") * node_count
    weighted = lax.dynamic_slice_in_dim(
        jnp.asarray(weighted_np, jnp.float32), offset, node_count, 1
    )
    rebuild = lax.dynamic_slice_in_dim(jnp.asarray(rebuild_np, jnp.float32), offset, node_count, 1)
    node_mass = lax.dynamic_slice_in_dim(all_mass, offset, node_count, 0)
    line_signed = jnp.asarray(along_x[:NXI], jnp.float32)
    total_length = length * lax.axis_size("sec")
    thickness = collision.reshape(1, 1, length, TUBES)
    node_speed = jnp.abs(line_signed).reshape(1, NXI, 1, 1)
    denominator = node_speed * total_length + thickness + pseudo_rate
    carry_rate = node_speed * total_length / denominator
    own_drive = pseudo_rate * distribution.reshape(node_rows, NXI, length, TUBES) / denominator
    count = lax.axis_size("sec")
    own_sweep = local_sweep(carry_rate, own_drive)
    own_pos = fetched((own_sweep[2][:, :, -1], own_sweep[3][:, :, -1]), 1, 1)
    own_neg = fetched((own_sweep[0][:, :, 0], own_sweep[1][:, :, 0]), 1, -1)
    own_span = 1
    old_moments = tree_sum(jnp.dot(weighted, distribution, precision=HIGH), ("vel",))
    own_pos, own_neg, old_moments = lax.optimization_barrier((own_pos, own_neg, old_moments))
    moment_drive = thickness * old_moments.reshape(5, 1, length, TUBES) / denominator
    moment_sweep = local_sweep(carry_rate, moment_drive)
    own_pos, own_neg, moment_pos, moment_neg = caught_up(
        own_pos, own_neg, own_span, moment_sweep, count
    )
    span = min(2 * own_span, count)
    while span < count - 1:
        own_pos, moment_pos = joint_next(own_pos, moment_pos, span, 1)
        own_neg, moment_neg = joint_next(own_neg, moment_neg, span, -1)
        span *= 2
        own_pos, own_neg, moment_pos, moment_neg = lax.optimization_barrier(
            (own_pos, own_neg, moment_pos, moment_neg)
        )
    own_field = joined_field(own_sweep, own_neg[1], own_pos[1])
    moment_field = joined_field(moment_sweep, moment_neg[1], moment_pos[1])
    basis = rebuild.reshape(5, node_rows, NXI, 1, 1)
    half_field = own_field + jnp.sum(basis * moment_field[:, None], axis=0)
    half_field = half_field.reshape(node_count, cell_count)
    half_moments = tree_sum(jnp.dot(weighted, half_field, precision=HIGH), ("vel",))
    residual = (half_moments - old_moments).reshape(5, length, TUBES)
    width = min(-(-JACOBI // length), lax.axis_size("sec") - 1)
    blocks = jnp.concatenate([lower_blocks, upper_blocks, diag_inverse], axis=0)
    wide = with_halo(
        jnp.concatenate([blocks.reshape(75, length, TUBES), residual], axis=0), width
    )
    lower_r = wide[:25]
    upper_r = wide[25:50]
    inverse_r = wide[50:75]
    residual_wide = wide[75:]
    correction = apply_block(inverse_r, residual_wide)
    edge_zero = jnp.zeros((5, 1, TUBES), jnp.float32)
    for sweep_index in range(JACOBI):
        from_left = jnp.concatenate([edge_zero, correction[:, :-1]], axis=1)
        from_right = jnp.concatenate([correction[:, 1:], edge_zero], axis=1)
        correction = apply_block(
            inverse_r,
            residual_wide - apply_block(lower_r, from_left) - apply_block(upper_r, from_right),
        )
    correction = correction[:, width * length : (width + 1) * length].reshape(5, cell_count)
    macro = half_moments + correction
    synthetic = half_field + jnp.dot(rebuild.T, correction, precision=HIGH)
    local_totals = jnp.sum(old_moments - macro, axis=1)[0:2]
    magnitude = jnp.sum(jnp.abs(synthetic), axis=1)
    line_loaded = jnp.sum((node_mass * magnitude).reshape(node_rows, NXI), axis=0)
    first_copy = (lax.axis_index("vel") == 0).astype(jnp.float32)
    gathered = tree_sum(
        jnp.concatenate([line_loaded, local_totals * first_copy]), ("vel", "sec")
    )
    loaded = gathered[:NXI]
    goal_mass = jnp.broadcast_to(gathered[NXI], (NXI,))
    goal_flow = jnp.broadcast_to(gathered[NXI + 1], (NXI,))
    spread = jnp.ones((NXI, NXI), jnp.float32)
    shift_mass = jnp.zeros((NXI,), jnp.float32)
    shift_flow = jnp.zeros((NXI,), jnp.float32)
    for newton_turn in range(NEWTON):
        growth = jnp.exp(shift_mass + shift_flow * line_signed)
        scaled = loaded * growth
        excess = loaded * (growth - 1.0)
        terms = jnp.stack(
            [scaled, scaled * line_signed, scaled * line_signed * line_signed, excess, excess * line_signed]
        )
        sums = jnp.dot(terms, spread, precision=HIGH)
        shift_mass, shift_flow = newton_update(shift_mass, shift_flow, sums, goal_mass, goal_flow)
    growth = jnp.exp(shift_mass + shift_flow * line_signed)
    synthetic_rows = synthetic.reshape(node_rows, NXI, cell_count)
    new_distribution = synthetic_rows + jnp.abs(synthetic_rows) * (growth[None, :, None] - 1.0)
    return (new_distribution.reshape(node_count, cell_count), macro)


def solution(mesh):
    in_specs = (P("vel", "sec"), P("sec"), P(None, "sec"), P(None, "sec"), P(None, "sec"))
    out_specs = (P("vel", "sec"), P(None, "sec"))
    return jax.shard_map(body, mesh=mesh, in_specs=in_specs, out_specs=out_specs, check_vma=False)
```

```python
import math

import jax
import jax.numpy as jnp
import numpy as np
from jax import lax
from jax.sharding import PartitionSpec as P

NXI = 24
TUBES = 128
JACOBI = 4
NEWTON = 2


HIGH = lax.Precision.HIGHEST
pseudo_rate = 1.0


def passed_along(block, axis, distance):
    devices = range(lax.axis_size(axis))
    route = [(i - distance, i) for i in devices if i - distance in devices]
    return lax.ppermute(block, axis, route)


def extended(array, sides, width):
    for axis, dim in sides:
        count, length = (lax.axis_size(axis), array.shape[dim])
        up = [(i, (i + 1) % count) for i in range(count - 1)]
        down = [(j, i) for i, j in up]
        last = lax.slice_in_dim(array, length - width, length, axis=dim)
        first = lax.slice_in_dim(array, 0, width, axis=dim)
        before = lax.ppermute(last, axis, up)
        after = lax.ppermute(first, axis, down)
        array = jnp.concatenate([before, array, after], axis=dim)
    return array


def hermite_rule(count):
    quarter = math.pi ** (-0.25)
    found = []
    last_slope = 1.0
    for index in range(count // 2):
        if index == 0:
            guess = math.sqrt(2.0 * count + 1.0) - 1.85575 * (2.0 * count + 1.0) ** (-0.16667)
        elif index == 1:
            guess = guess - 1.14 * count**0.426 / guess
        elif index == 2:
            guess = 1.86 * guess - 0.86 * found[0][0]
        elif index == 3:
            guess = 1.91 * guess - 0.91 * found[1][0]
        else:
            guess = 2.0 * guess - found[index - 2][0]
        for repeat in range(60):
            current = quarter
            previous = 0.0
            for order in range(count):
                older = previous
                previous = current
                current = (
                    guess * math.sqrt(2.0 / (order + 1)) * previous
                    - math.sqrt(order / (order + 1.0)) * older
                )
            last_slope = math.sqrt(2.0 * count) * previous
            guess = guess - current / last_slope
        found.append((guess, 2.0 / (last_slope * last_slope)))
    positive = found[::-1]
    points = [-pair[0] for pair in found] + [pair[0] for pair in positive]
    weights = [pair[1] for pair in found] + [pair[1] for pair in positive]
    return (np.array(points), np.array(weights))


def node_tables(axis_points):
    points, weights = hermite_rule(axis_points)
    node_index = np.arange(axis_points**3)
    idx_x = node_index % axis_points
    idx_z = node_index // axis_points % axis_points
    idx_y = node_index // (axis_points * axis_points)
    along_x = points[idx_x]
    along_y = points[idx_y]
    along_z = points[idx_z]
    node_weight = weights[idx_x] * weights[idx_y] * weights[idx_z] / math.pi**1.5
    energy = along_x**2 + along_y**2 + along_z**2 - 1.5
    moment_basis = np.stack([along_x * 0.0 + 1.0, along_x, along_y, along_z, energy])
    norm_scale = np.array([1.0, 0.5, 0.5, 0.5, 1.5])
    return (
        along_x,
        node_weight,
        moment_basis * node_weight[None, :],
        moment_basis / norm_scale[:, None],
    )


def apply_block(matrices, vector):
    shaped = matrices.reshape((5, 5) + vector.shape[1:])
    return jnp.sum(shaped * vector[None], axis=1)


def affine_combine(earlier_map, later_map):
    return (later_map[0] * earlier_map[0], later_map[0] * earlier_map[1] + later_map[1])


def newton_sums(loaded, signed, shift_mass, shift_flow):
    growth = jnp.exp(shift_mass + shift_flow * signed)
    scaled = loaded * growth
    excess = loaded * (growth - 1.0)
    return jnp.stack(
        [
            jnp.sum(scaled),
            jnp.sum(scaled * signed),
            jnp.sum(scaled * signed * signed),
            jnp.sum(excess),
            jnp.sum(excess * signed),
        ]
    )


def newton_update(shift_mass, shift_flow, sums, goal_mass, goal_flow):
    resid_mass = sums[3] - goal_mass
    resid_flow = sums[4] - goal_flow
    determinant = sums[0] * sums[2] - sums[1] * sums[1]
    new_mass = shift_mass - (sums[2] * resid_mass - sums[1] * resid_flow) / determinant
    new_flow = shift_flow - (sums[0] * resid_flow - sums[1] * resid_mass) / determinant
    return (new_mass, new_flow)


def received(block, distance):
    count = lax.axis_size("sec")
    if abs(distance) >= count:
        return jnp.zeros_like(block)
    return passed_along(block, "sec", distance)


def fetched(state, distance, sign):
    rate, drive = state
    got = received(jnp.concatenate([rate, drive], axis=0), sign * distance)
    return got[:1], got[1:]


def scan_first(rate, drive, sign):
    near_a, near_b = fetched((rate, drive), 1, sign)
    if lax.axis_size("sec") <= 2:
        return (near_a, near_b), 1
    far_a, far_b = fetched((rate, drive), 2, sign)
    return (near_a * far_a, near_a * far_b + near_b), 2


def scan_next(state, span, sign):
    got_a, got_b = fetched(state, span, sign)
    return (state[0] * got_a, state[0] * got_b + state[1]), span * 2


def exclusive_inflow(rate, drive, sign):
    state, span = scan_first(rate, drive, sign)
    while span < lax.axis_size("sec") - 1:
        state, span = scan_next(state, span, sign)
    return state[1]


def with_halo(array, width):
    parts = [received(array, d) for d in range(width, 0, -1)]
    parts.append(array)
    parts.extend(received(array, -d) for d in range(1, width + 1))
    return jnp.concatenate(parts, axis=1)


def group_sum(block, axis, low_bit, members):
    count = lax.axis_size(axis)
    if members == 2:
        pairs = [(i, i ^ (1 << low_bit)) for i in range(count)]
        return block + lax.ppermute(block, axis, pairs)
    mine = (lax.axis_index(axis) >> low_bit) % members
    shifted = [block]
    for step in range(1, members):
        pairs = []
        for i in range(count):
            place = (i >> low_bit) % members
            base = i - (place << low_bit)
            pairs.append((base + (((place + step) % members) << low_bit), i))
        shifted.append(lax.ppermute(block, axis, pairs))
    stacked = jnp.stack(shifted)
    total = None
    for member in range(members):
        value = lax.dynamic_index_in_dim(stacked, (member - mine) % members, 0, keepdims=False)
        total = value if total is None else total + value
    return total


def sum_plan(axis, count):
    bits = count.bit_length() - 1
    plan = []
    bit = 0
    if axis == "vel" and bits % 2 == 1:
        plan.append((0, 2))
        bit = 1
    elif axis == "vel" and bits >= 2:
        plan.append((0, 2))
        bit = 1
    while bit + 1 < bits:
        plan.append((bit, 4))
        bit += 2
    if bit < bits:
        plan.append((bit, 2))
    return plan


def tree_sum(block, axes):
    for axis in axes:
        count = lax.axis_size(axis)
        if count & (count - 1):
            block = lax.psum(block, axis)
            continue
        for low_bit, members in sum_plan(axis, count):
            block = group_sum(block, axis, low_bit, members)
    return block


def local_sweep(carry_rate, drive):
    half_nodes = NXI // 2
    shape = (1, half_nodes) + drive.shape[2:]
    prod_neg, local_neg = lax.associative_scan(
        affine_combine,
        (jnp.broadcast_to(carry_rate[:, :half_nodes], shape), drive[:, :half_nodes]),
        reverse=True,
        axis=2,
    )
    prod_pos, local_pos = lax.associative_scan(
        affine_combine,
        (jnp.broadcast_to(carry_rate[:, half_nodes:], shape), drive[:, half_nodes:]),
        axis=2,
    )
    return prod_neg, local_neg, prod_pos, local_pos


def joined_field(sweep, inflow_neg, inflow_pos):
    prod_neg, local_neg, prod_pos, local_pos = sweep
    field_neg = local_neg + prod_neg * inflow_neg[:, :, None, :]
    field_pos = local_pos + prod_pos * inflow_pos[:, :, None, :]
    return jnp.concatenate([field_neg, field_pos], axis=1)


def swept_field(carry_rate, drive):
    sweep = local_sweep(carry_rate, drive)
    inflow_pos = exclusive_inflow(sweep[2][:, :, -1], sweep[3][:, :, -1], 1)
    inflow_neg = exclusive_inflow(sweep[0][:, :, 0], sweep[1][:, :, 0], -1)
    return joined_field(sweep, inflow_neg, inflow_pos)


def caught_up_side(own, own_span, rate, drive, count, sign):
    reach = min(2 * own_span, count - 1)
    own_rows = own[1].shape[0]
    moment_rows = drive.shape[0]
    fetched_maps = {}
    for distance in range(1, reach + 1):
        if distance == own_span and own_span < count - 1:
            packed = jnp.concatenate([own[0], own[1], rate, drive], axis=0)
            got = received(packed, sign * distance)
            got_own = (got[:1], got[1 : 1 + own_rows])
            fetched_maps[distance] = (got[1 + own_rows : 2 + own_rows], got[2 + own_rows :])
        else:
            got = received(jnp.concatenate([rate, drive], axis=0), sign * distance)
            fetched_maps[distance] = (got[:1], got[1:])
    if own_span < count - 1:
        own = (own[0] * got_own[0], own[0] * got_own[1] + own[1])
    acc_a, acc_b = fetched_maps[reach]
    for distance in range(reach - 1, 0, -1):
        near_a, near_b = fetched_maps[distance]
        acc_a, acc_b = near_a * acc_a, near_a * acc_b + near_b
    return own, (acc_a, acc_b)


def caught_up(own_pos, own_neg, own_span, moment_sweep, count):
    own_pos, moment_pos = caught_up_side(
        own_pos, own_span, moment_sweep[2][:, :, -1], moment_sweep[3][:, :, -1], count, 1
    )
    own_neg, moment_neg = caught_up_side(
        own_neg, own_span, moment_sweep[0][:, :, 0], moment_sweep[1][:, :, 0], count, -1
    )
    return lax.optimization_barrier((own_pos, own_neg, moment_pos, moment_neg))


def joint_next(own, moment, span, sign):
    own_rows = own[1].shape[0]
    packed = jnp.concatenate([own[0], own[1], moment[1]], axis=0)
    got = received(packed, sign * span)
    got_a, got_own, got_moment = got[:1], got[1 : 1 + own_rows], got[1 + own_rows :]
    return (
        (own[0] * got_a, own[0] * got_own + own[1]),
        (own[0] * got_a, own[0] * got_moment + moment[1]),
    )


def line_block(matrices, vector):
    shaped = matrices.reshape(matrices.shape[:-1] + (5, 5))
    return jnp.sum(shaped * vector[..., None, :], axis=-1)


def body(distribution, collision, lower_blocks, upper_blocks, diag_inverse):
    node_count = distribution.shape[0]
    cell_count = distribution.shape[1]
    length = cell_count // TUBES
    node_rows = node_count // NXI
    count = lax.axis_size("sec")
    total_length = length * count
    share = TUBES // count
    along_x, node_weight, weighted_np, rebuild_np = node_tables(NXI)
    offset = lax.axis_index("vel") * node_count
    weighted = lax.dynamic_slice_in_dim(
        jnp.asarray(weighted_np, jnp.float32), offset, node_count, 1
    )
    rebuild = lax.dynamic_slice_in_dim(jnp.asarray(rebuild_np, jnp.float32), offset, node_count, 1)
    node_mass = lax.dynamic_slice_in_dim(jnp.asarray(node_weight, jnp.float32), offset, node_count, 0)
    line_signed = jnp.asarray(along_x[:NXI], jnp.float32)
    node_signed = jnp.asarray(np.tile(along_x[:NXI], node_rows), jnp.float32)
    packed = jnp.concatenate(
        [distribution, collision.reshape(1, cell_count), lower_blocks, upper_blocks, diag_inverse],
        axis=0,
    )
    rows = packed.shape[0]
    packed = packed.reshape(rows, length, TUBES).transpose(1, 2, 0)
    lines = lax.all_to_all(packed, "sec", 1, 0, tiled=True)
    dist_t = lines[:, :, :node_count]
    thickness = lines[:, :, node_count : node_count + 1]
    lower_t = lines[:, :, node_count + 1 : node_count + 26]
    upper_t = lines[:, :, node_count + 26 : node_count + 51]
    inverse_t = lines[:, :, node_count + 51 : node_count + 76]
    cells = total_length * share
    old_moments = tree_sum(
        jnp.dot(dist_t.reshape(cells, node_count), weighted.T, precision=HIGH), ("vel",)
    )
    target = jnp.dot(old_moments, rebuild, precision=HIGH).reshape(total_length, share, node_count)
    node_speed = jnp.abs(node_signed)
    denominator = node_speed * total_length + thickness + pseudo_rate
    carry_rate = node_speed * total_length / denominator
    drive_term = (thickness * target + pseudo_rate * dist_t) / denominator
    _, forward = lax.associative_scan(affine_combine, (carry_rate, drive_term), axis=0)
    _, backward = lax.associative_scan(
        affine_combine, (carry_rate, drive_term), reverse=True, axis=0
    )
    half_field = jnp.where(node_signed > 0, forward, backward)
    half_moments = tree_sum(
        jnp.dot(half_field.reshape(cells, node_count), weighted.T, precision=HIGH), ("vel",)
    )
    residual = (half_moments - old_moments).reshape(total_length, share, 5)
    correction = line_block(inverse_t, residual)
    edge_zero = jnp.zeros((1, share, 5), jnp.float32)
    for sweep_index in range(JACOBI):
        from_left = jnp.concatenate([edge_zero, correction[:-1]], axis=0)
        from_right = jnp.concatenate([correction[1:], edge_zero], axis=0)
        correction = line_block(
            inverse_t,
            residual - line_block(lower_t, from_left) - line_block(upper_t, from_right),
        )
    correction = correction.reshape(cells, 5)
    macro = half_moments + correction
    synthetic = half_field + jnp.dot(correction, rebuild, precision=HIGH).reshape(
        total_length, share, node_count
    )
    local_totals = jnp.sum(old_moments - macro, axis=0)[0:2]
    magnitude = jnp.sum(jnp.abs(synthetic), axis=(0, 1))
    line_loaded = jnp.sum((node_mass * magnitude).reshape(node_rows, NXI), axis=0)
    first_copy = (lax.axis_index("vel") == 0).astype(jnp.float32)
    back = jnp.concatenate([synthetic, macro.reshape(total_length, share, 5)], axis=2)
    back = lax.all_to_all(back, "sec", 0, 1, tiled=True)
    back = back.transpose(2, 0, 1).reshape(node_count + 5, cell_count)
    gathered = tree_sum(
        jnp.concatenate([line_loaded, local_totals * first_copy]), ("vel", "sec")
    )
    loaded = gathered[:NXI]
    goal_mass = jnp.broadcast_to(gathered[NXI], (NXI,))
    goal_flow = jnp.broadcast_to(gathered[NXI + 1], (NXI,))
    spread = jnp.ones((NXI, NXI), jnp.float32)
    shift_mass = jnp.zeros((NXI,), jnp.float32)
    shift_flow = jnp.zeros((NXI,), jnp.float32)
    for newton_turn in range(NEWTON):
        growth = jnp.exp(shift_mass + shift_flow * line_signed)
        scaled = loaded * growth
        excess = loaded * (growth - 1.0)
        terms = jnp.stack(
            [scaled, scaled * line_signed, scaled * line_signed * line_signed, excess, excess * line_signed]
        )
        sums = jnp.dot(terms, spread, precision=HIGH)
        shift_mass, shift_flow = newton_update(shift_mass, shift_flow, sums, goal_mass, goal_flow)
    growth = jnp.exp(shift_mass + shift_flow * line_signed)
    synthetic_rows = back[:node_count].reshape(node_rows, NXI, cell_count)
    new_distribution = synthetic_rows + jnp.abs(synthetic_rows) * (growth[None, :, None] - 1.0)
    return (new_distribution.reshape(node_count, cell_count), back[node_count:])


def solution(mesh):
    in_specs = (P("vel", "sec"), P("sec"), P(None, "sec"), P(None, "sec"), P(None, "sec"))
    out_specs = (P("vel", "sec"), P(None, "sec"))
    return jax.shard_map(body, mesh=mesh, in_specs=in_specs, out_specs=out_specs, check_vma=False)
```

```python
import math

import jax
import jax.numpy as jnp
import numpy as np
from jax import lax
from jax.experimental import pallas as pl
from jax.sharding import PartitionSpec as P

NXI = 24
TUBES = 128
JACOBI = 4
NEWTON = 2


HIGH = lax.Precision.HIGHEST
pseudo_rate = 1.0


def passed_along(block, axis, distance):
    devices = range(lax.axis_size(axis))
    route = [(i - distance, i) for i in devices if i - distance in devices]
    return lax.ppermute(block, axis, route)


def extended(array, sides, width):
    for axis, dim in sides:
        count, length = (lax.axis_size(axis), array.shape[dim])
        up = [(i, (i + 1) % count) for i in range(count - 1)]
        down = [(j, i) for i, j in up]
        last = lax.slice_in_dim(array, length - width, length, axis=dim)
        first = lax.slice_in_dim(array, 0, width, axis=dim)
        before = lax.ppermute(last, axis, up)
        after = lax.ppermute(first, axis, down)
        array = jnp.concatenate([before, array, after], axis=dim)
    return array


def hermite_rule(count):
    quarter = math.pi ** (-0.25)
    found = []
    last_slope = 1.0
    for index in range(count // 2):
        if index == 0:
            guess = math.sqrt(2.0 * count + 1.0) - 1.85575 * (2.0 * count + 1.0) ** (-0.16667)
        elif index == 1:
            guess = guess - 1.14 * count**0.426 / guess
        elif index == 2:
            guess = 1.86 * guess - 0.86 * found[0][0]
        elif index == 3:
            guess = 1.91 * guess - 0.91 * found[1][0]
        else:
            guess = 2.0 * guess - found[index - 2][0]
        for repeat in range(60):
            current = quarter
            previous = 0.0
            for order in range(count):
                older = previous
                previous = current
                current = (
                    guess * math.sqrt(2.0 / (order + 1)) * previous
                    - math.sqrt(order / (order + 1.0)) * older
                )
            last_slope = math.sqrt(2.0 * count) * previous
            guess = guess - current / last_slope
        found.append((guess, 2.0 / (last_slope * last_slope)))
    positive = found[::-1]
    points = [-pair[0] for pair in found] + [pair[0] for pair in positive]
    weights = [pair[1] for pair in found] + [pair[1] for pair in positive]
    return (np.array(points), np.array(weights))


def node_tables(axis_points):
    points, weights = hermite_rule(axis_points)
    node_index = np.arange(axis_points**3)
    idx_x = node_index % axis_points
    idx_z = node_index // axis_points % axis_points
    idx_y = node_index // (axis_points * axis_points)
    along_x = points[idx_x]
    along_y = points[idx_y]
    along_z = points[idx_z]
    node_weight = weights[idx_x] * weights[idx_y] * weights[idx_z] / math.pi**1.5
    energy = along_x**2 + along_y**2 + along_z**2 - 1.5
    moment_basis = np.stack([along_x * 0.0 + 1.0, along_x, along_y, along_z, energy])
    norm_scale = np.array([1.0, 0.5, 0.5, 0.5, 1.5])
    return (
        along_x,
        node_weight,
        moment_basis * node_weight[None, :],
        moment_basis / norm_scale[:, None],
    )


def apply_block(matrices, vector):
    shaped = matrices.reshape((5, 5) + vector.shape[1:])
    return jnp.sum(shaped * vector[None], axis=1)


def affine_combine(earlier_map, later_map):
    return (later_map[0] * earlier_map[0], later_map[0] * earlier_map[1] + later_map[1])


def newton_sums(loaded, signed, shift_mass, shift_flow):
    growth = jnp.exp(shift_mass + shift_flow * signed)
    scaled = loaded * growth
    excess = loaded * (growth - 1.0)
    return jnp.stack(
        [
            jnp.sum(scaled),
            jnp.sum(scaled * signed),
            jnp.sum(scaled * signed * signed),
            jnp.sum(excess),
            jnp.sum(excess * signed),
        ]
    )


def newton_update(shift_mass, shift_flow, sums, goal_mass, goal_flow):
    resid_mass = sums[3] - goal_mass
    resid_flow = sums[4] - goal_flow
    determinant = sums[0] * sums[2] - sums[1] * sums[1]
    new_mass = shift_mass - (sums[2] * resid_mass - sums[1] * resid_flow) / determinant
    new_flow = shift_flow - (sums[0] * resid_flow - sums[1] * resid_mass) / determinant
    return (new_mass, new_flow)


def received(block, distance):
    count = lax.axis_size("sec")
    if abs(distance) >= count:
        return jnp.zeros_like(block)
    return passed_along(block, "sec", distance)


def fetched(state, distance, sign):
    rate, drive = state
    got = received(jnp.concatenate([rate, drive], axis=0), sign * distance)
    return got[:1], got[1:]


def scan_first(rate, drive, sign):
    near_a, near_b = fetched((rate, drive), 1, sign)
    if lax.axis_size("sec") <= 2:
        return (near_a, near_b), 1
    far_a, far_b = fetched((rate, drive), 2, sign)
    return (near_a * far_a, near_a * far_b + near_b), 2


def scan_next(state, span, sign):
    got_a, got_b = fetched(state, span, sign)
    return (state[0] * got_a, state[0] * got_b + state[1]), span * 2


def exclusive_inflow(rate, drive, sign):
    state, span = scan_first(rate, drive, sign)
    while span < lax.axis_size("sec") - 1:
        state, span = scan_next(state, span, sign)
    return state[1]


def with_halo(array, width):
    parts = [received(array, d) for d in range(width, 0, -1)]
    parts.append(array)
    parts.extend(received(array, -d) for d in range(1, width + 1))
    return jnp.concatenate(parts, axis=1)


def group_sum(block, axis, low_bit, members):
    count = lax.axis_size(axis)
    if members == 2:
        pairs = [(i, i ^ (1 << low_bit)) for i in range(count)]
        return block + lax.ppermute(block, axis, pairs)
    mine = (lax.axis_index(axis) >> low_bit) % members
    shifted = [block]
    for step in range(1, members):
        pairs = []
        for i in range(count):
            place = (i >> low_bit) % members
            base = i - (place << low_bit)
            pairs.append((base + (((place + step) % members) << low_bit), i))
        shifted.append(lax.ppermute(block, axis, pairs))
    stacked = jnp.stack(shifted)
    total = None
    for member in range(members):
        value = lax.dynamic_index_in_dim(stacked, (member - mine) % members, 0, keepdims=False)
        total = value if total is None else total + value
    return total


def sum_plan(axis, count):
    bits = count.bit_length() - 1
    plan = []
    bit = 0
    if axis == "vel" and bits % 2 == 1:
        plan.append((0, 2))
        bit = 1
    elif axis == "vel" and bits >= 2:
        plan.append((0, 2))
        bit = 1
    while bit + 1 < bits:
        plan.append((bit, 4))
        bit += 2
    if bit < bits:
        plan.append((bit, 2))
    return plan


def tree_sum(block, axes):
    for axis in axes:
        count = lax.axis_size(axis)
        if count & (count - 1):
            block = lax.psum(block, axis)
            continue
        for low_bit, members in sum_plan(axis, count):
            block = group_sum(block, axis, low_bit, members)
    return block


def local_sweep(carry_rate, drive):
    half_nodes = NXI // 2
    shape = (1, half_nodes) + drive.shape[2:]
    prod_neg, local_neg = lax.associative_scan(
        affine_combine,
        (jnp.broadcast_to(carry_rate[:, :half_nodes], shape), drive[:, :half_nodes]),
        reverse=True,
        axis=2,
    )
    prod_pos, local_pos = lax.associative_scan(
        affine_combine,
        (jnp.broadcast_to(carry_rate[:, half_nodes:], shape), drive[:, half_nodes:]),
        axis=2,
    )
    return prod_neg, local_neg, prod_pos, local_pos


def joined_field(sweep, inflow_neg, inflow_pos):
    prod_neg, local_neg, prod_pos, local_pos = sweep
    field_neg = local_neg + prod_neg * inflow_neg[:, :, None, :]
    field_pos = local_pos + prod_pos * inflow_pos[:, :, None, :]
    return jnp.concatenate([field_neg, field_pos], axis=1)


def swept_field(carry_rate, drive):
    sweep = local_sweep(carry_rate, drive)
    inflow_pos = exclusive_inflow(sweep[2][:, :, -1], sweep[3][:, :, -1], 1)
    inflow_neg = exclusive_inflow(sweep[0][:, :, 0], sweep[1][:, :, 0], -1)
    return joined_field(sweep, inflow_neg, inflow_pos)


def caught_up_side(own, own_span, rate, drive, count, sign):
    reach = min(2 * own_span, count - 1)
    own_rows = own[1].shape[0]
    moment_rows = drive.shape[0]
    fetched_maps = {}
    for distance in range(1, reach + 1):
        if distance == own_span and own_span < count - 1:
            packed = jnp.concatenate([own[0], own[1], rate, drive], axis=0)
            got = received(packed, sign * distance)
            got_own = (got[:1], got[1 : 1 + own_rows])
            fetched_maps[distance] = (got[1 + own_rows : 2 + own_rows], got[2 + own_rows :])
        else:
            got = received(jnp.concatenate([rate, drive], axis=0), sign * distance)
            fetched_maps[distance] = (got[:1], got[1:])
    if own_span < count - 1:
        own = (own[0] * got_own[0], own[0] * got_own[1] + own[1])
    acc_a, acc_b = fetched_maps[reach]
    for distance in range(reach - 1, 0, -1):
        near_a, near_b = fetched_maps[distance]
        acc_a, acc_b = near_a * acc_a, near_a * acc_b + near_b
    return own, (acc_a, acc_b)


def caught_up(own_pos, own_neg, own_span, moment_sweep, count):
    own_pos, moment_pos = caught_up_side(
        own_pos, own_span, moment_sweep[2][:, :, -1], moment_sweep[3][:, :, -1], count, 1
    )
    own_neg, moment_neg = caught_up_side(
        own_neg, own_span, moment_sweep[0][:, :, 0], moment_sweep[1][:, :, 0], count, -1
    )
    return lax.optimization_barrier((own_pos, own_neg, moment_pos, moment_neg))


def joint_next(own, moment, span, sign):
    own_rows = own[1].shape[0]
    packed = jnp.concatenate([own[0], own[1], moment[1]], axis=0)
    got = received(packed, sign * span)
    got_a, got_own, got_moment = got[:1], got[1 : 1 + own_rows], got[1 + own_rows :]
    return (
        (own[0] * got_a, own[0] * got_own + own[1]),
        (own[0] * got_a, own[0] * got_moment + moment[1]),
    )


def sweep_kernel(rate_ref, drive_ref, sign_ref, out_ref):
    positions = rate_ref.shape[0]
    start = jnp.zeros(rate_ref.shape[1:], jnp.float32)

    def forward(p, carried):
        value = rate_ref[p] * carried + drive_ref[p]
        out_ref[p] = value
        return value

    lax.fori_loop(0, positions, forward, start)
    heading = sign_ref[...] > 0

    def backward(i, carried):
        p = positions - 1 - i
        value = rate_ref[p] * carried + drive_ref[p]
        out_ref[p] = jnp.where(heading, out_ref[p], value)
        return value

    lax.fori_loop(0, positions, backward, start)


def line_sweep(carry_rate, drive_term, node_signed):
    return pl.pallas_call(
        sweep_kernel,
        out_shape=jax.ShapeDtypeStruct(drive_term.shape, jnp.float32),
    )(carry_rate, drive_term, node_signed.reshape(1, -1))


def line_block(matrices, vector):
    shaped = matrices.reshape(matrices.shape[:-1] + (5, 5))
    return jnp.sum(shaped * vector[..., None, :], axis=-1)


def body(distribution, collision, lower_blocks, upper_blocks, diag_inverse):
    node_count = distribution.shape[0]
    cell_count = distribution.shape[1]
    length = cell_count // TUBES
    node_rows = node_count // NXI
    count = lax.axis_size("sec")
    total_length = length * count
    share = TUBES // count
    along_x, node_weight, weighted_np, rebuild_np = node_tables(NXI)
    offset = lax.axis_index("vel") * node_count
    weighted = lax.dynamic_slice_in_dim(
        jnp.asarray(weighted_np, jnp.float32), offset, node_count, 1
    )
    rebuild = lax.dynamic_slice_in_dim(jnp.asarray(rebuild_np, jnp.float32), offset, node_count, 1)
    node_mass = lax.dynamic_slice_in_dim(jnp.asarray(node_weight, jnp.float32), offset, node_count, 0)
    line_signed = jnp.asarray(along_x[:NXI], jnp.float32)
    node_signed = jnp.asarray(np.tile(along_x[:NXI], node_rows), jnp.float32)
    packed = jnp.concatenate(
        [distribution, collision.reshape(1, cell_count), lower_blocks, upper_blocks, diag_inverse],
        axis=0,
    )
    rows = packed.shape[0]
    packed = packed.reshape(rows, length, TUBES).transpose(1, 2, 0)
    lines = lax.all_to_all(packed, "sec", 1, 0, tiled=True)
    dist_t = lines[:, :, :node_count]
    thickness = lines[:, :, node_count : node_count + 1]
    lower_t = lines[:, :, node_count + 1 : node_count + 26]
    upper_t = lines[:, :, node_count + 26 : node_count + 51]
    inverse_t = lines[:, :, node_count + 51 : node_count + 76]
    cells = total_length * share
    old_moments = tree_sum(
        jnp.dot(dist_t.reshape(cells, node_count), weighted.T, precision=HIGH), ("vel",)
    )
    target = jnp.dot(old_moments, rebuild, precision=HIGH).reshape(total_length, share, node_count)
    node_speed = jnp.abs(node_signed)
    denominator = node_speed * total_length + thickness + pseudo_rate
    carry_rate = node_speed * total_length / denominator
    drive_term = (thickness * target + pseudo_rate * dist_t) / denominator
    carry_rate = jnp.broadcast_to(carry_rate, drive_term.shape)
    half_field = line_sweep(carry_rate, drive_term, node_signed)
    half_moments = tree_sum(
        jnp.dot(half_field.reshape(cells, node_count), weighted.T, precision=HIGH), ("vel",)
    )
    residual = (half_moments - old_moments).reshape(total_length, share, 5)
    correction = line_block(inverse_t, residual)
    edge_zero = jnp.zeros((1, share, 5), jnp.float32)
    for sweep_index in range(JACOBI):
        from_left = jnp.concatenate([edge_zero, correction[:-1]], axis=0)
        from_right = jnp.concatenate([correction[1:], edge_zero], axis=0)
        correction = line_block(
            inverse_t,
            residual - line_block(lower_t, from_left) - line_block(upper_t, from_right),
        )
    correction = correction.reshape(cells, 5)
    macro = half_moments + correction
    synthetic = half_field + jnp.dot(correction, rebuild, precision=HIGH).reshape(
        total_length, share, node_count
    )
    local_totals = jnp.sum(old_moments - macro, axis=0)[0:2]
    magnitude = jnp.sum(jnp.abs(synthetic), axis=(0, 1))
    line_loaded = jnp.sum((node_mass * magnitude).reshape(node_rows, NXI), axis=0)
    first_copy = (lax.axis_index("vel") == 0).astype(jnp.float32)
    back = jnp.concatenate([synthetic, macro.reshape(total_length, share, 5)], axis=2)
    back = lax.all_to_all(back, "sec", 0, 1, tiled=True)
    back = back.transpose(2, 0, 1).reshape(node_count + 5, cell_count)
    gathered = tree_sum(
        jnp.concatenate([line_loaded, local_totals * first_copy]), ("vel", "sec")
    )
    loaded = gathered[:NXI]
    goal_mass = jnp.broadcast_to(gathered[NXI], (NXI,))
    goal_flow = jnp.broadcast_to(gathered[NXI + 1], (NXI,))
    spread = jnp.ones((NXI, NXI), jnp.float32)
    shift_mass = jnp.zeros((NXI,), jnp.float32)
    shift_flow = jnp.zeros((NXI,), jnp.float32)
    for newton_turn in range(NEWTON):
        growth = jnp.exp(shift_mass + shift_flow * line_signed)
        scaled = loaded * growth
        excess = loaded * (growth - 1.0)
        terms = jnp.stack(
            [scaled, scaled * line_signed, scaled * line_signed * line_signed, excess, excess * line_signed]
        )
        sums = jnp.dot(terms, spread, precision=HIGH)
        shift_mass, shift_flow = newton_update(shift_mass, shift_flow, sums, goal_mass, goal_flow)
    growth = jnp.exp(shift_mass + shift_flow * line_signed)
    synthetic_rows = back[:node_count].reshape(node_rows, NXI, cell_count)
    new_distribution = synthetic_rows + jnp.abs(synthetic_rows) * (growth[None, :, None] - 1.0)
    return (new_distribution.reshape(node_count, cell_count), back[node_count:])


def solution(mesh):
    in_specs = (P("vel", "sec"), P("sec"), P(None, "sec"), P(None, "sec"), P(None, "sec"))
    out_specs = (P("vel", "sec"), P(None, "sec"))
    return jax.shard_map(body, mesh=mesh, in_specs=in_specs, out_specs=out_specs, check_vma=False)
```

```python
import math

import jax
import jax.numpy as jnp
import numpy as np
from jax import lax
from jax.experimental import pallas as pl
from jax.experimental.pallas import tpu as pltpu
from jax.sharding import PartitionSpec as P

NXI = 24
TUBES = 128
JACOBI = 4
NEWTON = 2


HIGH = lax.Precision.HIGHEST
pseudo_rate = 1.0


def passed_along(block, axis, distance):
    devices = range(lax.axis_size(axis))
    route = [(i - distance, i) for i in devices if i - distance in devices]
    return lax.ppermute(block, axis, route)


def extended(array, sides, width):
    for axis, dim in sides:
        count, length = (lax.axis_size(axis), array.shape[dim])
        up = [(i, (i + 1) % count) for i in range(count - 1)]
        down = [(j, i) for i, j in up]
        last = lax.slice_in_dim(array, length - width, length, axis=dim)
        first = lax.slice_in_dim(array, 0, width, axis=dim)
        before = lax.ppermute(last, axis, up)
        after = lax.ppermute(first, axis, down)
        array = jnp.concatenate([before, array, after], axis=dim)
    return array


def hermite_rule(count):
    quarter = math.pi ** (-0.25)
    found = []
    last_slope = 1.0
    for index in range(count // 2):
        if index == 0:
            guess = math.sqrt(2.0 * count + 1.0) - 1.85575 * (2.0 * count + 1.0) ** (-0.16667)
        elif index == 1:
            guess = guess - 1.14 * count**0.426 / guess
        elif index == 2:
            guess = 1.86 * guess - 0.86 * found[0][0]
        elif index == 3:
            guess = 1.91 * guess - 0.91 * found[1][0]
        else:
            guess = 2.0 * guess - found[index - 2][0]
        for repeat in range(60):
            current = quarter
            previous = 0.0
            for order in range(count):
                older = previous
                previous = current
                current = (
                    guess * math.sqrt(2.0 / (order + 1)) * previous
                    - math.sqrt(order / (order + 1.0)) * older
                )
            last_slope = math.sqrt(2.0 * count) * previous
            guess = guess - current / last_slope
        found.append((guess, 2.0 / (last_slope * last_slope)))
    positive = found[::-1]
    points = [-pair[0] for pair in found] + [pair[0] for pair in positive]
    weights = [pair[1] for pair in found] + [pair[1] for pair in positive]
    return (np.array(points), np.array(weights))


def node_tables(axis_points):
    points, weights = hermite_rule(axis_points)
    node_index = np.arange(axis_points**3)
    idx_x = node_index % axis_points
    idx_z = node_index // axis_points % axis_points
    idx_y = node_index // (axis_points * axis_points)
    along_x = points[idx_x]
    along_y = points[idx_y]
    along_z = points[idx_z]
    node_weight = weights[idx_x] * weights[idx_y] * weights[idx_z] / math.pi**1.5
    energy = along_x**2 + along_y**2 + along_z**2 - 1.5
    moment_basis = np.stack([along_x * 0.0 + 1.0, along_x, along_y, along_z, energy])
    norm_scale = np.array([1.0, 0.5, 0.5, 0.5, 1.5])
    return (
        along_x,
        node_weight,
        moment_basis * node_weight[None, :],
        moment_basis / norm_scale[:, None],
    )


def apply_block(matrices, vector):
    shaped = matrices.reshape((5, 5) + vector.shape[1:])
    return jnp.sum(shaped * vector[None], axis=1)


def affine_combine(earlier_map, later_map):
    return (later_map[0] * earlier_map[0], later_map[0] * earlier_map[1] + later_map[1])


def newton_sums(loaded, signed, shift_mass, shift_flow):
    growth = jnp.exp(shift_mass + shift_flow * signed)
    scaled = loaded * growth
    excess = loaded * (growth - 1.0)
    return jnp.stack(
        [
            jnp.sum(scaled),
            jnp.sum(scaled * signed),
            jnp.sum(scaled * signed * signed),
            jnp.sum(excess),
            jnp.sum(excess * signed),
        ]
    )


def newton_update(shift_mass, shift_flow, sums, goal_mass, goal_flow):
    resid_mass = sums[3] - goal_mass
    resid_flow = sums[4] - goal_flow
    determinant = sums[0] * sums[2] - sums[1] * sums[1]
    new_mass = shift_mass - (sums[2] * resid_mass - sums[1] * resid_flow) / determinant
    new_flow = shift_flow - (sums[0] * resid_flow - sums[1] * resid_mass) / determinant
    return (new_mass, new_flow)


def received(block, distance):
    count = lax.axis_size("sec")
    if abs(distance) >= count:
        return jnp.zeros_like(block)
    return passed_along(block, "sec", distance)


def fetched(state, distance, sign):
    rate, drive = state
    got = received(jnp.concatenate([rate, drive], axis=0), sign * distance)
    return got[:1], got[1:]


def scan_first(rate, drive, sign):
    near_a, near_b = fetched((rate, drive), 1, sign)
    if lax.axis_size("sec") <= 2:
        return (near_a, near_b), 1
    far_a, far_b = fetched((rate, drive), 2, sign)
    return (near_a * far_a, near_a * far_b + near_b), 2


def scan_next(state, span, sign):
    got_a, got_b = fetched(state, span, sign)
    return (state[0] * got_a, state[0] * got_b + state[1]), span * 2


def exclusive_inflow(rate, drive, sign):
    state, span = scan_first(rate, drive, sign)
    while span < lax.axis_size("sec") - 1:
        state, span = scan_next(state, span, sign)
    return state[1]


def with_halo(array, width):
    parts = [received(array, d) for d in range(width, 0, -1)]
    parts.append(array)
    parts.extend(received(array, -d) for d in range(1, width + 1))
    return jnp.concatenate(parts, axis=1)


def group_sum(block, axis, low_bit, members):
    count = lax.axis_size(axis)
    if members == 2:
        pairs = [(i, i ^ (1 << low_bit)) for i in range(count)]
        return block + lax.ppermute(block, axis, pairs)
    mine = (lax.axis_index(axis) >> low_bit) % members
    shifted = [block]
    for step in range(1, members):
        pairs = []
        for i in range(count):
            place = (i >> low_bit) % members
            base = i - (place << low_bit)
            pairs.append((base + (((place + step) % members) << low_bit), i))
        shifted.append(lax.ppermute(block, axis, pairs))
    stacked = jnp.stack(shifted)
    total = None
    for member in range(members):
        value = lax.dynamic_index_in_dim(stacked, (member - mine) % members, 0, keepdims=False)
        total = value if total is None else total + value
    return total


def sum_plan(axis, count):
    bits = count.bit_length() - 1
    plan = []
    bit = 0
    if axis == "vel" and bits % 2 == 1:
        plan.append((0, 2))
        bit = 1
    elif axis == "vel" and bits >= 2:
        plan.append((0, 2))
        bit = 1
    while bit + 1 < bits:
        plan.append((bit, 4))
        bit += 2
    if bit < bits:
        plan.append((bit, 2))
    return plan


def tree_sum(block, axes):
    for axis in axes:
        count = lax.axis_size(axis)
        if count & (count - 1):
            block = lax.psum(block, axis)
            continue
        for low_bit, members in sum_plan(axis, count):
            block = group_sum(block, axis, low_bit, members)
    return block


def local_sweep(carry_rate, drive):
    half_nodes = NXI // 2
    shape = (1, half_nodes) + drive.shape[2:]
    prod_neg, local_neg = lax.associative_scan(
        affine_combine,
        (jnp.broadcast_to(carry_rate[:, :half_nodes], shape), drive[:, :half_nodes]),
        reverse=True,
        axis=2,
    )
    prod_pos, local_pos = lax.associative_scan(
        affine_combine,
        (jnp.broadcast_to(carry_rate[:, half_nodes:], shape), drive[:, half_nodes:]),
        axis=2,
    )
    return prod_neg, local_neg, prod_pos, local_pos


def joined_field(sweep, inflow_neg, inflow_pos):
    prod_neg, local_neg, prod_pos, local_pos = sweep
    field_neg = local_neg + prod_neg * inflow_neg[:, :, None, :]
    field_pos = local_pos + prod_pos * inflow_pos[:, :, None, :]
    return jnp.concatenate([field_neg, field_pos], axis=1)


def swept_field(carry_rate, drive):
    sweep = local_sweep(carry_rate, drive)
    inflow_pos = exclusive_inflow(sweep[2][:, :, -1], sweep[3][:, :, -1], 1)
    inflow_neg = exclusive_inflow(sweep[0][:, :, 0], sweep[1][:, :, 0], -1)
    return joined_field(sweep, inflow_neg, inflow_pos)


def caught_up_side(own, own_span, rate, drive, count, sign):
    reach = min(2 * own_span, count - 1)
    own_rows = own[1].shape[0]
    moment_rows = drive.shape[0]
    fetched_maps = {}
    for distance in range(1, reach + 1):
        if distance == own_span and own_span < count - 1:
            packed = jnp.concatenate([own[0], own[1], rate, drive], axis=0)
            got = received(packed, sign * distance)
            got_own = (got[:1], got[1 : 1 + own_rows])
            fetched_maps[distance] = (got[1 + own_rows : 2 + own_rows], got[2 + own_rows :])
        else:
            got = received(jnp.concatenate([rate, drive], axis=0), sign * distance)
            fetched_maps[distance] = (got[:1], got[1:])
    if own_span < count - 1:
        own = (own[0] * got_own[0], own[0] * got_own[1] + own[1])
    acc_a, acc_b = fetched_maps[reach]
    for distance in range(reach - 1, 0, -1):
        near_a, near_b = fetched_maps[distance]
        acc_a, acc_b = near_a * acc_a, near_a * acc_b + near_b
    return own, (acc_a, acc_b)


def caught_up(own_pos, own_neg, own_span, moment_sweep, count):
    own_pos, moment_pos = caught_up_side(
        own_pos, own_span, moment_sweep[2][:, :, -1], moment_sweep[3][:, :, -1], count, 1
    )
    own_neg, moment_neg = caught_up_side(
        own_neg, own_span, moment_sweep[0][:, :, 0], moment_sweep[1][:, :, 0], count, -1
    )
    return lax.optimization_barrier((own_pos, own_neg, moment_pos, moment_neg))


def joint_next(own, moment, span, sign):
    own_rows = own[1].shape[0]
    packed = jnp.concatenate([own[0], own[1], moment[1]], axis=0)
    got = received(packed, sign * span)
    got_a, got_own, got_moment = got[:1], got[1 : 1 + own_rows], got[1 + own_rows :]
    return (
        (own[0] * got_a, own[0] * got_own + own[1]),
        (own[0] * got_a, own[0] * got_moment + moment[1]),
    )


def sweep_kernel(dist_ref, target_ref, thick_ref, speed_ref, sign_ref, out_ref, rate_ref, drive_ref):
    positions = dist_ref.shape[0]
    start = jnp.zeros(dist_ref.shape[1:], jnp.float32)
    reach = speed_ref[...] * (positions * 1.0)

    def forward(p, carried):
        thick = thick_ref[p]
        denominator = reach + thick + pseudo_rate
        rate = reach / denominator
        drive = (thick * target_ref[p] + pseudo_rate * dist_ref[p]) / denominator
        rate_ref[p] = rate
        drive_ref[p] = drive
        value = rate * carried + drive
        out_ref[p] = value
        return value

    lax.fori_loop(0, positions, forward, start)
    heading = sign_ref[...] > 0

    def backward(i, carried):
        p = positions - 1 - i
        value = rate_ref[p] * carried + drive_ref[p]
        out_ref[p] = jnp.where(heading, out_ref[p], value)
        return value

    lax.fori_loop(0, positions, backward, start)


def line_sweep(dist_t, target, thickness, node_signed):
    shape = dist_t.shape
    return pl.pallas_call(
        sweep_kernel,
        out_shape=jax.ShapeDtypeStruct(shape, jnp.float32),
        scratch_shapes=[pltpu.VMEM(shape, jnp.float32), pltpu.VMEM(shape, jnp.float32)],
    )(dist_t, target, thickness, jnp.abs(node_signed).reshape(1, -1), node_signed.reshape(1, -1))


def line_block(matrices, vector):
    shaped = matrices.reshape(matrices.shape[:-1] + (5, 5))
    return jnp.sum(shaped * vector[..., None, :], axis=-1)


def body(distribution, collision, lower_blocks, upper_blocks, diag_inverse):
    node_count = distribution.shape[0]
    cell_count = distribution.shape[1]
    length = cell_count // TUBES
    node_rows = node_count // NXI
    count = lax.axis_size("sec")
    total_length = length * count
    share = TUBES // count
    along_x, node_weight, weighted_np, rebuild_np = node_tables(NXI)
    offset = lax.axis_index("vel") * node_count
    weighted = lax.dynamic_slice_in_dim(
        jnp.asarray(weighted_np, jnp.float32), offset, node_count, 1
    )
    rebuild = lax.dynamic_slice_in_dim(jnp.asarray(rebuild_np, jnp.float32), offset, node_count, 1)
    node_mass = lax.dynamic_slice_in_dim(jnp.asarray(node_weight, jnp.float32), offset, node_count, 0)
    line_signed = jnp.asarray(along_x[:NXI], jnp.float32)
    node_signed = jnp.asarray(np.tile(along_x[:NXI], node_rows), jnp.float32)
    packed = jnp.concatenate(
        [distribution, collision.reshape(1, cell_count), lower_blocks, upper_blocks, diag_inverse],
        axis=0,
    )
    rows = packed.shape[0]
    packed = packed.reshape(rows, length, TUBES).transpose(1, 2, 0)
    lines = lax.all_to_all(packed, "sec", 1, 0, tiled=True)
    dist_t = lines[:, :, :node_count]
    thickness = lines[:, :, node_count : node_count + 1]
    lower_t = lines[:, :, node_count + 1 : node_count + 26]
    upper_t = lines[:, :, node_count + 26 : node_count + 51]
    inverse_t = lines[:, :, node_count + 51 : node_count + 76]
    cells = total_length * share
    old_moments = tree_sum(
        jnp.dot(dist_t.reshape(cells, node_count), weighted.T, precision=HIGH), ("vel",)
    )
    target = jnp.dot(old_moments, rebuild, precision=HIGH).reshape(total_length, share, node_count)
    half_field = line_sweep(dist_t, target, thickness, node_signed)
    half_moments = tree_sum(
        jnp.dot(half_field.reshape(cells, node_count), weighted.T, precision=HIGH), ("vel",)
    )
    residual = (half_moments - old_moments).reshape(total_length, share, 5)
    correction = line_block(inverse_t, residual)
    edge_zero = jnp.zeros((1, share, 5), jnp.float32)
    for sweep_index in range(JACOBI):
        from_left = jnp.concatenate([edge_zero, correction[:-1]], axis=0)
        from_right = jnp.concatenate([correction[1:], edge_zero], axis=0)
        correction = line_block(
            inverse_t,
            residual - line_block(lower_t, from_left) - line_block(upper_t, from_right),
        )
    correction = correction.reshape(cells, 5)
    macro = half_moments + correction
    synthetic = half_field + jnp.dot(correction, rebuild, precision=HIGH).reshape(
        total_length, share, node_count
    )
    local_totals = jnp.sum(old_moments - macro, axis=0)[0:2]
    magnitude = jnp.sum(jnp.abs(synthetic), axis=(0, 1))
    line_loaded = jnp.sum((node_mass * magnitude).reshape(node_rows, NXI), axis=0)
    first_copy = (lax.axis_index("vel") == 0).astype(jnp.float32)
    back = jnp.concatenate([synthetic, macro.reshape(total_length, share, 5)], axis=2)
    back = lax.all_to_all(back, "sec", 0, 1, tiled=True)
    back = back.transpose(2, 0, 1).reshape(node_count + 5, cell_count)
    gathered = tree_sum(
        jnp.concatenate([line_loaded, local_totals * first_copy]), ("vel", "sec")
    )
    loaded = gathered[:NXI]
    goal_mass = jnp.broadcast_to(gathered[NXI], (NXI,))
    goal_flow = jnp.broadcast_to(gathered[NXI + 1], (NXI,))
    spread = jnp.ones((NXI, NXI), jnp.float32)
    shift_mass = jnp.zeros((NXI,), jnp.float32)
    shift_flow = jnp.zeros((NXI,), jnp.float32)
    for newton_turn in range(NEWTON):
        growth = jnp.exp(shift_mass + shift_flow * line_signed)
        scaled = loaded * growth
        excess = loaded * (growth - 1.0)
        terms = jnp.stack(
            [scaled, scaled * line_signed, scaled * line_signed * line_signed, excess, excess * line_signed]
        )
        sums = jnp.dot(terms, spread, precision=HIGH)
        shift_mass, shift_flow = newton_update(shift_mass, shift_flow, sums, goal_mass, goal_flow)
    growth = jnp.exp(shift_mass + shift_flow * line_signed)
    synthetic_rows = back[:node_count].reshape(node_rows, NXI, cell_count)
    new_distribution = synthetic_rows + jnp.abs(synthetic_rows) * (growth[None, :, None] - 1.0)
    return (new_distribution.reshape(node_count, cell_count), back[node_count:])


def solution(mesh):
    in_specs = (P("vel", "sec"), P("sec"), P(None, "sec"), P(None, "sec"), P(None, "sec"))
    out_specs = (P("vel", "sec"), P(None, "sec"))
    return jax.shard_map(body, mesh=mesh, in_specs=in_specs, out_specs=out_specs, check_vma=False)
```

```python
import math

import jax
import jax.numpy as jnp
import numpy as np
from jax import lax
from jax.experimental import pallas as pl
from jax.sharding import PartitionSpec as P

NXI = 24
TUBES = 128
JACOBI = 4
NEWTON = 2


HIGH = lax.Precision.HIGHEST
pseudo_rate = 1.0


def passed_along(block, axis, distance):
    devices = range(lax.axis_size(axis))
    route = [(i - distance, i) for i in devices if i - distance in devices]
    return lax.ppermute(block, axis, route)


def extended(array, sides, width):
    for axis, dim in sides:
        count, length = (lax.axis_size(axis), array.shape[dim])
        up = [(i, (i + 1) % count) for i in range(count - 1)]
        down = [(j, i) for i, j in up]
        last = lax.slice_in_dim(array, length - width, length, axis=dim)
        first = lax.slice_in_dim(array, 0, width, axis=dim)
        before = lax.ppermute(last, axis, up)
        after = lax.ppermute(first, axis, down)
        array = jnp.concatenate([before, array, after], axis=dim)
    return array


def hermite_rule(count):
    quarter = math.pi ** (-0.25)
    found = []
    last_slope = 1.0
    for index in range(count // 2):
        if index == 0:
            guess = math.sqrt(2.0 * count + 1.0) - 1.85575 * (2.0 * count + 1.0) ** (-0.16667)
        elif index == 1:
            guess = guess - 1.14 * count**0.426 / guess
        elif index == 2:
            guess = 1.86 * guess - 0.86 * found[0][0]
        elif index == 3:
            guess = 1.91 * guess - 0.91 * found[1][0]
        else:
            guess = 2.0 * guess - found[index - 2][0]
        for repeat in range(60):
            current = quarter
            previous = 0.0
            for order in range(count):
                older = previous
                previous = current
                current = (
                    guess * math.sqrt(2.0 / (order + 1)) * previous
                    - math.sqrt(order / (order + 1.0)) * older
                )
            last_slope = math.sqrt(2.0 * count) * previous
            guess = guess - current / last_slope
        found.append((guess, 2.0 / (last_slope * last_slope)))
    positive = found[::-1]
    points = [-pair[0] for pair in found] + [pair[0] for pair in positive]
    weights = [pair[1] for pair in found] + [pair[1] for pair in positive]
    return (np.array(points), np.array(weights))


def node_tables(axis_points):
    points, weights = hermite_rule(axis_points)
    node_index = np.arange(axis_points**3)
    idx_x = node_index % axis_points
    idx_z = node_index // axis_points % axis_points
    idx_y = node_index // (axis_points * axis_points)
    along_x = points[idx_x]
    along_y = points[idx_y]
    along_z = points[idx_z]
    node_weight = weights[idx_x] * weights[idx_y] * weights[idx_z] / math.pi**1.5
    energy = along_x**2 + along_y**2 + along_z**2 - 1.5
    moment_basis = np.stack([along_x * 0.0 + 1.0, along_x, along_y, along_z, energy])
    norm_scale = np.array([1.0, 0.5, 0.5, 0.5, 1.5])
    return (
        along_x,
        node_weight,
        moment_basis * node_weight[None, :],
        moment_basis / norm_scale[:, None],
    )


def apply_block(matrices, vector):
    shaped = matrices.reshape((5, 5) + vector.shape[1:])
    return jnp.sum(shaped * vector[None], axis=1)


def affine_combine(earlier_map, later_map):
    return (later_map[0] * earlier_map[0], later_map[0] * earlier_map[1] + later_map[1])


def newton_sums(loaded, signed, shift_mass, shift_flow):
    growth = jnp.exp(shift_mass + shift_flow * signed)
    scaled = loaded * growth
    excess = loaded * (growth - 1.0)
    return jnp.stack(
        [
            jnp.sum(scaled),
            jnp.sum(scaled * signed),
            jnp.sum(scaled * signed * signed),
            jnp.sum(excess),
            jnp.sum(excess * signed),
        ]
    )


def newton_update(shift_mass, shift_flow, sums, goal_mass, goal_flow):
    resid_mass = sums[3] - goal_mass
    resid_flow = sums[4] - goal_flow
    determinant = sums[0] * sums[2] - sums[1] * sums[1]
    new_mass = shift_mass - (sums[2] * resid_mass - sums[1] * resid_flow) / determinant
    new_flow = shift_flow - (sums[0] * resid_flow - sums[1] * resid_mass) / determinant
    return (new_mass, new_flow)


def received(block, distance):
    count = lax.axis_size("sec")
    if abs(distance) >= count:
        return jnp.zeros_like(block)
    return passed_along(block, "sec", distance)


def fetched(state, distance, sign):
    rate, drive = state
    got = received(jnp.concatenate([rate, drive], axis=0), sign * distance)
    return got[:1], got[1:]


def scan_first(rate, drive, sign):
    near_a, near_b = fetched((rate, drive), 1, sign)
    if lax.axis_size("sec") <= 2:
        return (near_a, near_b), 1
    far_a, far_b = fetched((rate, drive), 2, sign)
    return (near_a * far_a, near_a * far_b + near_b), 2


def scan_next(state, span, sign):
    got_a, got_b = fetched(state, span, sign)
    return (state[0] * got_a, state[0] * got_b + state[1]), span * 2


def exclusive_inflow(rate, drive, sign):
    state, span = scan_first(rate, drive, sign)
    while span < lax.axis_size("sec") - 1:
        state, span = scan_next(state, span, sign)
    return state[1]


def with_halo(array, width):
    parts = [received(array, d) for d in range(width, 0, -1)]
    parts.append(array)
    parts.extend(received(array, -d) for d in range(1, width + 1))
    return jnp.concatenate(parts, axis=1)


def group_sum(block, axis, low_bit, members):
    count = lax.axis_size(axis)
    if members == 2:
        pairs = [(i, i ^ (1 << low_bit)) for i in range(count)]
        return block + lax.ppermute(block, axis, pairs)
    mine = (lax.axis_index(axis) >> low_bit) % members
    shifted = [block]
    for step in range(1, members):
        pairs = []
        for i in range(count):
            place = (i >> low_bit) % members
            base = i - (place << low_bit)
            pairs.append((base + (((place + step) % members) << low_bit), i))
        shifted.append(lax.ppermute(block, axis, pairs))
    stacked = jnp.stack(shifted)
    total = None
    for member in range(members):
        value = lax.dynamic_index_in_dim(stacked, (member - mine) % members, 0, keepdims=False)
        total = value if total is None else total + value
    return total


def sum_plan(axis, count):
    bits = count.bit_length() - 1
    plan = []
    bit = 0
    if axis == "vel" and bits % 2 == 1:
        plan.append((0, 2))
        bit = 1
    elif axis == "vel" and bits >= 2:
        plan.append((0, 2))
        bit = 1
    while bit + 1 < bits:
        plan.append((bit, 4))
        bit += 2
    if bit < bits:
        plan.append((bit, 2))
    return plan


def tree_sum(block, axes):
    for axis in axes:
        count = lax.axis_size(axis)
        if count & (count - 1):
            block = lax.psum(block, axis)
            continue
        for low_bit, members in sum_plan(axis, count):
            block = group_sum(block, axis, low_bit, members)
    return block


def local_sweep(carry_rate, drive):
    half_nodes = NXI // 2
    shape = (1, half_nodes) + drive.shape[2:]
    prod_neg, local_neg = lax.associative_scan(
        affine_combine,
        (jnp.broadcast_to(carry_rate[:, :half_nodes], shape), drive[:, :half_nodes]),
        reverse=True,
        axis=2,
    )
    prod_pos, local_pos = lax.associative_scan(
        affine_combine,
        (jnp.broadcast_to(carry_rate[:, half_nodes:], shape), drive[:, half_nodes:]),
        axis=2,
    )
    return prod_neg, local_neg, prod_pos, local_pos


def joined_field(sweep, inflow_neg, inflow_pos):
    prod_neg, local_neg, prod_pos, local_pos = sweep
    field_neg = local_neg + prod_neg * inflow_neg[:, :, None, :]
    field_pos = local_pos + prod_pos * inflow_pos[:, :, None, :]
    return jnp.concatenate([field_neg, field_pos], axis=1)


def swept_field(carry_rate, drive):
    sweep = local_sweep(carry_rate, drive)
    inflow_pos = exclusive_inflow(sweep[2][:, :, -1], sweep[3][:, :, -1], 1)
    inflow_neg = exclusive_inflow(sweep[0][:, :, 0], sweep[1][:, :, 0], -1)
    return joined_field(sweep, inflow_neg, inflow_pos)


def caught_up_side(own, own_span, rate, drive, count, sign):
    reach = min(2 * own_span, count - 1)
    own_rows = own[1].shape[0]
    moment_rows = drive.shape[0]
    fetched_maps = {}
    for distance in range(1, reach + 1):
        if distance == own_span and own_span < count - 1:
            packed = jnp.concatenate([own[0], own[1], rate, drive], axis=0)
            got = received(packed, sign * distance)
            got_own = (got[:1], got[1 : 1 + own_rows])
            fetched_maps[distance] = (got[1 + own_rows : 2 + own_rows], got[2 + own_rows :])
        else:
            got = received(jnp.concatenate([rate, drive], axis=0), sign * distance)
            fetched_maps[distance] = (got[:1], got[1:])
    if own_span < count - 1:
        own = (own[0] * got_own[0], own[0] * got_own[1] + own[1])
    acc_a, acc_b = fetched_maps[reach]
    for distance in range(reach - 1, 0, -1):
        near_a, near_b = fetched_maps[distance]
        acc_a, acc_b = near_a * acc_a, near_a * acc_b + near_b
    return own, (acc_a, acc_b)


def caught_up(own_pos, own_neg, own_span, moment_sweep, count):
    own_pos, moment_pos = caught_up_side(
        own_pos, own_span, moment_sweep[2][:, :, -1], moment_sweep[3][:, :, -1], count, 1
    )
    own_neg, moment_neg = caught_up_side(
        own_neg, own_span, moment_sweep[0][:, :, 0], moment_sweep[1][:, :, 0], count, -1
    )
    return lax.optimization_barrier((own_pos, own_neg, moment_pos, moment_neg))


def joint_next(own, moment, span, sign):
    own_rows = own[1].shape[0]
    packed = jnp.concatenate([own[0], own[1], moment[1]], axis=0)
    got = received(packed, sign * span)
    got_a, got_own, got_moment = got[:1], got[1 : 1 + own_rows], got[1 + own_rows :]
    return (
        (own[0] * got_a, own[0] * got_own + own[1]),
        (own[0] * got_a, own[0] * got_moment + moment[1]),
    )


def sweep_kernel(rate_ref, drive_ref, sign_ref, out_ref):
    positions = rate_ref.shape[0]
    start = jnp.zeros(rate_ref.shape[1:], jnp.float32)

    def forward(p, carried):
        value = rate_ref[p] * carried + drive_ref[p]
        out_ref[p] = value
        return value

    lax.fori_loop(0, positions, forward, start)
    heading = sign_ref[...] > 0

    def backward(i, carried):
        p = positions - 1 - i
        value = rate_ref[p] * carried + drive_ref[p]
        out_ref[p] = jnp.where(heading, out_ref[p], value)
        return value

    lax.fori_loop(0, positions, backward, start)


def line_sweep(carry_rate, drive_term, node_signed):
    return pl.pallas_call(
        sweep_kernel,
        out_shape=jax.ShapeDtypeStruct(drive_term.shape, jnp.float32),
    )(carry_rate, drive_term, node_signed.reshape(1, -1))


def line_block(matrices, vector):
    shaped = matrices.reshape(matrices.shape[:-1] + (5, 5))
    return jnp.sum(shaped * vector[..., None, :], axis=-1)


def body(distribution, collision, lower_blocks, upper_blocks, diag_inverse):
    node_count = distribution.shape[0]
    cell_count = distribution.shape[1]
    length = cell_count // TUBES
    node_rows = node_count // NXI
    count = lax.axis_size("sec")
    total_length = length * count
    share = TUBES // count
    along_x, node_weight, weighted_np, rebuild_np = node_tables(NXI)
    offset = lax.axis_index("vel") * node_count
    weighted = lax.dynamic_slice_in_dim(
        jnp.asarray(weighted_np, jnp.float32), offset, node_count, 1
    )
    rebuild = lax.dynamic_slice_in_dim(jnp.asarray(rebuild_np, jnp.float32), offset, node_count, 1)
    node_mass = lax.dynamic_slice_in_dim(jnp.asarray(node_weight, jnp.float32), offset, node_count, 0)
    line_signed = jnp.asarray(along_x[:NXI], jnp.float32)
    node_signed = jnp.asarray(np.tile(along_x[:NXI], node_rows), jnp.float32)
    packed = jnp.concatenate(
        [distribution, collision.reshape(1, cell_count), lower_blocks, upper_blocks, diag_inverse],
        axis=0,
    )
    rows = packed.shape[0]
    packed = packed.reshape(rows, length, TUBES).transpose(1, 2, 0)
    lines = lax.all_to_all(packed, "sec", 1, 0, tiled=True)
    dist_t = lines[:, :, :node_count]
    thickness = lines[:, :, node_count : node_count + 1]
    lower_t = lines[:, :, node_count + 1 : node_count + 26]
    upper_t = lines[:, :, node_count + 26 : node_count + 51]
    inverse_t = lines[:, :, node_count + 51 : node_count + 76]
    cells = total_length * share
    old_moments = tree_sum(
        jnp.dot(dist_t.reshape(cells, node_count), weighted.T, precision=HIGH), ("vel",)
    )
    node_speed = jnp.abs(node_signed)
    denominator = node_speed * total_length + thickness + pseudo_rate
    carry_rate = node_speed * total_length / denominator
    own_drive = pseudo_rate * dist_t / denominator
    carry_rate = jnp.broadcast_to(carry_rate, own_drive.shape)
    own_field = line_sweep(carry_rate, own_drive, node_signed)
    moment_signed = jnp.asarray(np.tile(along_x[:NXI], 5), jnp.float32)
    moment_speed = jnp.abs(moment_signed)
    moment_den = moment_speed * total_length + thickness + pseudo_rate
    moment_rate = moment_speed * total_length / moment_den
    moment_drive = thickness * jnp.repeat(
        old_moments.reshape(total_length, share, 5), NXI, axis=2
    ) / moment_den
    moment_field = line_sweep(moment_rate, moment_drive, moment_signed)
    chosen = jnp.asarray(
        (np.arange(node_count)[None, :] % NXI) == np.arange(NXI)[:, None], jnp.float32
    )
    spread_basis = (rebuild[:, None, :] * chosen[None]).reshape(5 * NXI, node_count)
    half_field = own_field + jnp.dot(
        moment_field.reshape(cells, 5 * NXI), spread_basis, precision=HIGH
    ).reshape(total_length, share, node_count)
    half_moments = tree_sum(
        jnp.dot(half_field.reshape(cells, node_count), weighted.T, precision=HIGH), ("vel",)
    )
    residual = (half_moments - old_moments).reshape(total_length, share, 5)
    correction = line_block(inverse_t, residual)
    edge_zero = jnp.zeros((1, share, 5), jnp.float32)
    for sweep_index in range(JACOBI):
        from_left = jnp.concatenate([edge_zero, correction[:-1]], axis=0)
        from_right = jnp.concatenate([correction[1:], edge_zero], axis=0)
        correction = line_block(
            inverse_t,
            residual - line_block(lower_t, from_left) - line_block(upper_t, from_right),
        )
    correction = correction.reshape(cells, 5)
    macro = half_moments + correction
    synthetic = half_field + jnp.dot(correction, rebuild, precision=HIGH).reshape(
        total_length, share, node_count
    )
    local_totals = jnp.sum(old_moments - macro, axis=0)[0:2]
    magnitude = jnp.sum(jnp.abs(synthetic), axis=(0, 1))
    line_loaded = jnp.sum((node_mass * magnitude).reshape(node_rows, NXI), axis=0)
    first_copy = (lax.axis_index("vel") == 0).astype(jnp.float32)
    back = jnp.concatenate([synthetic, macro.reshape(total_length, share, 5)], axis=2)
    back = lax.all_to_all(back, "sec", 0, 1, tiled=True)
    back = back.transpose(2, 0, 1).reshape(node_count + 5, cell_count)
    gathered = tree_sum(
        jnp.concatenate([line_loaded, local_totals * first_copy]), ("vel", "sec")
    )
    loaded = gathered[:NXI]
    goal_mass = jnp.broadcast_to(gathered[NXI], (NXI,))
    goal_flow = jnp.broadcast_to(gathered[NXI + 1], (NXI,))
    spread = jnp.ones((NXI, NXI), jnp.float32)
    shift_mass = jnp.zeros((NXI,), jnp.float32)
    shift_flow = jnp.zeros((NXI,), jnp.float32)
    for newton_turn in range(NEWTON):
        growth = jnp.exp(shift_mass + shift_flow * line_signed)
        scaled = loaded * growth
        excess = loaded * (growth - 1.0)
        terms = jnp.stack(
            [scaled, scaled * line_signed, scaled * line_signed * line_signed, excess, excess * line_signed]
        )
        sums = jnp.dot(terms, spread, precision=HIGH)
        shift_mass, shift_flow = newton_update(shift_mass, shift_flow, sums, goal_mass, goal_flow)
    growth = jnp.exp(shift_mass + shift_flow * line_signed)
    synthetic_rows = back[:node_count].reshape(node_rows, NXI, cell_count)
    new_distribution = synthetic_rows + jnp.abs(synthetic_rows) * (growth[None, :, None] - 1.0)
    return (new_distribution.reshape(node_count, cell_count), back[node_count:])


def solution(mesh):
    in_specs = (P("vel", "sec"), P("sec"), P(None, "sec"), P(None, "sec"), P(None, "sec"))
    out_specs = (P("vel", "sec"), P(None, "sec"))
    return jax.shard_map(body, mesh=mesh, in_specs=in_specs, out_specs=out_specs, check_vma=False)
```

```python
import math

import jax
import jax.numpy as jnp
import numpy as np
from jax import lax
from jax.experimental import pallas as pl
from jax.sharding import PartitionSpec as P

NXI = 24
TUBES = 128
JACOBI = 4
NEWTON = 2


HIGH = lax.Precision.HIGHEST
pseudo_rate = 1.0


def passed_along(block, axis, distance):
    devices = range(lax.axis_size(axis))
    route = [(i - distance, i) for i in devices if i - distance in devices]
    return lax.ppermute(block, axis, route)


def extended(array, sides, width):
    for axis, dim in sides:
        count, length = (lax.axis_size(axis), array.shape[dim])
        up = [(i, (i + 1) % count) for i in range(count - 1)]
        down = [(j, i) for i, j in up]
        last = lax.slice_in_dim(array, length - width, length, axis=dim)
        first = lax.slice_in_dim(array, 0, width, axis=dim)
        before = lax.ppermute(last, axis, up)
        after = lax.ppermute(first, axis, down)
        array = jnp.concatenate([before, array, after], axis=dim)
    return array


def hermite_rule(count):
    quarter = math.pi ** (-0.25)
    found = []
    last_slope = 1.0
    for index in range(count // 2):
        if index == 0:
            guess = math.sqrt(2.0 * count + 1.0) - 1.85575 * (2.0 * count + 1.0) ** (-0.16667)
        elif index == 1:
            guess = guess - 1.14 * count**0.426 / guess
        elif index == 2:
            guess = 1.86 * guess - 0.86 * found[0][0]
        elif index == 3:
            guess = 1.91 * guess - 0.91 * found[1][0]
        else:
            guess = 2.0 * guess - found[index - 2][0]
        for repeat in range(60):
            current = quarter
            previous = 0.0
            for order in range(count):
                older = previous
                previous = current
                current = (
                    guess * math.sqrt(2.0 / (order + 1)) * previous
                    - math.sqrt(order / (order + 1.0)) * older
                )
            last_slope = math.sqrt(2.0 * count) * previous
            guess = guess - current / last_slope
        found.append((guess, 2.0 / (last_slope * last_slope)))
    positive = found[::-1]
    points = [-pair[0] for pair in found] + [pair[0] for pair in positive]
    weights = [pair[1] for pair in found] + [pair[1] for pair in positive]
    return (np.array(points), np.array(weights))


def node_tables(axis_points):
    points, weights = hermite_rule(axis_points)
    node_index = np.arange(axis_points**3)
    idx_x = node_index % axis_points
    idx_z = node_index // axis_points % axis_points
    idx_y = node_index // (axis_points * axis_points)
    along_x = points[idx_x]
    along_y = points[idx_y]
    along_z = points[idx_z]
    node_weight = weights[idx_x] * weights[idx_y] * weights[idx_z] / math.pi**1.5
    energy = along_x**2 + along_y**2 + along_z**2 - 1.5
    moment_basis = np.stack([along_x * 0.0 + 1.0, along_x, along_y, along_z, energy])
    norm_scale = np.array([1.0, 0.5, 0.5, 0.5, 1.5])
    return (
        along_x,
        node_weight,
        moment_basis * node_weight[None, :],
        moment_basis / norm_scale[:, None],
    )


def apply_block(matrices, vector):
    shaped = matrices.reshape((5, 5) + vector.shape[1:])
    return jnp.sum(shaped * vector[None], axis=1)


def affine_combine(earlier_map, later_map):
    return (later_map[0] * earlier_map[0], later_map[0] * earlier_map[1] + later_map[1])


def newton_sums(loaded, signed, shift_mass, shift_flow):
    growth = jnp.exp(shift_mass + shift_flow * signed)
    scaled = loaded * growth
    excess = loaded * (growth - 1.0)
    return jnp.stack(
        [
            jnp.sum(scaled),
            jnp.sum(scaled * signed),
            jnp.sum(scaled * signed * signed),
            jnp.sum(excess),
            jnp.sum(excess * signed),
        ]
    )


def newton_update(shift_mass, shift_flow, sums, goal_mass, goal_flow):
    resid_mass = sums[3] - goal_mass
    resid_flow = sums[4] - goal_flow
    determinant = sums[0] * sums[2] - sums[1] * sums[1]
    new_mass = shift_mass - (sums[2] * resid_mass - sums[1] * resid_flow) / determinant
    new_flow = shift_flow - (sums[0] * resid_flow - sums[1] * resid_mass) / determinant
    return (new_mass, new_flow)


def received(block, distance):
    count = lax.axis_size("sec")
    if abs(distance) >= count:
        return jnp.zeros_like(block)
    return passed_along(block, "sec", distance)


def fetched(state, distance, sign):
    rate, drive = state
    got = received(jnp.concatenate([rate, drive], axis=0), sign * distance)
    return got[:1], got[1:]


def scan_first(rate, drive, sign):
    near_a, near_b = fetched((rate, drive), 1, sign)
    if lax.axis_size("sec") <= 2:
        return (near_a, near_b), 1
    far_a, far_b = fetched((rate, drive), 2, sign)
    return (near_a * far_a, near_a * far_b + near_b), 2


def scan_next(state, span, sign):
    got_a, got_b = fetched(state, span, sign)
    return (state[0] * got_a, state[0] * got_b + state[1]), span * 2


def exclusive_inflow(rate, drive, sign):
    state, span = scan_first(rate, drive, sign)
    while span < lax.axis_size("sec") - 1:
        state, span = scan_next(state, span, sign)
    return state[1]


def with_halo(array, width):
    parts = [received(array, d) for d in range(width, 0, -1)]
    parts.append(array)
    parts.extend(received(array, -d) for d in range(1, width + 1))
    return jnp.concatenate(parts, axis=1)


def group_sum(block, axis, low_bit, members):
    count = lax.axis_size(axis)
    if members == 2:
        pairs = [(i, i ^ (1 << low_bit)) for i in range(count)]
        return block + lax.ppermute(block, axis, pairs)
    mine = (lax.axis_index(axis) >> low_bit) % members
    shifted = [block]
    for step in range(1, members):
        pairs = []
        for i in range(count):
            place = (i >> low_bit) % members
            base = i - (place << low_bit)
            pairs.append((base + (((place + step) % members) << low_bit), i))
        shifted.append(lax.ppermute(block, axis, pairs))
    stacked = jnp.stack(shifted)
    total = None
    for member in range(members):
        value = lax.dynamic_index_in_dim(stacked, (member - mine) % members, 0, keepdims=False)
        total = value if total is None else total + value
    return total


def sum_plan(axis, count):
    bits = count.bit_length() - 1
    plan = []
    bit = 0
    if axis == "vel" and bits >= 2:
        plan.append((0, 2))
        plan.append((1, 1 << (bits - 1)))
        return plan
    while bit + 1 < bits:
        plan.append((bit, 4))
        bit += 2
    if bit < bits:
        plan.append((bit, 2))
    return plan


def tree_sum(block, axes):
    for axis in axes:
        count = lax.axis_size(axis)
        if count & (count - 1):
            block = lax.psum(block, axis)
            continue
        for low_bit, members in sum_plan(axis, count):
            block = group_sum(block, axis, low_bit, members)
    return block


def local_sweep(carry_rate, drive):
    half_nodes = NXI // 2
    shape = (1, half_nodes) + drive.shape[2:]
    prod_neg, local_neg = lax.associative_scan(
        affine_combine,
        (jnp.broadcast_to(carry_rate[:, :half_nodes], shape), drive[:, :half_nodes]),
        reverse=True,
        axis=2,
    )
    prod_pos, local_pos = lax.associative_scan(
        affine_combine,
        (jnp.broadcast_to(carry_rate[:, half_nodes:], shape), drive[:, half_nodes:]),
        axis=2,
    )
    return prod_neg, local_neg, prod_pos, local_pos


def joined_field(sweep, inflow_neg, inflow_pos):
    prod_neg, local_neg, prod_pos, local_pos = sweep
    field_neg = local_neg + prod_neg * inflow_neg[:, :, None, :]
    field_pos = local_pos + prod_pos * inflow_pos[:, :, None, :]
    return jnp.concatenate([field_neg, field_pos], axis=1)


def swept_field(carry_rate, drive):
    sweep = local_sweep(carry_rate, drive)
    inflow_pos = exclusive_inflow(sweep[2][:, :, -1], sweep[3][:, :, -1], 1)
    inflow_neg = exclusive_inflow(sweep[0][:, :, 0], sweep[1][:, :, 0], -1)
    return joined_field(sweep, inflow_neg, inflow_pos)


def caught_up_side(own, own_span, rate, drive, count, sign):
    reach = min(2 * own_span, count - 1)
    own_rows = own[1].shape[0]
    moment_rows = drive.shape[0]
    fetched_maps = {}
    for distance in range(1, reach + 1):
        if distance == own_span and own_span < count - 1:
            packed = jnp.concatenate([own[0], own[1], rate, drive], axis=0)
            got = received(packed, sign * distance)
            got_own = (got[:1], got[1 : 1 + own_rows])
            fetched_maps[distance] = (got[1 + own_rows : 2 + own_rows], got[2 + own_rows :])
        else:
            got = received(jnp.concatenate([rate, drive], axis=0), sign * distance)
            fetched_maps[distance] = (got[:1], got[1:])
    if own_span < count - 1:
        own = (own[0] * got_own[0], own[0] * got_own[1] + own[1])
    acc_a, acc_b = fetched_maps[reach]
    for distance in range(reach - 1, 0, -1):
        near_a, near_b = fetched_maps[distance]
        acc_a, acc_b = near_a * acc_a, near_a * acc_b + near_b
    return own, (acc_a, acc_b)


def caught_up(own_pos, own_neg, own_span, moment_sweep, count):
    own_pos, moment_pos = caught_up_side(
        own_pos, own_span, moment_sweep[2][:, :, -1], moment_sweep[3][:, :, -1], count, 1
    )
    own_neg, moment_neg = caught_up_side(
        own_neg, own_span, moment_sweep[0][:, :, 0], moment_sweep[1][:, :, 0], count, -1
    )
    return lax.optimization_barrier((own_pos, own_neg, moment_pos, moment_neg))


def joint_next(own, moment, span, sign):
    own_rows = own[1].shape[0]
    packed = jnp.concatenate([own[0], own[1], moment[1]], axis=0)
    got = received(packed, sign * span)
    got_a, got_own, got_moment = got[:1], got[1 : 1 + own_rows], got[1 + own_rows :]
    return (
        (own[0] * got_a, own[0] * got_own + own[1]),
        (own[0] * got_a, own[0] * got_moment + moment[1]),
    )


def sweep_kernel(rate_ref, drive_ref, sign_ref, out_ref):
    positions = rate_ref.shape[0]
    start = jnp.zeros(rate_ref.shape[1:], jnp.float32)

    def forward(p, carried):
        value = rate_ref[p] * carried + drive_ref[p]
        out_ref[p] = value
        return value

    lax.fori_loop(0, positions, forward, start)
    heading = sign_ref[...] > 0

    def backward(i, carried):
        p = positions - 1 - i
        value = rate_ref[p] * carried + drive_ref[p]
        out_ref[p] = jnp.where(heading, out_ref[p], value)
        return value

    lax.fori_loop(0, positions, backward, start)


def line_sweep(carry_rate, drive_term, node_signed):
    return pl.pallas_call(
        sweep_kernel,
        out_shape=jax.ShapeDtypeStruct(drive_term.shape, jnp.float32),
    )(carry_rate, drive_term, node_signed.reshape(1, -1))


def line_block(matrices, vector):
    shaped = matrices.reshape(matrices.shape[:-1] + (5, 5))
    return jnp.sum(shaped * vector[..., None, :], axis=-1)


def body(distribution, collision, lower_blocks, upper_blocks, diag_inverse):
    node_count = distribution.shape[0]
    cell_count = distribution.shape[1]
    length = cell_count // TUBES
    node_rows = node_count // NXI
    count = lax.axis_size("sec")
    total_length = length * count
    share = TUBES // count
    along_x, node_weight, weighted_np, rebuild_np = node_tables(NXI)
    offset = lax.axis_index("vel") * node_count
    weighted = lax.dynamic_slice_in_dim(
        jnp.asarray(weighted_np, jnp.float32), offset, node_count, 1
    )
    rebuild = lax.dynamic_slice_in_dim(jnp.asarray(rebuild_np, jnp.float32), offset, node_count, 1)
    node_mass = lax.dynamic_slice_in_dim(jnp.asarray(node_weight, jnp.float32), offset, node_count, 0)
    line_signed = jnp.asarray(along_x[:NXI], jnp.float32)
    node_signed = jnp.asarray(np.tile(along_x[:NXI], node_rows), jnp.float32)
    packed = jnp.concatenate(
        [distribution, collision.reshape(1, cell_count), lower_blocks, upper_blocks, diag_inverse],
        axis=0,
    )
    rows = packed.shape[0]
    packed = packed.reshape(rows, length, TUBES).transpose(1, 2, 0)
    lines = lax.all_to_all(packed, "sec", 1, 0, tiled=True)
    dist_t = lines[:, :, :node_count]
    thickness = lines[:, :, node_count : node_count + 1]
    lower_t = lines[:, :, node_count + 1 : node_count + 26]
    upper_t = lines[:, :, node_count + 26 : node_count + 51]
    inverse_t = lines[:, :, node_count + 51 : node_count + 76]
    cells = total_length * share
    old_moments = tree_sum(
        jnp.dot(dist_t.reshape(cells, node_count), weighted.T, precision=HIGH), ("vel",)
    )
    node_speed = jnp.abs(node_signed)
    denominator = node_speed * total_length + thickness + pseudo_rate
    carry_rate = node_speed * total_length / denominator
    own_drive = pseudo_rate * dist_t / denominator
    carry_rate = jnp.broadcast_to(carry_rate, own_drive.shape)
    own_field = line_sweep(carry_rate, own_drive, node_signed)
    moment_signed = jnp.asarray(np.tile(along_x[:NXI], 5), jnp.float32)
    moment_speed = jnp.abs(moment_signed)
    moment_den = moment_speed * total_length + thickness + pseudo_rate
    moment_rate = moment_speed * total_length / moment_den
    moment_drive = thickness * jnp.repeat(
        old_moments.reshape(total_length, share, 5), NXI, axis=2
    ) / moment_den
    moment_field = line_sweep(moment_rate, moment_drive, moment_signed)
    chosen = jnp.asarray(
        (np.arange(node_count)[None, :] % NXI) == np.arange(NXI)[:, None], jnp.float32
    )
    spread_basis = (rebuild[:, None, :] * chosen[None]).reshape(5 * NXI, node_count)
    half_field = own_field + jnp.dot(
        moment_field.reshape(cells, 5 * NXI), spread_basis, precision=HIGH
    ).reshape(total_length, share, node_count)
    half_moments = tree_sum(
        jnp.dot(half_field.reshape(cells, node_count), weighted.T, precision=HIGH), ("vel",)
    )
    residual = (half_moments - old_moments).reshape(total_length, share, 5)
    correction = line_block(inverse_t, residual)
    edge_zero = jnp.zeros((1, share, 5), jnp.float32)
    for sweep_index in range(JACOBI):
        from_left = jnp.concatenate([edge_zero, correction[:-1]], axis=0)
        from_right = jnp.concatenate([correction[1:], edge_zero], axis=0)
        correction = line_block(
            inverse_t,
            residual - line_block(lower_t, from_left) - line_block(upper_t, from_right),
        )
    correction = correction.reshape(cells, 5)
    macro = half_moments + correction
    synthetic = half_field + jnp.dot(correction, rebuild, precision=HIGH).reshape(
        total_length, share, node_count
    )
    local_totals = jnp.sum(old_moments - macro, axis=0)[0:2]
    magnitude = jnp.sum(jnp.abs(synthetic), axis=(0, 1))
    line_loaded = jnp.sum((node_mass * magnitude).reshape(node_rows, NXI), axis=0)
    first_copy = (lax.axis_index("vel") == 0).astype(jnp.float32)
    back = jnp.concatenate([synthetic, macro.reshape(total_length, share, 5)], axis=2)
    back = lax.all_to_all(back, "sec", 0, 1, tiled=True)
    back = back.transpose(2, 0, 1).reshape(node_count + 5, cell_count)
    gathered = tree_sum(
        jnp.concatenate([line_loaded, local_totals * first_copy]), ("vel", "sec")
    )
    loaded = gathered[:NXI]
    goal_mass = jnp.broadcast_to(gathered[NXI], (NXI,))
    goal_flow = jnp.broadcast_to(gathered[NXI + 1], (NXI,))
    spread = jnp.ones((NXI, NXI), jnp.float32)
    shift_mass = jnp.zeros((NXI,), jnp.float32)
    shift_flow = jnp.zeros((NXI,), jnp.float32)
    for newton_turn in range(NEWTON):
        growth = jnp.exp(shift_mass + shift_flow * line_signed)
        scaled = loaded * growth
        excess = loaded * (growth - 1.0)
        terms = jnp.stack(
            [scaled, scaled * line_signed, scaled * line_signed * line_signed, excess, excess * line_signed]
        )
        sums = jnp.dot(terms, spread, precision=HIGH)
        shift_mass, shift_flow = newton_update(shift_mass, shift_flow, sums, goal_mass, goal_flow)
    growth = jnp.exp(shift_mass + shift_flow * line_signed)
    synthetic_rows = back[:node_count].reshape(node_rows, NXI, cell_count)
    new_distribution = synthetic_rows + jnp.abs(synthetic_rows) * (growth[None, :, None] - 1.0)
    return (new_distribution.reshape(node_count, cell_count), back[node_count:])


def solution(mesh):
    in_specs = (P("vel", "sec"), P("sec"), P(None, "sec"), P(None, "sec"), P(None, "sec"))
    out_specs = (P("vel", "sec"), P(None, "sec"))
    return jax.shard_map(body, mesh=mesh, in_specs=in_specs, out_specs=out_specs, check_vma=False)
```

```python
import math

import jax
import jax.numpy as jnp
import numpy as np
from jax import lax
from jax.experimental import pallas as pl
from jax.sharding import PartitionSpec as P

NXI = 24
TUBES = 128
JACOBI = 4
NEWTON = 2


HIGH = lax.Precision.HIGHEST
pseudo_rate = 1.0


def passed_along(block, axis, distance):
    devices = range(lax.axis_size(axis))
    route = [(i - distance, i) for i in devices if i - distance in devices]
    return lax.ppermute(block, axis, route)


def extended(array, sides, width):
    for axis, dim in sides:
        count, length = (lax.axis_size(axis), array.shape[dim])
        up = [(i, (i + 1) % count) for i in range(count - 1)]
        down = [(j, i) for i, j in up]
        last = lax.slice_in_dim(array, length - width, length, axis=dim)
        first = lax.slice_in_dim(array, 0, width, axis=dim)
        before = lax.ppermute(last, axis, up)
        after = lax.ppermute(first, axis, down)
        array = jnp.concatenate([before, array, after], axis=dim)
    return array


def hermite_rule(count):
    quarter = math.pi ** (-0.25)
    found = []
    last_slope = 1.0
    for index in range(count // 2):
        if index == 0:
            guess = math.sqrt(2.0 * count + 1.0) - 1.85575 * (2.0 * count + 1.0) ** (-0.16667)
        elif index == 1:
            guess = guess - 1.14 * count**0.426 / guess
        elif index == 2:
            guess = 1.86 * guess - 0.86 * found[0][0]
        elif index == 3:
            guess = 1.91 * guess - 0.91 * found[1][0]
        else:
            guess = 2.0 * guess - found[index - 2][0]
        for repeat in range(60):
            current = quarter
            previous = 0.0
            for order in range(count):
                older = previous
                previous = current
                current = (
                    guess * math.sqrt(2.0 / (order + 1)) * previous
                    - math.sqrt(order / (order + 1.0)) * older
                )
            last_slope = math.sqrt(2.0 * count) * previous
            guess = guess - current / last_slope
        found.append((guess, 2.0 / (last_slope * last_slope)))
    positive = found[::-1]
    points = [-pair[0] for pair in found] + [pair[0] for pair in positive]
    weights = [pair[1] for pair in found] + [pair[1] for pair in positive]
    return (np.array(points), np.array(weights))


def node_tables(axis_points):
    points, weights = hermite_rule(axis_points)
    node_index = np.arange(axis_points**3)
    idx_x = node_index % axis_points
    idx_z = node_index // axis_points % axis_points
    idx_y = node_index // (axis_points * axis_points)
    along_x = points[idx_x]
    along_y = points[idx_y]
    along_z = points[idx_z]
    node_weight = weights[idx_x] * weights[idx_y] * weights[idx_z] / math.pi**1.5
    energy = along_x**2 + along_y**2 + along_z**2 - 1.5
    moment_basis = np.stack([along_x * 0.0 + 1.0, along_x, along_y, along_z, energy])
    norm_scale = np.array([1.0, 0.5, 0.5, 0.5, 1.5])
    return (
        along_x,
        node_weight,
        moment_basis * node_weight[None, :],
        moment_basis / norm_scale[:, None],
    )


def apply_block(matrices, vector):
    shaped = matrices.reshape((5, 5) + vector.shape[1:])
    return jnp.sum(shaped * vector[None], axis=1)


def affine_combine(earlier_map, later_map):
    return (later_map[0] * earlier_map[0], later_map[0] * earlier_map[1] + later_map[1])


def newton_sums(loaded, signed, shift_mass, shift_flow):
    growth = jnp.exp(shift_mass + shift_flow * signed)
    scaled = loaded * growth
    excess = loaded * (growth - 1.0)
    return jnp.stack(
        [
            jnp.sum(scaled),
            jnp.sum(scaled * signed),
            jnp.sum(scaled * signed * signed),
            jnp.sum(excess),
            jnp.sum(excess * signed),
        ]
    )


def newton_update(shift_mass, shift_flow, sums, goal_mass, goal_flow):
    resid_mass = sums[3] - goal_mass
    resid_flow = sums[4] - goal_flow
    determinant = sums[0] * sums[2] - sums[1] * sums[1]
    new_mass = shift_mass - (sums[2] * resid_mass - sums[1] * resid_flow) / determinant
    new_flow = shift_flow - (sums[0] * resid_flow - sums[1] * resid_mass) / determinant
    return (new_mass, new_flow)


def received(block, distance):
    count = lax.axis_size("sec")
    if abs(distance) >= count:
        return jnp.zeros_like(block)
    return passed_along(block, "sec", distance)


def fetched(state, distance, sign):
    rate, drive = state
    got = received(jnp.concatenate([rate, drive], axis=0), sign * distance)
    return got[:1], got[1:]


def scan_first(rate, drive, sign):
    near_a, near_b = fetched((rate, drive), 1, sign)
    if lax.axis_size("sec") <= 2:
        return (near_a, near_b), 1
    far_a, far_b = fetched((rate, drive), 2, sign)
    return (near_a * far_a, near_a * far_b + near_b), 2


def scan_next(state, span, sign):
    got_a, got_b = fetched(state, span, sign)
    return (state[0] * got_a, state[0] * got_b + state[1]), span * 2


def exclusive_inflow(rate, drive, sign):
    state, span = scan_first(rate, drive, sign)
    while span < lax.axis_size("sec") - 1:
        state, span = scan_next(state, span, sign)
    return state[1]


def with_halo(array, width):
    parts = [received(array, d) for d in range(width, 0, -1)]
    parts.append(array)
    parts.extend(received(array, -d) for d in range(1, width + 1))
    return jnp.concatenate(parts, axis=1)


def group_sum(block, axis, low_bit, members):
    count = lax.axis_size(axis)
    if members == 2:
        pairs = [(i, i ^ (1 << low_bit)) for i in range(count)]
        return block + lax.ppermute(block, axis, pairs)
    mine = (lax.axis_index(axis) >> low_bit) % members
    shifted = [block]
    for step in range(1, members):
        pairs = []
        for i in range(count):
            place = (i >> low_bit) % members
            base = i - (place << low_bit)
            pairs.append((base + (((place + step) % members) << low_bit), i))
        shifted.append(lax.ppermute(block, axis, pairs))
    stacked = jnp.stack(shifted)
    total = None
    for member in range(members):
        value = lax.dynamic_index_in_dim(stacked, (member - mine) % members, 0, keepdims=False)
        total = value if total is None else total + value
    return total


def sum_plan(axis, count):
    bits = count.bit_length() - 1
    plan = []
    bit = 0
    if axis == "vel" and bits % 2 == 1:
        plan.append((0, 2))
        bit = 1
    elif axis == "vel" and bits >= 2:
        plan.append((0, 2))
        bit = 1
    while bit + 1 < bits:
        plan.append((bit, 4))
        bit += 2
    if bit < bits:
        plan.append((bit, 2))
    return plan


def tree_sum(block, axes):
    for axis in axes:
        count = lax.axis_size(axis)
        if count & (count - 1):
            block = lax.psum(block, axis)
            continue
        for low_bit, members in sum_plan(axis, count):
            block = group_sum(block, axis, low_bit, members)
    return block


def local_sweep(carry_rate, drive):
    half_nodes = NXI // 2
    shape = (1, half_nodes) + drive.shape[2:]
    prod_neg, local_neg = lax.associative_scan(
        affine_combine,
        (jnp.broadcast_to(carry_rate[:, :half_nodes], shape), drive[:, :half_nodes]),
        reverse=True,
        axis=2,
    )
    prod_pos, local_pos = lax.associative_scan(
        affine_combine,
        (jnp.broadcast_to(carry_rate[:, half_nodes:], shape), drive[:, half_nodes:]),
        axis=2,
    )
    return prod_neg, local_neg, prod_pos, local_pos


def joined_field(sweep, inflow_neg, inflow_pos):
    prod_neg, local_neg, prod_pos, local_pos = sweep
    field_neg = local_neg + prod_neg * inflow_neg[:, :, None, :]
    field_pos = local_pos + prod_pos * inflow_pos[:, :, None, :]
    return jnp.concatenate([field_neg, field_pos], axis=1)


def swept_field(carry_rate, drive):
    sweep = local_sweep(carry_rate, drive)
    inflow_pos = exclusive_inflow(sweep[2][:, :, -1], sweep[3][:, :, -1], 1)
    inflow_neg = exclusive_inflow(sweep[0][:, :, 0], sweep[1][:, :, 0], -1)
    return joined_field(sweep, inflow_neg, inflow_pos)


def caught_up_side(own, own_span, rate, drive, count, sign):
    reach = min(2 * own_span, count - 1)
    own_rows = own[1].shape[0]
    moment_rows = drive.shape[0]
    fetched_maps = {}
    for distance in range(1, reach + 1):
        if distance == own_span and own_span < count - 1:
            packed = jnp.concatenate([own[0], own[1], rate, drive], axis=0)
            got = received(packed, sign * distance)
            got_own = (got[:1], got[1 : 1 + own_rows])
            fetched_maps[distance] = (got[1 + own_rows : 2 + own_rows], got[2 + own_rows :])
        else:
            got = received(jnp.concatenate([rate, drive], axis=0), sign * distance)
            fetched_maps[distance] = (got[:1], got[1:])
    if own_span < count - 1:
        own = (own[0] * got_own[0], own[0] * got_own[1] + own[1])
    acc_a, acc_b = fetched_maps[reach]
    for distance in range(reach - 1, 0, -1):
        near_a, near_b = fetched_maps[distance]
        acc_a, acc_b = near_a * acc_a, near_a * acc_b + near_b
    return own, (acc_a, acc_b)


def caught_up(own_pos, own_neg, own_span, moment_sweep, count):
    own_pos, moment_pos = caught_up_side(
        own_pos, own_span, moment_sweep[2][:, :, -1], moment_sweep[3][:, :, -1], count, 1
    )
    own_neg, moment_neg = caught_up_side(
        own_neg, own_span, moment_sweep[0][:, :, 0], moment_sweep[1][:, :, 0], count, -1
    )
    return lax.optimization_barrier((own_pos, own_neg, moment_pos, moment_neg))


def joint_next(own, moment, span, sign):
    own_rows = own[1].shape[0]
    packed = jnp.concatenate([own[0], own[1], moment[1]], axis=0)
    got = received(packed, sign * span)
    got_a, got_own, got_moment = got[:1], got[1 : 1 + own_rows], got[1 + own_rows :]
    return (
        (own[0] * got_a, own[0] * got_own + own[1]),
        (own[0] * got_a, own[0] * got_moment + moment[1]),
    )


def sweep_kernel(rate_ref, drive_ref, sign_ref, out_ref):
    positions = rate_ref.shape[0]
    start = jnp.zeros(rate_ref.shape[1:], jnp.float32)

    def forward(p, carried):
        value = rate_ref[p] * carried + drive_ref[p]
        out_ref[p] = value
        return value

    lax.fori_loop(0, positions, forward, start)
    heading = sign_ref[...] > 0

    def backward(i, carried):
        p = positions - 1 - i
        value = rate_ref[p] * carried + drive_ref[p]
        out_ref[p] = jnp.where(heading, out_ref[p], value)
        return value

    lax.fori_loop(0, positions, backward, start)


def line_sweep(carry_rate, drive_term, node_signed):
    return pl.pallas_call(
        sweep_kernel,
        out_shape=jax.ShapeDtypeStruct(drive_term.shape, jnp.float32),
    )(carry_rate, drive_term, node_signed.reshape(1, -1))


def line_block(matrices, vector):
    shaped = matrices.reshape(matrices.shape[:-1] + (5, 5))
    return jnp.sum(shaped * vector[..., None, :], axis=-1)


def body(distribution, collision, lower_blocks, upper_blocks, diag_inverse):
    node_count = distribution.shape[0]
    cell_count = distribution.shape[1]
    length = cell_count // TUBES
    node_rows = node_count // NXI
    count = lax.axis_size("sec")
    total_length = length * count
    share = TUBES // count
    along_x, node_weight, weighted_np, rebuild_np = node_tables(NXI)
    offset = lax.axis_index("vel") * node_count
    weighted = lax.dynamic_slice_in_dim(
        jnp.asarray(weighted_np, jnp.float32), offset, node_count, 1
    )
    rebuild = lax.dynamic_slice_in_dim(jnp.asarray(rebuild_np, jnp.float32), offset, node_count, 1)
    node_mass = lax.dynamic_slice_in_dim(jnp.asarray(node_weight, jnp.float32), offset, node_count, 0)
    line_signed = jnp.asarray(along_x[:NXI], jnp.float32)
    node_signed = jnp.asarray(np.tile(along_x[:NXI], node_rows), jnp.float32)
    pieces = [distribution, collision.reshape(1, cell_count), lower_blocks, upper_blocks, diag_inverse]
    packed = jnp.concatenate(
        [piece.reshape(-1, length, TUBES).transpose(1, 2, 0) for piece in pieces], axis=2
    )
    lines = lax.all_to_all(packed, "sec", 1, 0, tiled=True)
    dist_t = lines[:, :, :node_count]
    thickness = lines[:, :, node_count : node_count + 1]
    lower_t = lines[:, :, node_count + 1 : node_count + 26]
    upper_t = lines[:, :, node_count + 26 : node_count + 51]
    inverse_t = lines[:, :, node_count + 51 : node_count + 76]
    cells = total_length * share
    old_moments = tree_sum(
        jnp.dot(dist_t.reshape(cells, node_count), weighted.T, precision=HIGH), ("vel",)
    )
    node_speed = jnp.abs(node_signed)
    denominator = node_speed * total_length + thickness + pseudo_rate
    carry_rate = node_speed * total_length / denominator
    own_drive = pseudo_rate * dist_t / denominator
    carry_rate = jnp.broadcast_to(carry_rate, own_drive.shape)
    own_field = line_sweep(carry_rate, own_drive, node_signed)
    moment_signed = jnp.asarray(np.tile(along_x[:NXI], 5), jnp.float32)
    moment_speed = jnp.abs(moment_signed)
    moment_den = moment_speed * total_length + thickness + pseudo_rate
    moment_rate = moment_speed * total_length / moment_den
    moment_drive = thickness * jnp.repeat(
        old_moments.reshape(total_length, share, 5), NXI, axis=2
    ) / moment_den
    moment_field = line_sweep(moment_rate, moment_drive, moment_signed)
    chosen = jnp.asarray(
        (np.arange(node_count)[None, :] % NXI) == np.arange(NXI)[:, None], jnp.float32
    )
    spread_basis = (rebuild[:, None, :] * chosen[None]).reshape(5 * NXI, node_count)
    half_field = own_field + jnp.dot(
        moment_field.reshape(cells, 5 * NXI), spread_basis, precision=HIGH
    ).reshape(total_length, share, node_count)
    half_moments = tree_sum(
        jnp.dot(half_field.reshape(cells, node_count), weighted.T, precision=HIGH), ("vel",)
    )
    residual = (half_moments - old_moments).reshape(total_length, share, 5)
    correction = line_block(inverse_t, residual)
    edge_zero = jnp.zeros((1, share, 5), jnp.float32)
    for sweep_index in range(JACOBI):
        from_left = jnp.concatenate([edge_zero, correction[:-1]], axis=0)
        from_right = jnp.concatenate([correction[1:], edge_zero], axis=0)
        correction = line_block(
            inverse_t,
            residual - line_block(lower_t, from_left) - line_block(upper_t, from_right),
        )
    correction = correction.reshape(cells, 5)
    macro = half_moments + correction
    synthetic = half_field + jnp.dot(correction, rebuild, precision=HIGH).reshape(
        total_length, share, node_count
    )
    local_totals = jnp.sum(old_moments - macro, axis=0)[0:2]
    magnitude = jnp.sum(jnp.abs(synthetic), axis=(0, 1))
    line_loaded = jnp.sum((node_mass * magnitude).reshape(node_rows, NXI), axis=0)
    first_copy = (lax.axis_index("vel") == 0).astype(jnp.float32)
    back = jnp.concatenate([synthetic, macro.reshape(total_length, share, 5)], axis=2)
    back = lax.all_to_all(back, "sec", 0, 1, tiled=True)
    back = back.transpose(2, 0, 1).reshape(node_count + 5, cell_count)
    gathered = tree_sum(
        jnp.concatenate([line_loaded, local_totals * first_copy]), ("vel", "sec")
    )
    loaded = gathered[:NXI]
    goal_mass = jnp.broadcast_to(gathered[NXI], (NXI,))
    goal_flow = jnp.broadcast_to(gathered[NXI + 1], (NXI,))
    spread = jnp.ones((NXI, NXI), jnp.float32)
    shift_mass = jnp.zeros((NXI,), jnp.float32)
    shift_flow = jnp.zeros((NXI,), jnp.float32)
    for newton_turn in range(NEWTON):
        growth = jnp.exp(shift_mass + shift_flow * line_signed)
        scaled = loaded * growth
        excess = loaded * (growth - 1.0)
        terms = jnp.stack(
            [scaled, scaled * line_signed, scaled * line_signed * line_signed, excess, excess * line_signed]
        )
        sums = jnp.dot(terms, spread, precision=HIGH)
        shift_mass, shift_flow = newton_update(shift_mass, shift_flow, sums, goal_mass, goal_flow)
    growth = jnp.exp(shift_mass + shift_flow * line_signed)
    synthetic_rows = back[:node_count].reshape(node_rows, NXI, cell_count)
    new_distribution = synthetic_rows + jnp.abs(synthetic_rows) * (growth[None, :, None] - 1.0)
    return (new_distribution.reshape(node_count, cell_count), back[node_count:])


def solution(mesh):
    in_specs = (P("vel", "sec"), P("sec"), P(None, "sec"), P(None, "sec"), P(None, "sec"))
    out_specs = (P("vel", "sec"), P(None, "sec"))
    return jax.shard_map(body, mesh=mesh, in_specs=in_specs, out_specs=out_specs, check_vma=False)
```

```python
import math

import jax
import jax.numpy as jnp
import numpy as np
from jax import lax
from jax.experimental import pallas as pl
from jax.sharding import PartitionSpec as P

NXI = 24
TUBES = 128
JACOBI = 4
NEWTON = 2


HIGH = lax.Precision.HIGHEST
pseudo_rate = 1.0


def passed_along(block, axis, distance):
    devices = range(lax.axis_size(axis))
    route = [(i - distance, i) for i in devices if i - distance in devices]
    return lax.ppermute(block, axis, route)


def extended(array, sides, width):
    for axis, dim in sides:
        count, length = (lax.axis_size(axis), array.shape[dim])
        up = [(i, (i + 1) % count) for i in range(count - 1)]
        down = [(j, i) for i, j in up]
        last = lax.slice_in_dim(array, length - width, length, axis=dim)
        first = lax.slice_in_dim(array, 0, width, axis=dim)
        before = lax.ppermute(last, axis, up)
        after = lax.ppermute(first, axis, down)
        array = jnp.concatenate([before, array, after], axis=dim)
    return array


def hermite_rule(count):
    quarter = math.pi ** (-0.25)
    found = []
    last_slope = 1.0
    for index in range(count // 2):
        if index == 0:
            guess = math.sqrt(2.0 * count + 1.0) - 1.85575 * (2.0 * count + 1.0) ** (-0.16667)
        elif index == 1:
            guess = guess - 1.14 * count**0.426 / guess
        elif index == 2:
            guess = 1.86 * guess - 0.86 * found[0][0]
        elif index == 3:
            guess = 1.91 * guess - 0.91 * found[1][0]
        else:
            guess = 2.0 * guess - found[index - 2][0]
        for repeat in range(60):
            current = quarter
            previous = 0.0
            for order in range(count):
                older = previous
                previous = current
                current = (
                    guess * math.sqrt(2.0 / (order + 1)) * previous
                    - math.sqrt(order / (order + 1.0)) * older
                )
            last_slope = math.sqrt(2.0 * count) * previous
            guess = guess - current / last_slope
        found.append((guess, 2.0 / (last_slope * last_slope)))
    positive = found[::-1]
    points = [-pair[0] for pair in found] + [pair[0] for pair in positive]
    weights = [pair[1] for pair in found] + [pair[1] for pair in positive]
    return (np.array(points), np.array(weights))


def node_tables(axis_points):
    points, weights = hermite_rule(axis_points)
    node_index = np.arange(axis_points**3)
    idx_x = node_index % axis_points
    idx_z = node_index // axis_points % axis_points
    idx_y = node_index // (axis_points * axis_points)
    along_x = points[idx_x]
    along_y = points[idx_y]
    along_z = points[idx_z]
    node_weight = weights[idx_x] * weights[idx_y] * weights[idx_z] / math.pi**1.5
    energy = along_x**2 + along_y**2 + along_z**2 - 1.5
    moment_basis = np.stack([along_x * 0.0 + 1.0, along_x, along_y, along_z, energy])
    norm_scale = np.array([1.0, 0.5, 0.5, 0.5, 1.5])
    return (
        along_x,
        node_weight,
        moment_basis * node_weight[None, :],
        moment_basis / norm_scale[:, None],
    )


def apply_block(matrices, vector):
    shaped = matrices.reshape((5, 5) + vector.shape[1:])
    return jnp.sum(shaped * vector[None], axis=1)


def affine_combine(earlier_map, later_map):
    return (later_map[0] * earlier_map[0], later_map[0] * earlier_map[1] + later_map[1])


def newton_sums(loaded, signed, shift_mass, shift_flow):
    growth = jnp.exp(shift_mass + shift_flow * signed)
    scaled = loaded * growth
    excess = loaded * (growth - 1.0)
    return jnp.stack(
        [
            jnp.sum(scaled),
            jnp.sum(scaled * signed),
            jnp.sum(scaled * signed * signed),
            jnp.sum(excess),
            jnp.sum(excess * signed),
        ]
    )


def newton_update(shift_mass, shift_flow, sums, goal_mass, goal_flow):
    resid_mass = sums[3] - goal_mass
    resid_flow = sums[4] - goal_flow
    determinant = sums[0] * sums[2] - sums[1] * sums[1]
    new_mass = shift_mass - (sums[2] * resid_mass - sums[1] * resid_flow) / determinant
    new_flow = shift_flow - (sums[0] * resid_flow - sums[1] * resid_mass) / determinant
    return (new_mass, new_flow)


def received(block, distance):
    count = lax.axis_size("sec")
    if abs(distance) >= count:
        return jnp.zeros_like(block)
    return passed_along(block, "sec", distance)


def fetched(state, distance, sign):
    rate, drive = state
    got = received(jnp.concatenate([rate, drive], axis=0), sign * distance)
    return got[:1], got[1:]


def scan_first(rate, drive, sign):
    near_a, near_b = fetched((rate, drive), 1, sign)
    if lax.axis_size("sec") <= 2:
        return (near_a, near_b), 1
    far_a, far_b = fetched((rate, drive), 2, sign)
    return (near_a * far_a, near_a * far_b + near_b), 2


def scan_next(state, span, sign):
    got_a, got_b = fetched(state, span, sign)
    return (state[0] * got_a, state[0] * got_b + state[1]), span * 2


def exclusive_inflow(rate, drive, sign):
    state, span = scan_first(rate, drive, sign)
    while span < lax.axis_size("sec") - 1:
        state, span = scan_next(state, span, sign)
    return state[1]


def with_halo(array, width):
    parts = [received(array, d) for d in range(width, 0, -1)]
    parts.append(array)
    parts.extend(received(array, -d) for d in range(1, width + 1))
    return jnp.concatenate(parts, axis=1)


def group_sum(block, axis, low_bit, members):
    count = lax.axis_size(axis)
    if members == 2:
        pairs = [(i, i ^ (1 << low_bit)) for i in range(count)]
        return block + lax.ppermute(block, axis, pairs)
    mine = (lax.axis_index(axis) >> low_bit) % members
    shifted = [block]
    for step in range(1, members):
        pairs = []
        for i in range(count):
            place = (i >> low_bit) % members
            base = i - (place << low_bit)
            pairs.append((base + (((place + step) % members) << low_bit), i))
        shifted.append(lax.ppermute(block, axis, pairs))
    stacked = jnp.stack(shifted)
    total = None
    for member in range(members):
        value = lax.dynamic_index_in_dim(stacked, (member - mine) % members, 0, keepdims=False)
        total = value if total is None else total + value
    return total


def sum_plan(axis, count):
    bits = count.bit_length() - 1
    plan = []
    bit = 0
    if axis == "vel" and bits % 2 == 1:
        plan.append((0, 2))
        bit = 1
    elif axis == "vel" and bits >= 2:
        plan.append((0, 2))
        bit = 1
    while bit + 1 < bits:
        plan.append((bit, 4))
        bit += 2
    if bit < bits:
        plan.append((bit, 2))
    return plan


def tree_sum(block, axes):
    for axis in axes:
        count = lax.axis_size(axis)
        if count & (count - 1):
            block = lax.psum(block, axis)
            continue
        for low_bit, members in sum_plan(axis, count):
            block = group_sum(block, axis, low_bit, members)
    return block


def local_sweep(carry_rate, drive):
    half_nodes = NXI // 2
    shape = (1, half_nodes) + drive.shape[2:]
    prod_neg, local_neg = lax.associative_scan(
        affine_combine,
        (jnp.broadcast_to(carry_rate[:, :half_nodes], shape), drive[:, :half_nodes]),
        reverse=True,
        axis=2,
    )
    prod_pos, local_pos = lax.associative_scan(
        affine_combine,
        (jnp.broadcast_to(carry_rate[:, half_nodes:], shape), drive[:, half_nodes:]),
        axis=2,
    )
    return prod_neg, local_neg, prod_pos, local_pos


def joined_field(sweep, inflow_neg, inflow_pos):
    prod_neg, local_neg, prod_pos, local_pos = sweep
    field_neg = local_neg + prod_neg * inflow_neg[:, :, None, :]
    field_pos = local_pos + prod_pos * inflow_pos[:, :, None, :]
    return jnp.concatenate([field_neg, field_pos], axis=1)


def swept_field(carry_rate, drive):
    sweep = local_sweep(carry_rate, drive)
    inflow_pos = exclusive_inflow(sweep[2][:, :, -1], sweep[3][:, :, -1], 1)
    inflow_neg = exclusive_inflow(sweep[0][:, :, 0], sweep[1][:, :, 0], -1)
    return joined_field(sweep, inflow_neg, inflow_pos)


def caught_up_side(own, own_span, rate, drive, count, sign):
    reach = min(2 * own_span, count - 1)
    own_rows = own[1].shape[0]
    moment_rows = drive.shape[0]
    fetched_maps = {}
    for distance in range(1, reach + 1):
        if distance == own_span and own_span < count - 1:
            packed = jnp.concatenate([own[0], own[1], rate, drive], axis=0)
            got = received(packed, sign * distance)
            got_own = (got[:1], got[1 : 1 + own_rows])
            fetched_maps[distance] = (got[1 + own_rows : 2 + own_rows], got[2 + own_rows :])
        else:
            got = received(jnp.concatenate([rate, drive], axis=0), sign * distance)
            fetched_maps[distance] = (got[:1], got[1:])
    if own_span < count - 1:
        own = (own[0] * got_own[0], own[0] * got_own[1] + own[1])
    acc_a, acc_b = fetched_maps[reach]
    for distance in range(reach - 1, 0, -1):
        near_a, near_b = fetched_maps[distance]
        acc_a, acc_b = near_a * acc_a, near_a * acc_b + near_b
    return own, (acc_a, acc_b)


def caught_up(own_pos, own_neg, own_span, moment_sweep, count):
    own_pos, moment_pos = caught_up_side(
        own_pos, own_span, moment_sweep[2][:, :, -1], moment_sweep[3][:, :, -1], count, 1
    )
    own_neg, moment_neg = caught_up_side(
        own_neg, own_span, moment_sweep[0][:, :, 0], moment_sweep[1][:, :, 0], count, -1
    )
    return lax.optimization_barrier((own_pos, own_neg, moment_pos, moment_neg))


def joint_next(own, moment, span, sign):
    own_rows = own[1].shape[0]
    packed = jnp.concatenate([own[0], own[1], moment[1]], axis=0)
    got = received(packed, sign * span)
    got_a, got_own, got_moment = got[:1], got[1 : 1 + own_rows], got[1 + own_rows :]
    return (
        (own[0] * got_a, own[0] * got_own + own[1]),
        (own[0] * got_a, own[0] * got_moment + moment[1]),
    )


def sweep_kernel(rate_ref, drive_ref, sign_ref, out_ref):
    positions = rate_ref.shape[0]
    start = jnp.zeros(rate_ref.shape[1:], jnp.float32)

    def forward(p, carried):
        value = rate_ref[p] * carried + drive_ref[p]
        out_ref[p] = value
        return value

    lax.fori_loop(0, positions, forward, start)
    heading = sign_ref[...] > 0

    def backward(i, carried):
        p = positions - 1 - i
        value = rate_ref[p] * carried + drive_ref[p]
        out_ref[p] = jnp.where(heading, out_ref[p], value)
        return value

    lax.fori_loop(0, positions, backward, start)


def line_sweep(carry_rate, drive_term, node_signed):
    return pl.pallas_call(
        sweep_kernel,
        out_shape=jax.ShapeDtypeStruct(drive_term.shape, jnp.float32),
    )(carry_rate, drive_term, node_signed.reshape(1, -1))


def line_block(matrices, vector):
    shaped = matrices.reshape(matrices.shape[:-1] + (5, 5))
    return jnp.sum(shaped * vector[..., None, :], axis=-1)


def body(distribution, collision, lower_blocks, upper_blocks, diag_inverse):
    node_count = distribution.shape[0]
    cell_count = distribution.shape[1]
    length = cell_count // TUBES
    node_rows = node_count // NXI
    count = lax.axis_size("sec")
    total_length = length * count
    share = TUBES // count
    along_x, node_weight, weighted_np, rebuild_np = node_tables(NXI)
    offset = lax.axis_index("vel") * node_count
    weighted = lax.dynamic_slice_in_dim(
        jnp.asarray(weighted_np, jnp.float32), offset, node_count, 1
    )
    rebuild = lax.dynamic_slice_in_dim(jnp.asarray(rebuild_np, jnp.float32), offset, node_count, 1)
    node_mass = lax.dynamic_slice_in_dim(jnp.asarray(node_weight, jnp.float32), offset, node_count, 0)
    line_signed = jnp.asarray(along_x[:NXI], jnp.float32)
    node_signed = jnp.asarray(np.tile(along_x[:NXI], node_rows), jnp.float32)
    pieces = [distribution, collision.reshape(1, cell_count), lower_blocks, upper_blocks, diag_inverse]
    packed = jnp.concatenate(
        [piece.reshape(-1, length, TUBES).transpose(1, 2, 0) for piece in pieces], axis=2
    )
    lines = lax.all_to_all(packed, "sec", 1, 0, tiled=True)
    dist_t = lines[:, :, :node_count]
    thickness = lines[:, :, node_count : node_count + 1]
    lower_t = lines[:, :, node_count + 1 : node_count + 26]
    upper_t = lines[:, :, node_count + 26 : node_count + 51]
    inverse_t = lines[:, :, node_count + 51 : node_count + 76]
    cells = total_length * share
    old_part = jnp.dot(dist_t.reshape(cells, node_count), weighted.T, precision=HIGH)
    node_speed = jnp.abs(node_signed)
    denominator = node_speed * total_length + thickness + pseudo_rate
    carry_rate = node_speed * total_length / denominator
    own_drive = pseudo_rate * dist_t / denominator
    carry_rate = jnp.broadcast_to(carry_rate, own_drive.shape)
    own_field = line_sweep(carry_rate, own_drive, node_signed)
    moment_signed = jnp.asarray(np.tile(along_x[:NXI], 5), jnp.float32)
    moment_speed = jnp.abs(moment_signed)
    moment_den = moment_speed * total_length + thickness + pseudo_rate
    moment_rate = moment_speed * total_length / moment_den
    moment_drive = thickness * jnp.repeat(
        old_part.reshape(total_length, share, 5), NXI, axis=2
    ) / moment_den
    moment_part = line_sweep(moment_rate, moment_drive, moment_signed).reshape(cells, 5 * NXI)
    coupling = jnp.asarray(np.einsum(
        "irx,jrx->jxi",
        weighted_np.reshape(5, -1, NXI),
        rebuild_np.reshape(5, -1, NXI),
    ).reshape(5 * NXI, 5), jnp.float32)
    half_part = jnp.dot(
        own_field.reshape(cells, node_count), weighted.T, precision=HIGH
    ) + jnp.dot(moment_part, coupling, precision=HIGH)
    summed = tree_sum(jnp.concatenate([half_part, old_part, moment_part], axis=1), ("vel",))
    half_moments = summed[:, :5]
    old_moments = summed[:, 5:10]
    moment_field = summed[:, 10:]
    chosen = jnp.asarray(
        (np.arange(node_count)[None, :] % NXI) == np.arange(NXI)[:, None], jnp.float32
    )
    spread_basis = (rebuild[:, None, :] * chosen[None]).reshape(5 * NXI, node_count)
    half_field = own_field + jnp.dot(moment_field, spread_basis, precision=HIGH).reshape(
        total_length, share, node_count
    )
    residual = (half_moments - old_moments).reshape(total_length, share, 5)
    correction = line_block(inverse_t, residual)
    edge_zero = jnp.zeros((1, share, 5), jnp.float32)
    for sweep_index in range(JACOBI):
        from_left = jnp.concatenate([edge_zero, correction[:-1]], axis=0)
        from_right = jnp.concatenate([correction[1:], edge_zero], axis=0)
        correction = line_block(
            inverse_t,
            residual - line_block(lower_t, from_left) - line_block(upper_t, from_right),
        )
    correction = correction.reshape(cells, 5)
    macro = half_moments + correction
    synthetic = half_field + jnp.dot(correction, rebuild, precision=HIGH).reshape(
        total_length, share, node_count
    )
    local_totals = jnp.sum(old_moments - macro, axis=0)[0:2]
    magnitude = jnp.sum(jnp.abs(synthetic), axis=(0, 1))
    line_loaded = jnp.sum((node_mass * magnitude).reshape(node_rows, NXI), axis=0)
    first_copy = (lax.axis_index("vel") == 0).astype(jnp.float32)
    back = jnp.concatenate([synthetic, macro.reshape(total_length, share, 5)], axis=2)
    back = lax.all_to_all(back, "sec", 0, 1, tiled=True)
    back = back.transpose(2, 0, 1).reshape(node_count + 5, cell_count)
    gathered = tree_sum(
        jnp.concatenate([line_loaded, local_totals * first_copy]), ("vel", "sec")
    )
    loaded = gathered[:NXI]
    goal_mass = jnp.broadcast_to(gathered[NXI], (NXI,))
    goal_flow = jnp.broadcast_to(gathered[NXI + 1], (NXI,))
    spread = jnp.ones((NXI, NXI), jnp.float32)
    shift_mass = jnp.zeros((NXI,), jnp.float32)
    shift_flow = jnp.zeros((NXI,), jnp.float32)
    for newton_turn in range(NEWTON):
        growth = jnp.exp(shift_mass + shift_flow * line_signed)
        scaled = loaded * growth
        excess = loaded * (growth - 1.0)
        terms = jnp.stack(
            [scaled, scaled * line_signed, scaled * line_signed * line_signed, excess, excess * line_signed]
        )
        sums = jnp.dot(terms, spread, precision=HIGH)
        shift_mass, shift_flow = newton_update(shift_mass, shift_flow, sums, goal_mass, goal_flow)
    growth = jnp.exp(shift_mass + shift_flow * line_signed)
    synthetic_rows = back[:node_count].reshape(node_rows, NXI, cell_count)
    new_distribution = synthetic_rows + jnp.abs(synthetic_rows) * (growth[None, :, None] - 1.0)
    return (new_distribution.reshape(node_count, cell_count), back[node_count:])


def solution(mesh):
    in_specs = (P("vel", "sec"), P("sec"), P(None, "sec"), P(None, "sec"), P(None, "sec"))
    out_specs = (P("vel", "sec"), P(None, "sec"))
    return jax.shard_map(body, mesh=mesh, in_specs=in_specs, out_specs=out_specs, check_vma=False)
```

```python
import math

import jax
import jax.numpy as jnp
import numpy as np
from jax import lax
from jax.experimental import pallas as pl
from jax.sharding import PartitionSpec as P

NXI = 24
TUBES = 128
JACOBI = 4
NEWTON = 2


HIGH = lax.Precision.HIGHEST
pseudo_rate = 1.0


def passed_along(block, axis, distance):
    devices = range(lax.axis_size(axis))
    route = [(i - distance, i) for i in devices if i - distance in devices]
    return lax.ppermute(block, axis, route)


def extended(array, sides, width):
    for axis, dim in sides:
        count, length = (lax.axis_size(axis), array.shape[dim])
        up = [(i, (i + 1) % count) for i in range(count - 1)]
        down = [(j, i) for i, j in up]
        last = lax.slice_in_dim(array, length - width, length, axis=dim)
        first = lax.slice_in_dim(array, 0, width, axis=dim)
        before = lax.ppermute(last, axis, up)
        after = lax.ppermute(first, axis, down)
        array = jnp.concatenate([before, array, after], axis=dim)
    return array


def hermite_rule(count):
    quarter = math.pi ** (-0.25)
    found = []
    last_slope = 1.0
    for index in range(count // 2):
        if index == 0:
            guess = math.sqrt(2.0 * count + 1.0) - 1.85575 * (2.0 * count + 1.0) ** (-0.16667)
        elif index == 1:
            guess = guess - 1.14 * count**0.426 / guess
        elif index == 2:
            guess = 1.86 * guess - 0.86 * found[0][0]
        elif index == 3:
            guess = 1.91 * guess - 0.91 * found[1][0]
        else:
            guess = 2.0 * guess - found[index - 2][0]
        for repeat in range(60):
            current = quarter
            previous = 0.0
            for order in range(count):
                older = previous
                previous = current
                current = (
                    guess * math.sqrt(2.0 / (order + 1)) * previous
                    - math.sqrt(order / (order + 1.0)) * older
                )
            last_slope = math.sqrt(2.0 * count) * previous
            guess = guess - current / last_slope
        found.append((guess, 2.0 / (last_slope * last_slope)))
    positive = found[::-1]
    points = [-pair[0] for pair in found] + [pair[0] for pair in positive]
    weights = [pair[1] for pair in found] + [pair[1] for pair in positive]
    return (np.array(points), np.array(weights))


def node_tables(axis_points):
    points, weights = hermite_rule(axis_points)
    node_index = np.arange(axis_points**3)
    idx_x = node_index % axis_points
    idx_z = node_index // axis_points % axis_points
    idx_y = node_index // (axis_points * axis_points)
    along_x = points[idx_x]
    along_y = points[idx_y]
    along_z = points[idx_z]
    node_weight = weights[idx_x] * weights[idx_y] * weights[idx_z] / math.pi**1.5
    energy = along_x**2 + along_y**2 + along_z**2 - 1.5
    moment_basis = np.stack([along_x * 0.0 + 1.0, along_x, along_y, along_z, energy])
    norm_scale = np.array([1.0, 0.5, 0.5, 0.5, 1.5])
    return (
        along_x,
        node_weight,
        moment_basis * node_weight[None, :],
        moment_basis / norm_scale[:, None],
    )


def apply_block(matrices, vector):
    shaped = matrices.reshape((5, 5) + vector.shape[1:])
    return jnp.sum(shaped * vector[None], axis=1)


def affine_combine(earlier_map, later_map):
    return (later_map[0] * earlier_map[0], later_map[0] * earlier_map[1] + later_map[1])


def newton_sums(loaded, signed, shift_mass, shift_flow):
    growth = jnp.exp(shift_mass + shift_flow * signed)
    scaled = loaded * growth
    excess = loaded * (growth - 1.0)
    return jnp.stack(
        [
            jnp.sum(scaled),
            jnp.sum(scaled * signed),
            jnp.sum(scaled * signed * signed),
            jnp.sum(excess),
            jnp.sum(excess * signed),
        ]
    )


def newton_update(shift_mass, shift_flow, sums, goal_mass, goal_flow):
    resid_mass = sums[3] - goal_mass
    resid_flow = sums[4] - goal_flow
    determinant = sums[0] * sums[2] - sums[1] * sums[1]
    new_mass = shift_mass - (sums[2] * resid_mass - sums[1] * resid_flow) / determinant
    new_flow = shift_flow - (sums[0] * resid_flow - sums[1] * resid_mass) / determinant
    return (new_mass, new_flow)


def received(block, distance):
    count = lax.axis_size("sec")
    if abs(distance) >= count:
        return jnp.zeros_like(block)
    return passed_along(block, "sec", distance)


def fetched(state, distance, sign):
    rate, drive = state
    got = received(jnp.concatenate([rate, drive], axis=0), sign * distance)
    return got[:1], got[1:]


def scan_first(rate, drive, sign):
    near_a, near_b = fetched((rate, drive), 1, sign)
    if lax.axis_size("sec") <= 2:
        return (near_a, near_b), 1
    far_a, far_b = fetched((rate, drive), 2, sign)
    return (near_a * far_a, near_a * far_b + near_b), 2


def scan_next(state, span, sign):
    got_a, got_b = fetched(state, span, sign)
    return (state[0] * got_a, state[0] * got_b + state[1]), span * 2


def exclusive_inflow(rate, drive, sign):
    state, span = scan_first(rate, drive, sign)
    while span < lax.axis_size("sec") - 1:
        state, span = scan_next(state, span, sign)
    return state[1]


def with_halo(array, width):
    parts = [received(array, d) for d in range(width, 0, -1)]
    parts.append(array)
    parts.extend(received(array, -d) for d in range(1, width + 1))
    return jnp.concatenate(parts, axis=1)


def group_sum(block, axis, low_bit, members):
    count = lax.axis_size(axis)
    if members == 2:
        pairs = [(i, i ^ (1 << low_bit)) for i in range(count)]
        return block + lax.ppermute(block, axis, pairs)
    mine = (lax.axis_index(axis) >> low_bit) % members
    shifted = [block]
    for step in range(1, members):
        pairs = []
        for i in range(count):
            place = (i >> low_bit) % members
            base = i - (place << low_bit)
            pairs.append((base + (((place + step) % members) << low_bit), i))
        shifted.append(lax.ppermute(block, axis, pairs))
    stacked = jnp.stack(shifted)
    total = None
    for member in range(members):
        value = lax.dynamic_index_in_dim(stacked, (member - mine) % members, 0, keepdims=False)
        total = value if total is None else total + value
    return total


def sum_plan(axis, count):
    bits = count.bit_length() - 1
    plan = []
    bit = 0
    if axis == "vel" and bits % 2 == 1:
        plan.append((0, 2))
        bit = 1
    elif axis == "vel" and bits >= 2:
        plan.append((0, 2))
        bit = 1
    while bit + 1 < bits:
        plan.append((bit, 4))
        bit += 2
    if bit < bits:
        plan.append((bit, 2))
    return plan


def tree_sum(block, axes):
    for axis in axes:
        count = lax.axis_size(axis)
        if count & (count - 1):
            block = lax.psum(block, axis)
            continue
        for low_bit, members in sum_plan(axis, count):
            block = group_sum(block, axis, low_bit, members)
    return block


def local_sweep(carry_rate, drive):
    half_nodes = NXI // 2
    shape = (1, half_nodes) + drive.shape[2:]
    prod_neg, local_neg = lax.associative_scan(
        affine_combine,
        (jnp.broadcast_to(carry_rate[:, :half_nodes], shape), drive[:, :half_nodes]),
        reverse=True,
        axis=2,
    )
    prod_pos, local_pos = lax.associative_scan(
        affine_combine,
        (jnp.broadcast_to(carry_rate[:, half_nodes:], shape), drive[:, half_nodes:]),
        axis=2,
    )
    return prod_neg, local_neg, prod_pos, local_pos


def joined_field(sweep, inflow_neg, inflow_pos):
    prod_neg, local_neg, prod_pos, local_pos = sweep
    field_neg = local_neg + prod_neg * inflow_neg[:, :, None, :]
    field_pos = local_pos + prod_pos * inflow_pos[:, :, None, :]
    return jnp.concatenate([field_neg, field_pos], axis=1)


def swept_field(carry_rate, drive):
    sweep = local_sweep(carry_rate, drive)
    inflow_pos = exclusive_inflow(sweep[2][:, :, -1], sweep[3][:, :, -1], 1)
    inflow_neg = exclusive_inflow(sweep[0][:, :, 0], sweep[1][:, :, 0], -1)
    return joined_field(sweep, inflow_neg, inflow_pos)


def caught_up_side(own, own_span, rate, drive, count, sign):
    reach = min(2 * own_span, count - 1)
    own_rows = own[1].shape[0]
    moment_rows = drive.shape[0]
    fetched_maps = {}
    for distance in range(1, reach + 1):
        if distance == own_span and own_span < count - 1:
            packed = jnp.concatenate([own[0], own[1], rate, drive], axis=0)
            got = received(packed, sign * distance)
            got_own = (got[:1], got[1 : 1 + own_rows])
            fetched_maps[distance] = (got[1 + own_rows : 2 + own_rows], got[2 + own_rows :])
        else:
            got = received(jnp.concatenate([rate, drive], axis=0), sign * distance)
            fetched_maps[distance] = (got[:1], got[1:])
    if own_span < count - 1:
        own = (own[0] * got_own[0], own[0] * got_own[1] + own[1])
    acc_a, acc_b = fetched_maps[reach]
    for distance in range(reach - 1, 0, -1):
        near_a, near_b = fetched_maps[distance]
        acc_a, acc_b = near_a * acc_a, near_a * acc_b + near_b
    return own, (acc_a, acc_b)


def caught_up(own_pos, own_neg, own_span, moment_sweep, count):
    own_pos, moment_pos = caught_up_side(
        own_pos, own_span, moment_sweep[2][:, :, -1], moment_sweep[3][:, :, -1], count, 1
    )
    own_neg, moment_neg = caught_up_side(
        own_neg, own_span, moment_sweep[0][:, :, 0], moment_sweep[1][:, :, 0], count, -1
    )
    return lax.optimization_barrier((own_pos, own_neg, moment_pos, moment_neg))


def joint_next(own, moment, span, sign):
    own_rows = own[1].shape[0]
    packed = jnp.concatenate([own[0], own[1], moment[1]], axis=0)
    got = received(packed, sign * span)
    got_a, got_own, got_moment = got[:1], got[1 : 1 + own_rows], got[1 + own_rows :]
    return (
        (own[0] * got_a, own[0] * got_own + own[1]),
        (own[0] * got_a, own[0] * got_moment + moment[1]),
    )


def sweep_kernel(rate_ref, drive_ref, sign_ref, out_ref):
    positions = rate_ref.shape[0]
    start = jnp.zeros(rate_ref.shape[1:], jnp.float32)

    def forward(p, carried):
        value = rate_ref[p] * carried + drive_ref[p]
        out_ref[p] = value
        return value

    lax.fori_loop(0, positions, forward, start)
    heading = sign_ref[...] > 0

    def backward(i, carried):
        p = positions - 1 - i
        value = rate_ref[p] * carried + drive_ref[p]
        out_ref[p] = jnp.where(heading, out_ref[p], value)
        return value

    lax.fori_loop(0, positions, backward, start)


def line_sweep(carry_rate, drive_term, node_signed):
    return pl.pallas_call(
        sweep_kernel,
        out_shape=jax.ShapeDtypeStruct(drive_term.shape, jnp.float32),
    )(carry_rate, drive_term, node_signed.reshape(1, -1))


def line_block(matrices, vector):
    shaped = matrices.reshape(matrices.shape[:-1] + (5, 5))
    return jnp.sum(shaped * vector[..., None, :], axis=-1)


def body(distribution, collision, lower_blocks, upper_blocks, diag_inverse):
    node_count = distribution.shape[0]
    cell_count = distribution.shape[1]
    length = cell_count // TUBES
    node_rows = node_count // NXI
    count = lax.axis_size("sec")
    total_length = length * count
    share = TUBES // count
    along_x, node_weight, weighted_np, rebuild_np = node_tables(NXI)
    offset = lax.axis_index("vel") * node_count
    weighted = lax.dynamic_slice_in_dim(
        jnp.asarray(weighted_np, jnp.float32), offset, node_count, 1
    )
    rebuild = lax.dynamic_slice_in_dim(jnp.asarray(rebuild_np, jnp.float32), offset, node_count, 1)
    node_mass = lax.dynamic_slice_in_dim(jnp.asarray(node_weight, jnp.float32), offset, node_count, 0)
    line_signed = jnp.asarray(along_x[:NXI], jnp.float32)
    node_signed = jnp.asarray(np.tile(along_x[:NXI], node_rows), jnp.float32)
    packed = jnp.concatenate(
        [distribution, collision.reshape(1, cell_count), lower_blocks, upper_blocks, diag_inverse],
        axis=0,
    )
    packed = packed.reshape(packed.shape[0], length, TUBES)
    lines = lax.all_to_all(packed, "sec", 2, 1, tiled=True).transpose(1, 2, 0)
    dist_t = lines[:, :, :node_count]
    thickness = lines[:, :, node_count : node_count + 1]
    lower_t = lines[:, :, node_count + 1 : node_count + 26]
    upper_t = lines[:, :, node_count + 26 : node_count + 51]
    inverse_t = lines[:, :, node_count + 51 : node_count + 76]
    cells = total_length * share
    old_moments = tree_sum(
        jnp.dot(dist_t.reshape(cells, node_count), weighted.T, precision=HIGH), ("vel",)
    )
    node_speed = jnp.abs(node_signed)
    denominator = node_speed * total_length + thickness + pseudo_rate
    carry_rate = node_speed * total_length / denominator
    own_drive = pseudo_rate * dist_t / denominator
    carry_rate = jnp.broadcast_to(carry_rate, own_drive.shape)
    own_field = line_sweep(carry_rate, own_drive, node_signed)
    moment_signed = jnp.asarray(np.tile(along_x[:NXI], 5), jnp.float32)
    moment_speed = jnp.abs(moment_signed)
    moment_den = moment_speed * total_length + thickness + pseudo_rate
    moment_rate = moment_speed * total_length / moment_den
    moment_drive = thickness * jnp.repeat(
        old_moments.reshape(total_length, share, 5), NXI, axis=2
    ) / moment_den
    moment_field = line_sweep(moment_rate, moment_drive, moment_signed)
    chosen = jnp.asarray(
        (np.arange(node_count)[None, :] % NXI) == np.arange(NXI)[:, None], jnp.float32
    )
    spread_basis = (rebuild[:, None, :] * chosen[None]).reshape(5 * NXI, node_count)
    half_field = own_field + jnp.dot(
        moment_field.reshape(cells, 5 * NXI), spread_basis, precision=HIGH
    ).reshape(total_length, share, node_count)
    half_moments = tree_sum(
        jnp.dot(half_field.reshape(cells, node_count), weighted.T, precision=HIGH), ("vel",)
    )
    residual = (half_moments - old_moments).reshape(total_length, share, 5)
    correction = line_block(inverse_t, residual)
    edge_zero = jnp.zeros((1, share, 5), jnp.float32)
    for sweep_index in range(JACOBI):
        from_left = jnp.concatenate([edge_zero, correction[:-1]], axis=0)
        from_right = jnp.concatenate([correction[1:], edge_zero], axis=0)
        correction = line_block(
            inverse_t,
            residual - line_block(lower_t, from_left) - line_block(upper_t, from_right),
        )
    correction = correction.reshape(cells, 5)
    macro = half_moments + correction
    synthetic = half_field + jnp.dot(correction, rebuild, precision=HIGH).reshape(
        total_length, share, node_count
    )
    local_totals = jnp.sum(old_moments - macro, axis=0)[0:2]
    magnitude = jnp.sum(jnp.abs(synthetic), axis=(0, 1))
    line_loaded = jnp.sum((node_mass * magnitude).reshape(node_rows, NXI), axis=0)
    first_copy = (lax.axis_index("vel") == 0).astype(jnp.float32)
    back = jnp.concatenate([synthetic, macro.reshape(total_length, share, 5)], axis=2)
    back = lax.all_to_all(back, "sec", 0, 1, tiled=True)
    back = back.transpose(2, 0, 1).reshape(node_count + 5, cell_count)
    gathered = tree_sum(
        jnp.concatenate([line_loaded, local_totals * first_copy]), ("vel", "sec")
    )
    loaded = gathered[:NXI]
    goal_mass = jnp.broadcast_to(gathered[NXI], (NXI,))
    goal_flow = jnp.broadcast_to(gathered[NXI + 1], (NXI,))
    spread = jnp.ones((NXI, NXI), jnp.float32)
    shift_mass = jnp.zeros((NXI,), jnp.float32)
    shift_flow = jnp.zeros((NXI,), jnp.float32)
    for newton_turn in range(NEWTON):
        growth = jnp.exp(shift_mass + shift_flow * line_signed)
        scaled = loaded * growth
        excess = loaded * (growth - 1.0)
        terms = jnp.stack(
            [scaled, scaled * line_signed, scaled * line_signed * line_signed, excess, excess * line_signed]
        )
        sums = jnp.dot(terms, spread, precision=HIGH)
        shift_mass, shift_flow = newton_update(shift_mass, shift_flow, sums, goal_mass, goal_flow)
    growth = jnp.exp(shift_mass + shift_flow * line_signed)
    synthetic_rows = back[:node_count].reshape(node_rows, NXI, cell_count)
    new_distribution = synthetic_rows + jnp.abs(synthetic_rows) * (growth[None, :, None] - 1.0)
    return (new_distribution.reshape(node_count, cell_count), back[node_count:])


def solution(mesh):
    in_specs = (P("vel", "sec"), P("sec"), P(None, "sec"), P(None, "sec"), P(None, "sec"))
    out_specs = (P("vel", "sec"), P(None, "sec"))
    return jax.shard_map(body, mesh=mesh, in_specs=in_specs, out_specs=out_specs, check_vma=False)
```

```python
import math

import jax
import jax.numpy as jnp
import numpy as np
from jax import lax
from jax.experimental import pallas as pl
from jax.sharding import PartitionSpec as P

NXI = 24
TUBES = 128
JACOBI = 4
NEWTON = 2


HIGH = lax.Precision.HIGHEST
pseudo_rate = 1.0


def passed_along(block, axis, distance):
    devices = range(lax.axis_size(axis))
    route = [(i - distance, i) for i in devices if i - distance in devices]
    return lax.ppermute(block, axis, route)


def extended(array, sides, width):
    for axis, dim in sides:
        count, length = (lax.axis_size(axis), array.shape[dim])
        up = [(i, (i + 1) % count) for i in range(count - 1)]
        down = [(j, i) for i, j in up]
        last = lax.slice_in_dim(array, length - width, length, axis=dim)
        first = lax.slice_in_dim(array, 0, width, axis=dim)
        before = lax.ppermute(last, axis, up)
        after = lax.ppermute(first, axis, down)
        array = jnp.concatenate([before, array, after], axis=dim)
    return array


def hermite_rule(count):
    quarter = math.pi ** (-0.25)
    found = []
    last_slope = 1.0
    for index in range(count // 2):
        if index == 0:
            guess = math.sqrt(2.0 * count + 1.0) - 1.85575 * (2.0 * count + 1.0) ** (-0.16667)
        elif index == 1:
            guess = guess - 1.14 * count**0.426 / guess
        elif index == 2:
            guess = 1.86 * guess - 0.86 * found[0][0]
        elif index == 3:
            guess = 1.91 * guess - 0.91 * found[1][0]
        else:
            guess = 2.0 * guess - found[index - 2][0]
        for repeat in range(60):
            current = quarter
            previous = 0.0
            for order in range(count):
                older = previous
                previous = current
                current = (
                    guess * math.sqrt(2.0 / (order + 1)) * previous
                    - math.sqrt(order / (order + 1.0)) * older
                )
            last_slope = math.sqrt(2.0 * count) * previous
            guess = guess - current / last_slope
        found.append((guess, 2.0 / (last_slope * last_slope)))
    positive = found[::-1]
    points = [-pair[0] for pair in found] + [pair[0] for pair in positive]
    weights = [pair[1] for pair in found] + [pair[1] for pair in positive]
    return (np.array(points), np.array(weights))


def node_tables(axis_points):
    points, weights = hermite_rule(axis_points)
    node_index = np.arange(axis_points**3)
    idx_x = node_index % axis_points
    idx_z = node_index // axis_points % axis_points
    idx_y = node_index // (axis_points * axis_points)
    along_x = points[idx_x]
    along_y = points[idx_y]
    along_z = points[idx_z]
    node_weight = weights[idx_x] * weights[idx_y] * weights[idx_z] / math.pi**1.5
    energy = along_x**2 + along_y**2 + along_z**2 - 1.5
    moment_basis = np.stack([along_x * 0.0 + 1.0, along_x, along_y, along_z, energy])
    norm_scale = np.array([1.0, 0.5, 0.5, 0.5, 1.5])
    return (
        along_x,
        node_weight,
        moment_basis * node_weight[None, :],
        moment_basis / norm_scale[:, None],
    )


def apply_block(matrices, vector):
    shaped = matrices.reshape((5, 5) + vector.shape[1:])
    return jnp.sum(shaped * vector[None], axis=1)


def affine_combine(earlier_map, later_map):
    return (later_map[0] * earlier_map[0], later_map[0] * earlier_map[1] + later_map[1])


def newton_sums(loaded, signed, shift_mass, shift_flow):
    growth = jnp.exp(shift_mass + shift_flow * signed)
    scaled = loaded * growth
    excess = loaded * (growth - 1.0)
    return jnp.stack(
        [
            jnp.sum(scaled),
            jnp.sum(scaled * signed),
            jnp.sum(scaled * signed * signed),
            jnp.sum(excess),
            jnp.sum(excess * signed),
        ]
    )


def newton_update(shift_mass, shift_flow, sums, goal_mass, goal_flow):
    resid_mass = sums[3] - goal_mass
    resid_flow = sums[4] - goal_flow
    determinant = sums[0] * sums[2] - sums[1] * sums[1]
    new_mass = shift_mass - (sums[2] * resid_mass - sums[1] * resid_flow) / determinant
    new_flow = shift_flow - (sums[0] * resid_flow - sums[1] * resid_mass) / determinant
    return (new_mass, new_flow)


def received(block, distance):
    count = lax.axis_size("sec")
    if abs(distance) >= count:
        return jnp.zeros_like(block)
    return passed_along(block, "sec", distance)


def fetched(state, distance, sign):
    rate, drive = state
    got = received(jnp.concatenate([rate, drive], axis=0), sign * distance)
    return got[:1], got[1:]


def scan_first(rate, drive, sign):
    near_a, near_b = fetched((rate, drive), 1, sign)
    if lax.axis_size("sec") <= 2:
        return (near_a, near_b), 1
    far_a, far_b = fetched((rate, drive), 2, sign)
    return (near_a * far_a, near_a * far_b + near_b), 2


def scan_next(state, span, sign):
    got_a, got_b = fetched(state, span, sign)
    return (state[0] * got_a, state[0] * got_b + state[1]), span * 2


def exclusive_inflow(rate, drive, sign):
    state, span = scan_first(rate, drive, sign)
    while span < lax.axis_size("sec") - 1:
        state, span = scan_next(state, span, sign)
    return state[1]


def with_halo(array, width):
    parts = [received(array, d) for d in range(width, 0, -1)]
    parts.append(array)
    parts.extend(received(array, -d) for d in range(1, width + 1))
    return jnp.concatenate(parts, axis=1)


def group_sum(block, axis, low_bit, members):
    count = lax.axis_size(axis)
    if members == 2:
        pairs = [(i, i ^ (1 << low_bit)) for i in range(count)]
        return block + lax.ppermute(block, axis, pairs)
    mine = (lax.axis_index(axis) >> low_bit) % members
    shifted = [block]
    for step in range(1, members):
        pairs = []
        for i in range(count):
            place = (i >> low_bit) % members
            base = i - (place << low_bit)
            pairs.append((base + (((place + step) % members) << low_bit), i))
        shifted.append(lax.ppermute(block, axis, pairs))
    stacked = jnp.stack(shifted)
    total = None
    for member in range(members):
        value = lax.dynamic_index_in_dim(stacked, (member - mine) % members, 0, keepdims=False)
        total = value if total is None else total + value
    return total


def sum_plan(axis, count, pair_first=False):
    bits = count.bit_length() - 1
    plan = []
    bit = 0
    if axis == "vel" and (bits % 2 == 1 or pair_first):
        plan.append((0, 2))
        bit = 1
    while bit + 1 < bits:
        plan.append((bit, 4))
        bit += 2
    if bit < bits:
        plan.append((bit, 2))
    return plan


def tree_sum(block, axes, pair_first=False):
    for axis in axes:
        count = lax.axis_size(axis)
        if count & (count - 1):
            block = lax.psum(block, axis)
            continue
        for low_bit, members in sum_plan(axis, count, pair_first):
            block = group_sum(block, axis, low_bit, members)
    return block


def local_sweep(carry_rate, drive):
    half_nodes = NXI // 2
    shape = (1, half_nodes) + drive.shape[2:]
    prod_neg, local_neg = lax.associative_scan(
        affine_combine,
        (jnp.broadcast_to(carry_rate[:, :half_nodes], shape), drive[:, :half_nodes]),
        reverse=True,
        axis=2,
    )
    prod_pos, local_pos = lax.associative_scan(
        affine_combine,
        (jnp.broadcast_to(carry_rate[:, half_nodes:], shape), drive[:, half_nodes:]),
        axis=2,
    )
    return prod_neg, local_neg, prod_pos, local_pos


def joined_field(sweep, inflow_neg, inflow_pos):
    prod_neg, local_neg, prod_pos, local_pos = sweep
    field_neg = local_neg + prod_neg * inflow_neg[:, :, None, :]
    field_pos = local_pos + prod_pos * inflow_pos[:, :, None, :]
    return jnp.concatenate([field_neg, field_pos], axis=1)


def swept_field(carry_rate, drive):
    sweep = local_sweep(carry_rate, drive)
    inflow_pos = exclusive_inflow(sweep[2][:, :, -1], sweep[3][:, :, -1], 1)
    inflow_neg = exclusive_inflow(sweep[0][:, :, 0], sweep[1][:, :, 0], -1)
    return joined_field(sweep, inflow_neg, inflow_pos)


def caught_up_side(own, own_span, rate, drive, count, sign):
    reach = min(2 * own_span, count - 1)
    own_rows = own[1].shape[0]
    moment_rows = drive.shape[0]
    fetched_maps = {}
    for distance in range(1, reach + 1):
        if distance == own_span and own_span < count - 1:
            packed = jnp.concatenate([own[0], own[1], rate, drive], axis=0)
            got = received(packed, sign * distance)
            got_own = (got[:1], got[1 : 1 + own_rows])
            fetched_maps[distance] = (got[1 + own_rows : 2 + own_rows], got[2 + own_rows :])
        else:
            got = received(jnp.concatenate([rate, drive], axis=0), sign * distance)
            fetched_maps[distance] = (got[:1], got[1:])
    if own_span < count - 1:
        own = (own[0] * got_own[0], own[0] * got_own[1] + own[1])
    acc_a, acc_b = fetched_maps[reach]
    for distance in range(reach - 1, 0, -1):
        near_a, near_b = fetched_maps[distance]
        acc_a, acc_b = near_a * acc_a, near_a * acc_b + near_b
    return own, (acc_a, acc_b)


def caught_up(own_pos, own_neg, own_span, moment_sweep, count):
    own_pos, moment_pos = caught_up_side(
        own_pos, own_span, moment_sweep[2][:, :, -1], moment_sweep[3][:, :, -1], count, 1
    )
    own_neg, moment_neg = caught_up_side(
        own_neg, own_span, moment_sweep[0][:, :, 0], moment_sweep[1][:, :, 0], count, -1
    )
    return lax.optimization_barrier((own_pos, own_neg, moment_pos, moment_neg))


def joint_next(own, moment, span, sign):
    own_rows = own[1].shape[0]
    packed = jnp.concatenate([own[0], own[1], moment[1]], axis=0)
    got = received(packed, sign * span)
    got_a, got_own, got_moment = got[:1], got[1 : 1 + own_rows], got[1 + own_rows :]
    return (
        (own[0] * got_a, own[0] * got_own + own[1]),
        (own[0] * got_a, own[0] * got_moment + moment[1]),
    )


def sweep_kernel(rate_ref, drive_ref, sign_ref, out_ref):
    positions = rate_ref.shape[0]
    start = jnp.zeros(rate_ref.shape[1:], jnp.float32)

    def forward(p, carried):
        value = rate_ref[p] * carried + drive_ref[p]
        out_ref[p] = value
        return value

    lax.fori_loop(0, positions, forward, start)
    heading = sign_ref[...] > 0

    def backward(i, carried):
        p = positions - 1 - i
        value = rate_ref[p] * carried + drive_ref[p]
        out_ref[p] = jnp.where(heading, out_ref[p], value)
        return value

    lax.fori_loop(0, positions, backward, start)


def line_sweep(carry_rate, drive_term, node_signed):
    return pl.pallas_call(
        sweep_kernel,
        out_shape=jax.ShapeDtypeStruct(drive_term.shape, jnp.float32),
    )(carry_rate, drive_term, node_signed.reshape(1, -1))


def line_block(matrices, vector):
    shaped = matrices.reshape(matrices.shape[:-1] + (5, 5))
    return jnp.sum(shaped * vector[..., None, :], axis=-1)


def body(distribution, collision, lower_blocks, upper_blocks, diag_inverse):
    node_count = distribution.shape[0]
    cell_count = distribution.shape[1]
    length = cell_count // TUBES
    node_rows = node_count // NXI
    count = lax.axis_size("sec")
    total_length = length * count
    share = TUBES // count
    along_x, node_weight, weighted_np, rebuild_np = node_tables(NXI)
    offset = lax.axis_index("vel") * node_count
    weighted = lax.dynamic_slice_in_dim(
        jnp.asarray(weighted_np, jnp.float32), offset, node_count, 1
    )
    rebuild = lax.dynamic_slice_in_dim(jnp.asarray(rebuild_np, jnp.float32), offset, node_count, 1)
    node_mass = lax.dynamic_slice_in_dim(jnp.asarray(node_weight, jnp.float32), offset, node_count, 0)
    line_signed = jnp.asarray(along_x[:NXI], jnp.float32)
    node_signed = jnp.asarray(np.tile(along_x[:NXI], node_rows), jnp.float32)
    packed = jnp.concatenate(
        [distribution, collision.reshape(1, cell_count), lower_blocks, upper_blocks, diag_inverse],
        axis=0,
    )
    packed = packed.reshape(packed.shape[0], length, TUBES)
    lines = lax.all_to_all(packed, "sec", 2, 1, tiled=True).transpose(1, 2, 0)
    dist_t = lines[:, :, :node_count]
    thickness = lines[:, :, node_count : node_count + 1]
    lower_t = lines[:, :, node_count + 1 : node_count + 26]
    upper_t = lines[:, :, node_count + 26 : node_count + 51]
    inverse_t = lines[:, :, node_count + 51 : node_count + 76]
    cells = total_length * share
    old_moments = tree_sum(
        jnp.dot(dist_t.reshape(cells, node_count), weighted.T, precision=HIGH), ("vel",)
    )
    node_speed = jnp.abs(node_signed)
    denominator = node_speed * total_length + thickness + pseudo_rate
    carry_rate = node_speed * total_length / denominator
    own_drive = pseudo_rate * dist_t / denominator
    carry_rate = jnp.broadcast_to(carry_rate, own_drive.shape)
    own_field = line_sweep(carry_rate, own_drive, node_signed)
    moment_signed = jnp.asarray(np.tile(along_x[:NXI], 5), jnp.float32)
    moment_speed = jnp.abs(moment_signed)
    moment_den = moment_speed * total_length + thickness + pseudo_rate
    moment_rate = moment_speed * total_length / moment_den
    moment_drive = thickness * jnp.repeat(
        old_moments.reshape(total_length, share, 5), NXI, axis=2
    ) / moment_den
    moment_field = line_sweep(moment_rate, moment_drive, moment_signed)
    chosen = jnp.asarray(
        (np.arange(node_count)[None, :] % NXI) == np.arange(NXI)[:, None], jnp.float32
    )
    spread_basis = (rebuild[:, None, :] * chosen[None]).reshape(5 * NXI, node_count)
    half_field = own_field + jnp.dot(
        moment_field.reshape(cells, 5 * NXI), spread_basis, precision=HIGH
    ).reshape(total_length, share, node_count)
    half_moments = tree_sum(
        jnp.dot(half_field.reshape(cells, node_count), weighted.T, precision=HIGH), ("vel",)
    )
    residual = (half_moments - old_moments).reshape(total_length, share, 5)
    correction = line_block(inverse_t, residual)
    edge_zero = jnp.zeros((1, share, 5), jnp.float32)
    for sweep_index in range(JACOBI):
        from_left = jnp.concatenate([edge_zero, correction[:-1]], axis=0)
        from_right = jnp.concatenate([correction[1:], edge_zero], axis=0)
        correction = line_block(
            inverse_t,
            residual - line_block(lower_t, from_left) - line_block(upper_t, from_right),
        )
    correction = correction.reshape(cells, 5)
    macro = half_moments + correction
    synthetic = half_field + jnp.dot(correction, rebuild, precision=HIGH).reshape(
        total_length, share, node_count
    )
    local_totals = jnp.sum(old_moments - macro, axis=0)[0:2]
    magnitude = jnp.sum(jnp.abs(synthetic), axis=(0, 1))
    line_loaded = jnp.sum((node_mass * magnitude).reshape(node_rows, NXI), axis=0)
    first_copy = (lax.axis_index("vel") == 0).astype(jnp.float32)
    back = jnp.concatenate([synthetic, macro.reshape(total_length, share, 5)], axis=2)
    back = lax.all_to_all(back, "sec", 0, 1, tiled=True)
    back = back.transpose(2, 0, 1).reshape(node_count + 5, cell_count)
    gathered = tree_sum(
        jnp.concatenate([line_loaded, local_totals * first_copy]), ("vel", "sec"), True
    )
    loaded = gathered[:NXI]
    goal_mass = jnp.broadcast_to(gathered[NXI], (NXI,))
    goal_flow = jnp.broadcast_to(gathered[NXI + 1], (NXI,))
    spread = jnp.ones((NXI, NXI), jnp.float32)
    shift_mass = jnp.zeros((NXI,), jnp.float32)
    shift_flow = jnp.zeros((NXI,), jnp.float32)
    for newton_turn in range(NEWTON):
        growth = jnp.exp(shift_mass + shift_flow * line_signed)
        scaled = loaded * growth
        excess = loaded * (growth - 1.0)
        terms = jnp.stack(
            [scaled, scaled * line_signed, scaled * line_signed * line_signed, excess, excess * line_signed]
        )
        sums = jnp.dot(terms, spread, precision=HIGH)
        shift_mass, shift_flow = newton_update(shift_mass, shift_flow, sums, goal_mass, goal_flow)
    growth = jnp.exp(shift_mass + shift_flow * line_signed)
    synthetic_rows = back[:node_count].reshape(node_rows, NXI, cell_count)
    new_distribution = synthetic_rows + jnp.abs(synthetic_rows) * (growth[None, :, None] - 1.0)
    return (new_distribution.reshape(node_count, cell_count), back[node_count:])


def solution(mesh):
    in_specs = (P("vel", "sec"), P("sec"), P(None, "sec"), P(None, "sec"), P(None, "sec"))
    out_specs = (P("vel", "sec"), P(None, "sec"))
    return jax.shard_map(body, mesh=mesh, in_specs=in_specs, out_specs=out_specs, check_vma=False)
```
